32 devices in a mesh: grp: 2 (over y), seq: 4 (over z), mdl: 4 (over x, core).
Axes of the slice: x: 2, y: 2, z: 4, core: 2. Of those that a mesh axis runs over, the one named last changes fastest.
Arguments:
- query_proj: bfloat16 [2048, 4096], P(('grp', 'seq'), 'mdl'), parts along dimension 0, may hold values from -12 to 12, as said below
- key_proj: bfloat16 [2048, 4096], P(('grp', 'seq'), 'mdl'), parts along dimension 0, may hold values from -6 to 6
- value_proj: bfloat16 [2048, 4096], P(('grp', 'seq'), 'mdl'), parts along dimension 0, may hold values from -12 to 12, as said below
- gate_proj: bfloat16 [2048, 4096], P(('grp', 'seq'), 'mdl'), parts along dimension 0, may hold values from -6 to 6
- log_decay: float32 [32, 2048], P('mdl', ('grp', 'seq')), parts along dimension 1, may hold values from -2 to 0, as said below
- act_exponent: int32 [3, 4096], P(None, 'mdl'), may hold values from -5 to -2
- norm_gain: float32 [4096], P('mdl'), may hold values from 0.1 to 1.9
- out_weight: bfloat16 [4096, 6144], P('seq', 'mdl'), may hold values from -0.09375 to 0.09375
- weight_exponent: int32 [6144], P('mdl'), may hold values from -12 to -9
Outputs:
- layer_out: bfloat16 [2048, 6144], P(('grp', 'seq'), 'mdl'), parts along dimension 0
The draws below stay inside these ranges and needn't reach their ends.
There are 2 independent parts, one for each index of `grp`. The reference program is written for one: setup_inputs(seed, part) draws one part's arguments, and reference() takes and returns one part's arrays. A program takes and returns all parts, laid end to end along the dimension named above; an argument that names none is the same for every part. Nothing has to cross between parts.
Inputs may be any that keep to these rules, and one draw needn't show every extreme that they name: Rows of query_proj differ in scale. Columns of value_proj differ in scale. `log_decay`: negative everywhere.
All inputs are finite; a program needn't handle non-finite values.
Results may differ from the reference program's by a relative error of at most 0.0062.
Values may be sent and summed in bfloat16 or wider, within the bound.
No kernel may reach another device: no remote copies, remote signals or barrier semaphores. Data moves between devices by JAX's collectives and lax.ppermute only.
A program may use at most 64 MiB of HBM per device.

```python
import math
import jax
import jax.numpy as jnp
from jax import lax

D = 6144
HEAD_COUNT = 32
HDIM = 128
BLK = 256
TOK_DEV = 256
SEQUENCE_LENGTH = 1024
INNER = 4096


def draw_query_proj(key, part):
    noise_key, scale_key = jax.random.split(key)
    base_values = jnp.clip(jax.random.normal(noise_key, (SEQUENCE_LENGTH, INNER), jnp.float32), -4.0, 4.0)
    row_scale = jnp.exp(jax.random.uniform(scale_key, (SEQUENCE_LENGTH, 1), jnp.float32, math.log(0.3), math.log(3.0)))
    return (base_values * row_scale).astype(jnp.bfloat16)


def draw_value_proj(key, part):
    noise_key, scale_key = jax.random.split(jax.random.fold_in(key, 7))
    base_values = jnp.clip(jax.random.normal(noise_key, (SEQUENCE_LENGTH, INNER), jnp.float32), -4.0, 4.0)
    column_scale = jnp.exp(jax.random.uniform(scale_key, (1, INNER), jnp.float32, math.log(0.3), math.log(3.0)))
    return (base_values * column_scale).astype(jnp.bfloat16)


def draw_log_decay(key, part):
    random_subkeys = jax.random.split(jax.random.fold_in(key, 11), 7)
    device_count = SEQUENCE_LENGTH // TOK_DEV
    fast_share = 0.5
    fast_heads = jax.random.uniform(random_subkeys[0], (HEAD_COUNT,), jnp.float32) < fast_share
    fast_rate = jnp.exp(jax.random.uniform(random_subkeys[1], (HEAD_COUNT,), jnp.float32, math.log(5.0), math.log(9.0))) / BLK
    slow_rate = jnp.exp(jax.random.uniform(random_subkeys[2], (HEAD_COUNT,), jnp.float32, math.log(0.15), math.log(0.5))) / SEQUENCE_LENGTH
    base_rate = jnp.where(fast_heads, fast_rate, slow_rate)
    device_factor = jnp.exp(jax.random.uniform(random_subkeys[3], (HEAD_COUNT, device_count, 1), jnp.float32, math.log(0.5), math.log(2.0)))
    device_factor = jnp.broadcast_to(device_factor, (HEAD_COUNT, device_count, TOK_DEV)).reshape(HEAD_COUNT, SEQUENCE_LENGTH)
    position_factor = jnp.exp(jax.random.uniform(random_subkeys[4], (HEAD_COUNT, SEQUENCE_LENGTH), jnp.float32, math.log(0.7), math.log(1.4)))
    decay_rates = base_rate[:, None] * device_factor * position_factor
    spike_position = jax.random.randint(random_subkeys[5], (3,), 0, SEQUENCE_LENGTH)
    spike_strength = jnp.log(jax.random.uniform(random_subkeys[6], (3, HEAD_COUNT), jnp.float32, 0.6, 0.8))
    position_grid = jnp.arange(SEQUENCE_LENGTH)
    spike_events = (position_grid[None, :] == spike_position[:, None]).astype(jnp.float32)
    spike_flags = jnp.sum(spike_strength[:, :, None] * spike_events[:, None, :], axis=0)
    return (spike_flags - decay_rates).astype(jnp.float32)


def place_ends(values, own_key, low, largest):
    longest = values.shape.index(max(values.shape))
    spots = []
    for shift in (0, 1):
        where = [jax.random.randint(jax.random.fold_in(own_key, axis), (), 0, length) for axis, length in enumerate(values.shape)]
        where[longest] = (where[longest] + shift) % values.shape[longest]
        spots.append(tuple(where))
    return values.at[spots[0]].set(low).at[spots[1]].set(largest)


def block_levels(key, extent, cuts, low, top_value):
    def one(dim, parts):
        draws = jax.random.uniform(jax.random.fold_in(jax.random.fold_in(key, 6), dim), (parts,), jnp.float32, low / len(cuts), top_value / len(cuts))
        return jnp.repeat(jnp.exp(draws), extent[dim] // parts).reshape((-1,) + (1,) * (len(extent) - dim - 1))

    loudness = one(*cuts[0])
    for cut in cuts[1:]:
        loudness = loudness * one(*cut)
    return loudness


def centred(stream_key, shape, scale, most, cuts=(), kind=jnp.bfloat16):
    drawn = jax.random.normal(stream_key, shape, jnp.float32) * scale
    if len(cuts) > 0:
        drawn = block_levels(stream_key, shape, cuts, -0.22, 0.18) * drawn
    return jnp.clip(drawn, min=-most, max=most).astype(kind)


def setup_inputs(seed: int = 0, part: int = 0) -> dict:
    seeds = jax.random.split(jax.random.key(seed), 10)
    part_keys = jax.random.split(jax.random.fold_in(seeds[9], part), 10)
    query_proj = draw_query_proj(jax.random.fold_in(jax.random.fold_in(seeds[9], part), 71), part)
    key_proj = centred(part_keys[1], (SEQUENCE_LENGTH, INNER), 1.0, 6.0, ((0, 4), (1, 4)))
    value_proj = draw_value_proj(jax.random.fold_in(jax.random.fold_in(seeds[9], part), 71), part)
    gate_proj = centred(part_keys[3], (SEQUENCE_LENGTH, INNER), 1.0, 6.0, ((0, 4), (1, 4)))
    log_decay = draw_log_decay(jax.random.fold_in(jax.random.fold_in(seeds[9], part), 71), part)
    act_exponent = place_ends(jax.random.randint(seeds[5], (3, INNER), -5, -1), jax.random.fold_in(seeds[5], 1), -5, (-1) - 1).astype(jnp.int32)
    norm_gain = jnp.clip(1.0 + 0.18 * jax.random.normal(seeds[6], (INNER,), jnp.float32), 0.1, 1.9)
    out_weight = centred(seeds[7], (INNER, D), INNER ** -0.5, 0.09375, ((0, 4), (1, 4)))
    weight_exponent = place_ends(jax.random.randint(seeds[8], (D,), -12, -8), jax.random.fold_in(seeds[8], 1), -12, (-8) - 1).astype(jnp.int32)
    return dict(query_proj=query_proj, key_proj=key_proj, value_proj=value_proj, gate_proj=gate_proj, log_decay=log_decay, act_exponent=act_exponent, norm_gain=norm_gain, out_weight=out_weight, weight_exponent=weight_exponent)


def power_two(exponent):
    result = jnp.zeros(exponent.shape, jnp.float32)
    for exponent_value in range(-16, 0):
        result = result + jnp.where(exponent == exponent_value, 2.0 ** exponent_value, 0.0)
    return result

def fake_quant(matrix, exponent):
    scale = power_two(exponent)
    levels = jnp.clip(jnp.floor(matrix.astype(jnp.float32) / scale + 0.5), -127.0, 127.0)
    return (levels * scale).astype(jnp.bfloat16)

def reference(query_proj, key_proj, value_proj, gate_proj, log_decay, act_exponent, norm_gain, out_weight, weight_exponent):
    queries = fake_quant(query_proj, act_exponent[0][None, :])
    keys_quant = fake_quant(key_proj, act_exponent[1][None, :])
    values = fake_quant(value_proj, act_exponent[2][None, :])
    weights = fake_quant(out_weight, weight_exponent[None, :])
    query_feat = jax.nn.silu(queries.astype(jnp.float32)).astype(jnp.bfloat16)
    key_feat = jax.nn.silu(keys_quant.astype(jnp.float32)).astype(jnp.bfloat16)
    nblocks = SEQUENCE_LENGTH // BLK
    causal_mask = jnp.arange(BLK)[:, None] >= jnp.arange(BLK)[None, :]

    def one_head(head_index):
        first_col = (head_index * HDIM).astype(jnp.int32)
        head_query = lax.dynamic_slice_in_dim(query_feat, first_col, HDIM, 1).reshape(nblocks, BLK, HDIM)
        head_key = lax.dynamic_slice_in_dim(key_feat, first_col, HDIM, 1).reshape(nblocks, BLK, HDIM)
        head_value = lax.dynamic_slice_in_dim(values, first_col, HDIM, 1).reshape(nblocks, BLK, HDIM)
        head_decay = lax.dynamic_slice_in_dim(log_decay, head_index.astype(jnp.int32), 1, 0).reshape(nblocks, BLK)

        def advance(state, inputs):
            block_query, block_key, block_value, block_decay = inputs
            cumulative = jnp.cumsum(block_decay)
            scores = jnp.dot(block_query, block_key.T, preferred_element_type=jnp.float32)
            decay_gap = cumulative[:, None] - cumulative[None, :]
            decay_mask = jnp.where(causal_mask, jnp.exp(jnp.minimum(decay_gap, 0.0)), 0.0)
            block_probs = (scores * decay_mask).astype(jnp.bfloat16)
            within_block = jnp.dot(block_probs, block_value, preferred_element_type=jnp.float32)
            from_state = jnp.exp(cumulative)[:, None] * jnp.dot(block_query.astype(jnp.float32), state, precision=lax.Precision.HIGHEST)
            weighted = (block_key.astype(jnp.float32) * jnp.exp(cumulative[-1] - cumulative)[:, None]).astype(jnp.bfloat16)
            new_state = jnp.exp(cumulative[-1]) * state + jnp.dot(weighted.T, block_value, preferred_element_type=jnp.float32)
            return (new_state, within_block + from_state)
        _, outputs = lax.scan(advance, jnp.zeros((HDIM, HDIM), jnp.float32), (head_query, head_key, head_value, head_decay))
        return outputs.reshape(SEQUENCE_LENGTH, HDIM)
    heads_out = lax.map(one_head, jnp.arange(HEAD_COUNT, dtype=jnp.int32))
    mean_square = lax.optimization_barrier(jnp.mean(heads_out * heads_out, axis=-1, keepdims=True))
    normed = heads_out * lax.rsqrt(mean_square + 1e-05)
    normed = jnp.transpose(normed, (1, 0, 2)).reshape(SEQUENCE_LENGTH, INNER)
    attn = (normed * norm_gain[None, :] * jax.nn.sigmoid(gate_proj.astype(jnp.float32))).astype(jnp.bfloat16)
    return jnp.dot(attn, weights, preferred_element_type=jnp.float32).astype(jnp.bfloat16)
```

```python
import jax
import jax.numpy as jnp
from jax import lax
from jax.sharding import PartitionSpec as P

HDIM = 128
BLK = 256


def power_two(exponent):
    result = jnp.zeros(exponent.shape, jnp.float32)
    for exponent_value in range(-16, 0):
        result = result + jnp.where(exponent == exponent_value, 2.0**exponent_value, 0.0)
    return result


def fake_quant(matrix, exponent):
    scale = power_two(exponent)
    levels = jnp.clip(jnp.floor(matrix.astype(jnp.float32) / scale + 0.5), -127.0, 127.0)
    return (levels * scale).astype(jnp.bfloat16)


def per_device(
    n_seq,
    n_mdl,
    query_proj,
    key_proj,
    value_proj,
    gate_proj,
    log_decay,
    act_exponent,
    norm_gain,
    out_weight,
    weight_exponent,
):
    weights = fake_quant(out_weight, weight_exponent[None, :])
    tok_rows = query_proj.shape[0]
    feat_here = query_proj.shape[1]
    heads_here = log_decay.shape[0]
    nblocks = tok_rows // BLK
    queries = fake_quant(query_proj, act_exponent[0][None, :])
    keys_quant = fake_quant(key_proj, act_exponent[1][None, :])
    values = fake_quant(value_proj, act_exponent[2][None, :]).reshape(
        nblocks, BLK, heads_here, HDIM
    )
    query_feat = (
        jax.nn.silu(queries.astype(jnp.float32))
        .astype(jnp.bfloat16)
        .reshape(nblocks, BLK, heads_here, HDIM)
    )
    key_feat = (
        jax.nn.silu(keys_quant.astype(jnp.float32))
        .astype(jnp.bfloat16)
        .reshape(nblocks, BLK, heads_here, HDIM)
    )
    decay_cum = jnp.cumsum(log_decay.reshape(heads_here, nblocks, BLK), axis=2)
    block_total = decay_cum[:, :, -1]
    scores = jnp.einsum("bihd,bjhd->hbij", query_feat, key_feat, preferred_element_type=jnp.float32)
    decay_gap = decay_cum[:, :, :, None] - decay_cum[:, :, None, :]
    causal_mask = jnp.arange(BLK)[:, None] >= jnp.arange(BLK)[None, :]
    decay_mask = jnp.where(causal_mask, jnp.exp(jnp.minimum(decay_gap, 0.0)), 0.0)
    block_probs = (scores * decay_mask).astype(jnp.bfloat16)
    within_block = jnp.einsum(
        "hbij,bjhd->bihd", block_probs, values, preferred_element_type=jnp.float32
    )
    tail_decay = jnp.transpose(jnp.exp(block_total[:, :, None] - decay_cum), (1, 2, 0))
    weighted = (key_feat.astype(jnp.float32) * tail_decay[..., None]).astype(jnp.bfloat16)
    block_states = jnp.einsum(
        "bjhd,bjhe->bhde", weighted, values, preferred_element_type=jnp.float32
    )
    block_gain = jnp.exp(block_total).T

    def advance(carried, inputs):
        gain_here, state_here = inputs
        return (gain_here[:, None, None] * carried + state_here, carried)

    local_end, entry_local = lax.scan(
        advance, jnp.zeros((heads_here, HDIM, HDIM), jnp.float32), (block_gain, block_states)
    )
    device_log = jnp.sum(block_total, axis=1)
    packed = jnp.concatenate(
        [
            local_end.reshape(heads_here, HDIM * HDIM),
            jnp.broadcast_to(device_log[:, None], (heads_here, HDIM)),
        ],
        axis=1,
    )
    gathered = lax.all_gather(packed, "seq", axis=0, tiled=False)
    gathered_states = gathered[:, :, : HDIM * HDIM].reshape(n_seq, heads_here, HDIM, HDIM)
    gathered_logs = gathered[:, :, HDIM * HDIM]
    position = lax.axis_index("seq")
    end_offsets = jnp.cumsum(gathered_logs, axis=0)
    start_offsets = end_offsets - gathered_logs
    own_start = lax.dynamic_index_in_dim(start_offsets, position, 0, keepdims=False)
    earlier = jnp.arange(gathered_logs.shape[0])[:, None] < position
    state_weight = jnp.where(
        earlier, jnp.exp(jnp.minimum(own_start[None, :] - end_offsets, 0.0)), 0.0
    )
    incoming = jnp.einsum(
        "nh,nhde->hde", state_weight, gathered_states, precision=lax.Precision.HIGHEST
    )
    before = jnp.cumsum(block_total, axis=1) - block_total
    entry_state = entry_local + jnp.exp(before).T[:, :, None, None] * incoming[None]
    from_state = jnp.einsum(
        "bihd,bhde->bihe",
        query_feat.astype(jnp.float32),
        entry_state,
        precision=lax.Precision.HIGHEST,
    )
    position_decay = jnp.transpose(jnp.exp(decay_cum), (1, 2, 0))[..., None]
    attended = within_block + position_decay * from_state
    mean_square = jnp.mean(attended * attended, axis=-1, keepdims=True)
    normed = (attended * lax.rsqrt(mean_square + 1e-05)).reshape(tok_rows, heads_here * HDIM)
    attn = (normed * norm_gain[None, :] * jax.nn.sigmoid(gate_proj.astype(jnp.float32))).astype(
        jnp.bfloat16
    )

    rows_w = out_weight.shape[0]
    blocks_here = feat_here // rows_w
    piece = rows_w // n_mdl
    x = attn.reshape(tok_rows, blocks_here, n_mdl, piece)
    x = jnp.transpose(x, (2, 0, 1, 3))
    x = lax.all_to_all(x, "mdl", 0, 0)
    x = jnp.transpose(x, (0, 2, 1, 3)).reshape(n_seq, tok_rows, piece)
    x = lax.all_to_all(x, "seq", 0, 0)
    x = lax.all_gather(x, "mdl", axis=0, tiled=False)
    partial = jnp.einsum(
        "usti,uic->stc",
        x,
        weights.reshape(n_mdl, piece, weights.shape[1]),
        preferred_element_type=jnp.float32,
    ).astype(jnp.bfloat16)
    partial = partial.reshape(n_seq * tok_rows, weights.shape[1])
    return lax.psum_scatter(partial, "seq", scatter_dimension=0, tiled=True)


def solution(mesh):
    in_specs = (
        P(("grp", "seq"), "mdl"),
        P(("grp", "seq"), "mdl"),
        P(("grp", "seq"), "mdl"),
        P(("grp", "seq"), "mdl"),
        P("mdl", ("grp", "seq")),
        P(None, "mdl"),
        P("mdl"),
        P("seq", "mdl"),
        P("mdl"),
    )
    out_specs = P(("grp", "seq"), "mdl")
    n_seq = mesh.shape["seq"]
    n_mdl = mesh.shape["mdl"]

    def body(*args):
        return per_device(n_seq, n_mdl, *args)

    return jax.shard_map(
        body, mesh=mesh, in_specs=in_specs, out_specs=out_specs, check_vma=False
    )
```

```python
import jax
import jax.numpy as jnp
from jax import lax
from jax.sharding import PartitionSpec as P

HDIM = 128
BLK = 256


def power_two(exponent):
    result = jnp.zeros(exponent.shape, jnp.float32)
    for exponent_value in range(-16, 0):
        result = result + jnp.where(exponent == exponent_value, 2.0**exponent_value, 0.0)
    return result


def fake_quant(matrix, exponent):
    scale = power_two(exponent)
    levels = jnp.clip(jnp.floor(matrix.astype(jnp.float32) / scale + 0.5), -127.0, 127.0)
    return (levels * scale).astype(jnp.bfloat16)


def per_device(
    n_seq,
    n_mdl,
    query_proj,
    key_proj,
    value_proj,
    gate_proj,
    log_decay,
    act_exponent,
    norm_gain,
    out_weight,
    weight_exponent,
):
    weights = fake_quant(out_weight, weight_exponent[None, :])
    tok_rows = query_proj.shape[0]
    feat_here = query_proj.shape[1]
    heads_here = log_decay.shape[0]
    nblocks = tok_rows // BLK
    queries = fake_quant(query_proj, act_exponent[0][None, :])
    keys_quant = fake_quant(key_proj, act_exponent[1][None, :])
    values = fake_quant(value_proj, act_exponent[2][None, :]).reshape(
        nblocks, BLK, heads_here, HDIM
    )
    query_feat = (
        jax.nn.silu(queries.astype(jnp.float32))
        .astype(jnp.bfloat16)
        .reshape(nblocks, BLK, heads_here, HDIM)
    )
    key_feat = (
        jax.nn.silu(keys_quant.astype(jnp.float32))
        .astype(jnp.bfloat16)
        .reshape(nblocks, BLK, heads_here, HDIM)
    )
    decay_cum = jnp.cumsum(log_decay.reshape(heads_here, nblocks, BLK), axis=2)
    block_total = decay_cum[:, :, -1]
    scores = jnp.einsum("bihd,bjhd->hbij", query_feat, key_feat, preferred_element_type=jnp.float32)
    decay_gap = decay_cum[:, :, :, None] - decay_cum[:, :, None, :]
    causal_mask = jnp.arange(BLK)[:, None] >= jnp.arange(BLK)[None, :]
    decay_mask = jnp.where(causal_mask, jnp.exp(jnp.minimum(decay_gap, 0.0)), 0.0)
    block_probs = (scores * decay_mask).astype(jnp.bfloat16)
    within_block = jnp.einsum(
        "hbij,bjhd->bihd", block_probs, values, preferred_element_type=jnp.float32
    )
    tail_decay = jnp.transpose(jnp.exp(block_total[:, :, None] - decay_cum), (1, 2, 0))
    weighted = (key_feat.astype(jnp.float32) * tail_decay[..., None]).astype(jnp.bfloat16)
    block_states = jnp.einsum(
        "bjhd,bjhe->bhde", weighted, values, preferred_element_type=jnp.float32
    )
    block_gain = jnp.exp(block_total).T

    def advance(carried, inputs):
        gain_here, state_here = inputs
        return (gain_here[:, None, None] * carried + state_here, carried)

    local_end, entry_local = lax.scan(
        advance, jnp.zeros((heads_here, HDIM, HDIM), jnp.float32), (block_gain, block_states)
    )
    device_log = jnp.sum(block_total, axis=1)
    log_hi = device_log.astype(jnp.bfloat16)
    log_lo = (device_log - log_hi.astype(jnp.float32)).astype(jnp.bfloat16)
    packed = jnp.concatenate(
        [
            local_end.astype(jnp.bfloat16).reshape(heads_here, HDIM * HDIM),
            jnp.broadcast_to(log_hi[:, None], (heads_here, HDIM)),
            jnp.broadcast_to(log_lo[:, None], (heads_here, HDIM)),
        ],
        axis=1,
    )
    gathered = lax.all_gather(packed, "seq", axis=0, tiled=False)
    gathered_states = (
        gathered[:, :, : HDIM * HDIM].astype(jnp.float32).reshape(n_seq, heads_here, HDIM, HDIM)
    )
    gathered_logs = gathered[:, :, HDIM * HDIM].astype(jnp.float32) + gathered[
        :, :, HDIM * HDIM + HDIM
    ].astype(jnp.float32)
    position = lax.axis_index("seq")
    end_offsets = jnp.cumsum(gathered_logs, axis=0)
    start_offsets = end_offsets - gathered_logs
    own_start = lax.dynamic_index_in_dim(start_offsets, position, 0, keepdims=False)
    earlier = jnp.arange(gathered_logs.shape[0])[:, None] < position
    state_weight = jnp.where(
        earlier, jnp.exp(jnp.minimum(own_start[None, :] - end_offsets, 0.0)), 0.0
    )
    incoming = jnp.einsum(
        "nh,nhde->hde", state_weight, gathered_states, precision=lax.Precision.HIGHEST
    )
    before = jnp.cumsum(block_total, axis=1) - block_total
    entry_state = entry_local + jnp.exp(before).T[:, :, None, None] * incoming[None]
    from_state = jnp.einsum(
        "bihd,bhde->bihe",
        query_feat.astype(jnp.float32),
        entry_state,
        precision=lax.Precision.HIGHEST,
    )
    position_decay = jnp.transpose(jnp.exp(decay_cum), (1, 2, 0))[..., None]
    attended = within_block + position_decay * from_state
    mean_square = jnp.mean(attended * attended, axis=-1, keepdims=True)
    normed = (attended * lax.rsqrt(mean_square + 1e-05)).reshape(tok_rows, heads_here * HDIM)
    attn = (normed * norm_gain[None, :] * jax.nn.sigmoid(gate_proj.astype(jnp.float32))).astype(
        jnp.bfloat16
    )

    rows_w = out_weight.shape[0]
    blocks_here = feat_here // rows_w
    piece = rows_w // n_mdl
    s_me = lax.axis_index("seq")
    m_me = lax.axis_index("mdl")
    pieces = jnp.transpose(attn.reshape(tok_rows, n_seq, piece), (1, 0, 2))
    pieces = jnp.roll(pieces, -s_me, axis=0)
    received = []
    for k in range(n_seq):
        perm = []
        for s in range(n_seq):
            for m in range(n_mdl):
                j = (s + k) % n_seq
                f = m * blocks_here + j // n_mdl
                perm.append((s * n_mdl + m, f * n_mdl + j % n_mdl))
        received.append(lax.ppermute(pieces[k], ("seq", "mdl"), perm))
    received = jnp.stack(received)
    j_me = (s_me % blocks_here) * n_mdl + m_me
    x = jnp.roll(jnp.flip(received, 0), j_me + 1, axis=0)
    x = lax.all_gather(x, "mdl", axis=0, tiled=False)
    partial = jnp.einsum(
        "usti,uic->stc",
        x,
        weights.reshape(n_mdl, piece, weights.shape[1]),
        preferred_element_type=jnp.float32,
    ).astype(jnp.bfloat16)
    partial = partial.reshape(n_seq * tok_rows, weights.shape[1])
    return lax.psum_scatter(partial, "seq", scatter_dimension=0, tiled=True)


def solution(mesh):
    in_specs = (
        P(("grp", "seq"), "mdl"),
        P(("grp", "seq"), "mdl"),
        P(("grp", "seq"), "mdl"),
        P(("grp", "seq"), "mdl"),
        P("mdl", ("grp", "seq")),
        P(None, "mdl"),
        P("mdl"),
        P("seq", "mdl"),
        P("mdl"),
    )
    out_specs = P(("grp", "seq"), "mdl")
    n_seq = mesh.shape["seq"]
    n_mdl = mesh.shape["mdl"]

    def body(*args):
        return per_device(n_seq, n_mdl, *args)

    return jax.shard_map(
        body, mesh=mesh, in_specs=in_specs, out_specs=out_specs, check_vma=False
    )
```

```python
import jax
import jax.numpy as jnp
from jax import lax
from jax.sharding import PartitionSpec as P

HDIM = 128
BLK = 256


def power_two(exponent):
    result = jnp.zeros(exponent.shape, jnp.float32)
    for exponent_value in range(-16, 0):
        result = result + jnp.where(exponent == exponent_value, 2.0**exponent_value, 0.0)
    return result


def fake_quant(matrix, exponent):
    scale = power_two(exponent)
    levels = jnp.clip(jnp.floor(matrix.astype(jnp.float32) / scale + 0.5), -127.0, 127.0)
    return (levels * scale).astype(jnp.bfloat16)


def per_device(
    n_seq,
    n_mdl,
    query_proj,
    key_proj,
    value_proj,
    gate_proj,
    log_decay,
    act_exponent,
    norm_gain,
    out_weight,
    weight_exponent,
):
    weights = fake_quant(out_weight, weight_exponent[None, :])
    tok_rows = query_proj.shape[0]
    feat_here = query_proj.shape[1]
    heads_here = log_decay.shape[0]
    nblocks = tok_rows // BLK
    queries = fake_quant(query_proj, act_exponent[0][None, :])
    keys_quant = fake_quant(key_proj, act_exponent[1][None, :])
    values = fake_quant(value_proj, act_exponent[2][None, :]).reshape(
        nblocks, BLK, heads_here, HDIM
    )
    query_feat = (
        jax.nn.silu(queries.astype(jnp.float32))
        .astype(jnp.bfloat16)
        .reshape(nblocks, BLK, heads_here, HDIM)
    )
    key_feat = (
        jax.nn.silu(keys_quant.astype(jnp.float32))
        .astype(jnp.bfloat16)
        .reshape(nblocks, BLK, heads_here, HDIM)
    )
    decay_cum = jnp.cumsum(log_decay.reshape(heads_here, nblocks, BLK), axis=2)
    block_total = decay_cum[:, :, -1]
    scores = jnp.einsum("bihd,bjhd->hbij", query_feat, key_feat, preferred_element_type=jnp.float32)
    decay_gap = decay_cum[:, :, :, None] - decay_cum[:, :, None, :]
    causal_mask = jnp.arange(BLK)[:, None] >= jnp.arange(BLK)[None, :]
    decay_mask = jnp.where(causal_mask, jnp.exp(jnp.minimum(decay_gap, 0.0)), 0.0)
    block_probs = (scores * decay_mask).astype(jnp.bfloat16)
    within_block = jnp.einsum(
        "hbij,bjhd->bihd", block_probs, values, preferred_element_type=jnp.float32
    )
    tail_decay = jnp.transpose(jnp.exp(block_total[:, :, None] - decay_cum), (1, 2, 0))
    weighted = (key_feat.astype(jnp.float32) * tail_decay[..., None]).astype(jnp.bfloat16)
    block_states = jnp.einsum(
        "bjhd,bjhe->bhde", weighted, values, preferred_element_type=jnp.float32
    )
    block_gain = jnp.exp(block_total).T

    def advance(carried, inputs):
        gain_here, state_here = inputs
        return (gain_here[:, None, None] * carried + state_here, carried)

    local_end, entry_local = lax.scan(
        advance, jnp.zeros((heads_here, HDIM, HDIM), jnp.float32), (block_gain, block_states)
    )
    device_log = jnp.sum(block_total, axis=1)
    log_hi = device_log.astype(jnp.bfloat16)
    log_lo = (device_log - log_hi.astype(jnp.float32)).astype(jnp.bfloat16)
    packed = jnp.concatenate(
        [
            local_end.astype(jnp.bfloat16).reshape(heads_here, HDIM * HDIM),
            jnp.broadcast_to(log_hi[:, None], (heads_here, HDIM)),
            jnp.broadcast_to(log_lo[:, None], (heads_here, HDIM)),
        ],
        axis=1,
    )
    gathered = lax.all_gather(packed, "seq", axis=0, tiled=False)
    gathered_states = (
        gathered[:, :, : HDIM * HDIM].astype(jnp.float32).reshape(n_seq, heads_here, HDIM, HDIM)
    )
    gathered_logs = gathered[:, :, HDIM * HDIM].astype(jnp.float32) + gathered[
        :, :, HDIM * HDIM + HDIM
    ].astype(jnp.float32)
    position = lax.axis_index("seq")
    end_offsets = jnp.cumsum(gathered_logs, axis=0)
    start_offsets = end_offsets - gathered_logs
    own_start = lax.dynamic_index_in_dim(start_offsets, position, 0, keepdims=False)
    earlier = jnp.arange(gathered_logs.shape[0])[:, None] < position
    state_weight = jnp.where(
        earlier, jnp.exp(jnp.minimum(own_start[None, :] - end_offsets, 0.0)), 0.0
    )
    incoming = jnp.einsum(
        "nh,nhde->hde", state_weight, gathered_states, precision=lax.Precision.HIGHEST
    )
    before = jnp.cumsum(block_total, axis=1) - block_total
    entry_state = entry_local + jnp.exp(before).T[:, :, None, None] * incoming[None]
    from_state = jnp.einsum(
        "bihd,bhde->bihe",
        query_feat.astype(jnp.float32),
        entry_state,
        precision=lax.Precision.HIGHEST,
    )
    position_decay = jnp.transpose(jnp.exp(decay_cum), (1, 2, 0))[..., None]
    attended = within_block + position_decay * from_state
    mean_square = jnp.mean(attended * attended, axis=-1, keepdims=True)
    normed = (attended * lax.rsqrt(mean_square + 1e-05)).reshape(tok_rows, heads_here * HDIM)
    attn = (normed * norm_gain[None, :] * jax.nn.sigmoid(gate_proj.astype(jnp.float32))).astype(
        jnp.bfloat16
    )

    rows_w, cols_w = weights.shape
    blocks_here = feat_here // rows_w
    piece = rows_w // n_mdl
    s_me = lax.axis_index("seq")
    m_me = lax.axis_index("mdl")
    received = []
    for k in range(n_seq):
        perm = []
        for s in range(n_seq):
            for m in range(n_mdl):
                j = (s + k) % n_seq
                f = m * blocks_here + j // n_mdl
                perm.append((s * n_mdl + m, f * n_mdl + j % n_mdl))
        j_send = (s_me + k) % n_seq
        chunk = lax.dynamic_slice_in_dim(attn, j_send * piece, piece, axis=1)
        received.append(lax.ppermute(chunk, ("seq", "mdl"), perm))
    received = jnp.stack(received)
    j_me = (s_me % blocks_here) * n_mdl + m_me
    x = jnp.take(received, (j_me - jnp.arange(n_seq)) % n_seq, axis=0)

    n_x = n_mdl // 2
    core = m_me % 2
    xi = m_me // 2
    got = [x]
    for d in range(1, n_x):
        perm = [(mu, ((mu // 2 + d) % n_x) * 2 + mu % 2) for mu in range(n_mdl)]
        got.append(lax.ppermute(x, "mdl", perm))
    own = jnp.stack(got)
    other = lax.ppermute(own, "mdl", [(mu, mu ^ 1) for mu in range(n_mdl)])
    gathered_x = jnp.stack([own, other], axis=1)
    d_idx = jnp.arange(n_x)[:, None]
    e_idx = jnp.arange(2)[None, :]
    mu_tab = 2 * ((xi - d_idx) % n_x) + jnp.where(e_idx == 0, core, 1 - core)
    w_perm = jnp.take(
        weights.reshape(n_mdl, piece, cols_w), mu_tab.reshape(-1), axis=0
    ).reshape(n_x, 2, piece, cols_w)
    acc = jnp.einsum(
        "desti,deic->stc", gathered_x, w_perm, preferred_element_type=jnp.float32
    )

    for i in range(1, n_seq):
        t_r = jnp.clip(s_me + n_seq - i, 0, n_seq - 1)
        t_l = jnp.clip(s_me - n_seq + i, 0, n_seq - 1)
        send_r = lax.dynamic_index_in_dim(acc, t_r, 0, keepdims=False).astype(jnp.bfloat16)
        send_l = lax.dynamic_index_in_dim(acc, t_l, 0, keepdims=False).astype(jnp.bfloat16)
        recv_r = lax.ppermute(send_r, "seq", [(z, z + 1) for z in range(i)])
        recv_l = lax.ppermute(send_l, "seq", [(z, z - 1) for z in range(n_seq - i, n_seq)])
        u_r = jnp.clip(s_me - 1 + n_seq - i, 0, n_seq - 1)
        u_l = jnp.clip(s_me + 1 - n_seq + i, 0, n_seq - 1)
        acc = acc.at[u_r].add(recv_r.astype(jnp.float32))
        acc = acc.at[u_l].add(recv_l.astype(jnp.float32))
    return lax.dynamic_index_in_dim(acc, s_me, 0, keepdims=False).astype(jnp.bfloat16)


def solution(mesh):
    in_specs = (
        P(("grp", "seq"), "mdl"),
        P(("grp", "seq"), "mdl"),
        P(("grp", "seq"), "mdl"),
        P(("grp", "seq"), "mdl"),
        P("mdl", ("grp", "seq")),
        P(None, "mdl"),
        P("mdl"),
        P("seq", "mdl"),
        P("mdl"),
    )
    out_specs = P(("grp", "seq"), "mdl")
    n_seq = mesh.shape["seq"]
    n_mdl = mesh.shape["mdl"]

    def body(*args):
        return per_device(n_seq, n_mdl, *args)

    return jax.shard_map(
        body, mesh=mesh, in_specs=in_specs, out_specs=out_specs, check_vma=False
    )
```

```python
import jax
import jax.numpy as jnp
from jax import lax
from jax.sharding import PartitionSpec as P

HDIM = 128
BLK = 256


def power_two(exponent):
    result = jnp.zeros(exponent.shape, jnp.float32)
    for exponent_value in range(-16, 0):
        result = result + jnp.where(exponent == exponent_value, 2.0**exponent_value, 0.0)
    return result


def fake_quant(matrix, exponent):
    scale = power_two(exponent)
    levels = jnp.clip(jnp.floor(matrix.astype(jnp.float32) / scale + 0.5), -127.0, 127.0)
    return (levels * scale).astype(jnp.bfloat16)


def per_device(
    n_seq,
    n_mdl,
    query_proj,
    key_proj,
    value_proj,
    gate_proj,
    log_decay,
    act_exponent,
    norm_gain,
    out_weight,
    weight_exponent,
):
    weights = fake_quant(out_weight, weight_exponent[None, :])
    tok_rows = query_proj.shape[0]
    feat_here = query_proj.shape[1]
    heads_here = log_decay.shape[0]
    nblocks = tok_rows // BLK
    queries = fake_quant(query_proj, act_exponent[0][None, :])
    keys_quant = fake_quant(key_proj, act_exponent[1][None, :])
    values = fake_quant(value_proj, act_exponent[2][None, :]).reshape(
        nblocks, BLK, heads_here, HDIM
    )
    query_feat = (
        jax.nn.silu(queries.astype(jnp.float32))
        .astype(jnp.bfloat16)
        .reshape(nblocks, BLK, heads_here, HDIM)
    )
    key_feat = (
        jax.nn.silu(keys_quant.astype(jnp.float32))
        .astype(jnp.bfloat16)
        .reshape(nblocks, BLK, heads_here, HDIM)
    )
    decay_cum = jnp.cumsum(log_decay.reshape(heads_here, nblocks, BLK), axis=2)
    block_total = decay_cum[:, :, -1]
    scores = jnp.einsum("bihd,bjhd->hbij", query_feat, key_feat, preferred_element_type=jnp.float32)
    decay_gap = decay_cum[:, :, :, None] - decay_cum[:, :, None, :]
    causal_mask = jnp.arange(BLK)[:, None] >= jnp.arange(BLK)[None, :]
    decay_mask = jnp.where(causal_mask, jnp.exp(jnp.minimum(decay_gap, 0.0)), 0.0)
    block_probs = (scores * decay_mask).astype(jnp.bfloat16)
    within_block = jnp.einsum(
        "hbij,bjhd->bihd", block_probs, values, preferred_element_type=jnp.float32
    )
    tail_decay = jnp.transpose(jnp.exp(block_total[:, :, None] - decay_cum), (1, 2, 0))
    weighted = (key_feat.astype(jnp.float32) * tail_decay[..., None]).astype(jnp.bfloat16)
    block_states = jnp.einsum(
        "bjhd,bjhe->bhde", weighted, values, preferred_element_type=jnp.float32
    )
    block_gain = jnp.exp(block_total).T

    def advance(carried, inputs):
        gain_here, state_here = inputs
        return (gain_here[:, None, None] * carried + state_here, carried)

    local_end, entry_local = lax.scan(
        advance, jnp.zeros((heads_here, HDIM, HDIM), jnp.float32), (block_gain, block_states)
    )
    device_log = jnp.sum(block_total, axis=1)
    log_hi = device_log.astype(jnp.bfloat16)
    log_lo = (device_log - log_hi.astype(jnp.float32)).astype(jnp.bfloat16)
    packed = jnp.concatenate(
        [
            local_end.astype(jnp.bfloat16).reshape(heads_here, HDIM * HDIM),
            jnp.broadcast_to(log_hi[:, None], (heads_here, HDIM)),
            jnp.broadcast_to(log_lo[:, None], (heads_here, HDIM)),
        ],
        axis=1,
    )
    gathered = lax.all_gather(packed, "seq", axis=0, tiled=False)
    gathered_states = (
        gathered[:, :, : HDIM * HDIM].astype(jnp.float32).reshape(n_seq, heads_here, HDIM, HDIM)
    )
    gathered_logs = gathered[:, :, HDIM * HDIM].astype(jnp.float32) + gathered[
        :, :, HDIM * HDIM + HDIM
    ].astype(jnp.float32)
    position = lax.axis_index("seq")
    end_offsets = jnp.cumsum(gathered_logs, axis=0)
    start_offsets = end_offsets - gathered_logs
    own_start = lax.dynamic_index_in_dim(start_offsets, position, 0, keepdims=False)
    earlier = jnp.arange(gathered_logs.shape[0])[:, None] < position
    state_weight = jnp.where(
        earlier, jnp.exp(jnp.minimum(own_start[None, :] - end_offsets, 0.0)), 0.0
    )
    incoming = jnp.einsum(
        "nh,nhde->hde", state_weight, gathered_states, precision=lax.Precision.HIGHEST
    )
    before = jnp.cumsum(block_total, axis=1) - block_total
    entry_state = entry_local + jnp.exp(before).T[:, :, None, None] * incoming[None]
    from_state = jnp.einsum(
        "bihd,bhde->bihe",
        query_feat.astype(jnp.float32),
        entry_state,
        precision=lax.Precision.HIGHEST,
    )
    position_decay = jnp.transpose(jnp.exp(decay_cum), (1, 2, 0))[..., None]
    attended = within_block + position_decay * from_state
    mean_square = jnp.mean(attended * attended, axis=-1, keepdims=True)
    normed = (attended * lax.rsqrt(mean_square + 1e-05)).reshape(tok_rows, heads_here * HDIM)
    attn = (normed * norm_gain[None, :] * jax.nn.sigmoid(gate_proj.astype(jnp.float32))).astype(
        jnp.bfloat16
    )

    rows_w, cols_w = weights.shape
    blocks_here = feat_here // rows_w
    piece = rows_w // n_mdl
    s_me = lax.axis_index("seq")
    m_me = lax.axis_index("mdl")
    received = []
    for k in range(n_seq):
        perm = []
        for s in range(n_seq):
            for m in range(n_mdl):
                j = (s + k) % n_seq
                f = m * blocks_here + j // n_mdl
                perm.append((s * n_mdl + m, f * n_mdl + j % n_mdl))
        j_send = (s_me + k) % n_seq
        chunk = lax.dynamic_slice_in_dim(attn, j_send * piece, piece, axis=1)
        received.append(lax.ppermute(chunk, ("seq", "mdl"), perm))
    received = jnp.stack(received)
    j_me = (s_me % blocks_here) * n_mdl + m_me
    x = jnp.take(received, (j_me - jnp.arange(n_seq)) % n_seq, axis=0)

    n_x = n_mdl // 2
    core = m_me % 2
    xi = m_me // 2
    got = [x]
    for d in range(1, n_x):
        perm = [(mu, ((mu // 2 + d) % n_x) * 2 + mu % 2) for mu in range(n_mdl)]
        got.append(lax.ppermute(x, "mdl", perm))
    own = jnp.stack(got)
    other = lax.ppermute(own, "mdl", [(mu, mu ^ 1) for mu in range(n_mdl)])
    gathered_x = jnp.stack([own, other], axis=1)
    d_idx = jnp.arange(n_x)[:, None]
    e_idx = jnp.arange(2)[None, :]
    mu_tab = 2 * ((xi - d_idx) % n_x) + jnp.where(e_idx == 0, core, 1 - core)
    w_perm = jnp.take(
        weights.reshape(n_mdl, piece, cols_w), mu_tab.reshape(-1), axis=0
    ).reshape(n_x, 2, piece, cols_w)

    def partial_for(target):
        rows = lax.dynamic_index_in_dim(gathered_x, target, 2, keepdims=False)
        return jnp.einsum(
            "deti,deic->tc", rows, w_perm, preferred_element_type=jnp.float32
        )

    recv_r = None
    recv_l = None
    for i in range(1, n_seq):
        t_r = jnp.clip(s_me + n_seq - i, 0, n_seq - 1)
        t_l = jnp.clip(s_me - n_seq + i, 0, n_seq - 1)
        send_r = partial_for(t_r)
        send_l = partial_for(t_l)
        if recv_r is not None:
            send_r = send_r + recv_r.astype(jnp.float32)
            send_l = send_l + recv_l.astype(jnp.float32)
        recv_r = lax.ppermute(
            send_r.astype(jnp.bfloat16), "seq", [(z, z + 1) for z in range(i)]
        )
        recv_l = lax.ppermute(
            send_l.astype(jnp.bfloat16), "seq", [(z, z - 1) for z in range(n_seq - i, n_seq)]
        )
    total = partial_for(s_me)
    if recv_r is not None:
        total = total + recv_r.astype(jnp.float32) + recv_l.astype(jnp.float32)
    return total.astype(jnp.bfloat16)


def solution(mesh):
    in_specs = (
        P(("grp", "seq"), "mdl"),
        P(("grp", "seq"), "mdl"),
        P(("grp", "seq"), "mdl"),
        P(("grp", "seq"), "mdl"),
        P("mdl", ("grp", "seq")),
        P(None, "mdl"),
        P("mdl"),
        P("seq", "mdl"),
        P("mdl"),
    )
    out_specs = P(("grp", "seq"), "mdl")
    n_seq = mesh.shape["seq"]
    n_mdl = mesh.shape["mdl"]

    def body(*args):
        return per_device(n_seq, n_mdl, *args)

    return jax.shard_map(
        body, mesh=mesh, in_specs=in_specs, out_specs=out_specs, check_vma=False
    )
```

```python
import jax
import jax.numpy as jnp
from jax import lax
from jax.sharding import PartitionSpec as P

HDIM = 128
BLK = 256


def power_two(exponent):
    result = jnp.zeros(exponent.shape, jnp.float32)
    for exponent_value in range(-16, 0):
        result = result + jnp.where(exponent == exponent_value, 2.0**exponent_value, 0.0)
    return result


def fake_quant(matrix, exponent):
    scale = power_two(exponent)
    levels = jnp.clip(jnp.floor(matrix.astype(jnp.float32) / scale + 0.5), -127.0, 127.0)
    return (levels * scale).astype(jnp.bfloat16)


def per_device(
    n_seq,
    n_mdl,
    query_proj,
    key_proj,
    value_proj,
    gate_proj,
    log_decay,
    act_exponent,
    norm_gain,
    out_weight,
    weight_exponent,
):
    weights = fake_quant(out_weight, weight_exponent[None, :])
    tok_rows = query_proj.shape[0]
    feat_here = query_proj.shape[1]
    heads_here = log_decay.shape[0]
    nblocks = tok_rows // BLK
    queries = fake_quant(query_proj, act_exponent[0][None, :])
    keys_quant = fake_quant(key_proj, act_exponent[1][None, :])
    values = fake_quant(value_proj, act_exponent[2][None, :]).reshape(
        nblocks, BLK, heads_here, HDIM
    )
    query_feat = (
        jax.nn.silu(queries.astype(jnp.float32))
        .astype(jnp.bfloat16)
        .reshape(nblocks, BLK, heads_here, HDIM)
    )
    key_feat = (
        jax.nn.silu(keys_quant.astype(jnp.float32))
        .astype(jnp.bfloat16)
        .reshape(nblocks, BLK, heads_here, HDIM)
    )
    decay_cum = jnp.cumsum(log_decay.reshape(heads_here, nblocks, BLK), axis=2)
    block_total = decay_cum[:, :, -1]
    scores = jnp.einsum("bihd,bjhd->hbij", query_feat, key_feat, preferred_element_type=jnp.float32)
    decay_gap = decay_cum[:, :, :, None] - decay_cum[:, :, None, :]
    causal_mask = jnp.arange(BLK)[:, None] >= jnp.arange(BLK)[None, :]
    decay_mask = jnp.where(causal_mask, jnp.exp(jnp.minimum(decay_gap, 0.0)), 0.0)
    block_probs = (scores * decay_mask).astype(jnp.bfloat16)
    within_block = jnp.einsum(
        "hbij,bjhd->bihd", block_probs, values, preferred_element_type=jnp.float32
    )
    tail_decay = jnp.transpose(jnp.exp(block_total[:, :, None] - decay_cum), (1, 2, 0))
    weighted = (key_feat.astype(jnp.float32) * tail_decay[..., None]).astype(jnp.bfloat16)
    block_states = jnp.einsum(
        "bjhd,bjhe->bhde", weighted, values, preferred_element_type=jnp.float32
    )
    block_gain = jnp.exp(block_total).T

    def advance(carried, inputs):
        gain_here, state_here = inputs
        return (gain_here[:, None, None] * carried + state_here, carried)

    local_end, entry_local = lax.scan(
        advance, jnp.zeros((heads_here, HDIM, HDIM), jnp.float32), (block_gain, block_states)
    )
    device_log = jnp.sum(block_total, axis=1)
    log_hi = device_log.astype(jnp.bfloat16)
    log_lo = (device_log - log_hi.astype(jnp.float32)).astype(jnp.bfloat16)
    packed = jnp.concatenate(
        [
            local_end.astype(jnp.bfloat16).reshape(heads_here, HDIM * HDIM),
            jnp.broadcast_to(log_hi[:, None], (heads_here, HDIM)),
            jnp.broadcast_to(log_lo[:, None], (heads_here, HDIM)),
        ],
        axis=1,
    )
    gathered = lax.all_gather(packed, "seq", axis=0, tiled=False)
    gathered_states = (
        gathered[:, :, : HDIM * HDIM].astype(jnp.float32).reshape(n_seq, heads_here, HDIM, HDIM)
    )
    gathered_logs = gathered[:, :, HDIM * HDIM].astype(jnp.float32) + gathered[
        :, :, HDIM * HDIM + HDIM
    ].astype(jnp.float32)
    position = lax.axis_index("seq")
    end_offsets = jnp.cumsum(gathered_logs, axis=0)
    start_offsets = end_offsets - gathered_logs
    own_start = lax.dynamic_index_in_dim(start_offsets, position, 0, keepdims=False)
    earlier = jnp.arange(gathered_logs.shape[0])[:, None] < position
    state_weight = jnp.where(
        earlier, jnp.exp(jnp.minimum(own_start[None, :] - end_offsets, 0.0)), 0.0
    )
    incoming = jnp.einsum(
        "nh,nhde->hde", state_weight, gathered_states, precision=lax.Precision.HIGHEST
    )
    before = jnp.cumsum(block_total, axis=1) - block_total
    entry_state = entry_local + jnp.exp(before).T[:, :, None, None] * incoming[None]
    from_state = jnp.einsum(
        "bihd,bhde->bihe",
        query_feat.astype(jnp.float32),
        entry_state,
        precision=lax.Precision.HIGHEST,
    )
    position_decay = jnp.transpose(jnp.exp(decay_cum), (1, 2, 0))[..., None]
    attended = within_block + position_decay * from_state
    mean_square = jnp.mean(attended * attended, axis=-1, keepdims=True)
    normed = (attended * lax.rsqrt(mean_square + 1e-05)).reshape(tok_rows, heads_here * HDIM)
    attn = (normed * norm_gain[None, :] * jax.nn.sigmoid(gate_proj.astype(jnp.float32))).astype(
        jnp.bfloat16
    )

    rows_w, cols_w = weights.shape
    blocks_here = feat_here // rows_w
    piece = rows_w // n_mdl
    s_me = lax.axis_index("seq")
    m_me = lax.axis_index("mdl")
    received = []
    for k in range(n_seq):
        perm = []
        for s in range(n_seq):
            for m in range(n_mdl):
                j = (s + k) % n_seq
                f = m * blocks_here + j // n_mdl
                perm.append((s * n_mdl + m, f * n_mdl + j % n_mdl))
        j_send = (s_me + k) % n_seq
        chunk = lax.dynamic_slice_in_dim(attn, j_send * piece, piece, axis=1)
        received.append(lax.ppermute(chunk, ("seq", "mdl"), perm))
    received = jnp.stack(received)
    j_me = (s_me % blocks_here) * n_mdl + m_me
    x = jnp.take(received, (j_me - jnp.arange(n_seq)) % n_seq, axis=0)

    n_x = n_mdl // 2
    core = m_me % 2
    xi = m_me // 2
    got = [x]
    for d in range(1, n_x):
        perm = [(mu, ((mu // 2 + d) % n_x) * 2 + mu % 2) for mu in range(n_mdl)]
        got.append(lax.ppermute(x, "mdl", perm))
    own = jnp.stack(got)
    other = lax.ppermute(own, "mdl", [(mu, mu ^ 1) for mu in range(n_mdl)])
    gathered_x = jnp.stack([own, other], axis=1)
    d_idx = jnp.arange(n_x)[:, None]
    e_idx = jnp.arange(2)[None, :]
    mu_tab = 2 * ((xi - d_idx) % n_x) + jnp.where(e_idx == 0, core, 1 - core)
    w_perm = jnp.take(
        weights.reshape(n_mdl, piece, cols_w), mu_tab.reshape(-1), axis=0
    ).reshape(n_x, 2, piece, cols_w)

    def partial_for(target):
        rows = lax.dynamic_index_in_dim(gathered_x, target, 2, keepdims=False)
        return jnp.einsum(
            "deti,deic->tc", rows, w_perm, preferred_element_type=jnp.float32
        )

    if n_seq > 8:
        partial = jnp.concatenate([partial_for(t) for t in range(n_seq)], axis=0)
        return lax.psum_scatter(
            partial.astype(jnp.bfloat16), "seq", scatter_dimension=0, tiled=True
        )

    parts = [partial_for(t) for t in range(n_seq)]
    total = lax.dynamic_index_in_dim(jnp.stack(parts), s_me, 0, keepdims=False)
    came_r = {}
    for z in range(n_seq - 1):
        for t in range(n_seq - 1, z, -1):
            value = parts[t] if z == 0 else parts[t] + came_r[(z - 1, t)].astype(jnp.float32)
            came_r[(z, t)] = lax.ppermute(value.astype(jnp.bfloat16), "seq", [(z, z + 1)])
    came_l = {}
    for z in range(n_seq - 1, 0, -1):
        for t in range(z):
            value = (
                parts[t] if z == n_seq - 1 else parts[t] + came_l[(z + 1, t)].astype(jnp.float32)
            )
            came_l[(z, t)] = lax.ppermute(value.astype(jnp.bfloat16), "seq", [(z, z - 1)])
    for z in range(1, n_seq):
        total = total + came_r[(z - 1, z)].astype(jnp.float32)
    for z in range(n_seq - 1):
        total = total + came_l[(z + 1, z)].astype(jnp.float32)
    return total.astype(jnp.bfloat16)


def solution(mesh):
    in_specs = (
        P(("grp", "seq"), "mdl"),
        P(("grp", "seq"), "mdl"),
        P(("grp", "seq"), "mdl"),
        P(("grp", "seq"), "mdl"),
        P("mdl", ("grp", "seq")),
        P(None, "mdl"),
        P("mdl"),
        P("seq", "mdl"),
        P("mdl"),
    )
    out_specs = P(("grp", "seq"), "mdl")
    n_seq = mesh.shape["seq"]
    n_mdl = mesh.shape["mdl"]

    def body(*args):
        return per_device(n_seq, n_mdl, *args)

    return jax.shard_map(
        body, mesh=mesh, in_specs=in_specs, out_specs=out_specs, check_vma=False
    )
```

```python
import jax
import jax.numpy as jnp
from jax import lax
from jax.sharding import PartitionSpec as P

HDIM = 128
BLK = 256


def power_two(exponent):
    result = jnp.zeros(exponent.shape, jnp.float32)
    for exponent_value in range(-16, 0):
        result = result + jnp.where(exponent == exponent_value, 2.0**exponent_value, 0.0)
    return result


def fake_quant(matrix, exponent):
    scale = power_two(exponent)
    levels = jnp.clip(jnp.floor(matrix.astype(jnp.float32) / scale + 0.5), -127.0, 127.0)
    return (levels * scale).astype(jnp.bfloat16)


def per_device(
    n_seq,
    n_mdl,
    query_proj,
    key_proj,
    value_proj,
    gate_proj,
    log_decay,
    act_exponent,
    norm_gain,
    out_weight,
    weight_exponent,
):
    tok_rows = query_proj.shape[0]
    feat_here = query_proj.shape[1]
    heads_here = log_decay.shape[0]
    nblocks = tok_rows // BLK
    queries = fake_quant(query_proj, act_exponent[0][None, :])
    keys_quant = fake_quant(key_proj, act_exponent[1][None, :])
    values = fake_quant(value_proj, act_exponent[2][None, :]).reshape(
        nblocks, BLK, heads_here, HDIM
    )
    query_feat = (
        jax.nn.silu(queries.astype(jnp.float32))
        .astype(jnp.bfloat16)
        .reshape(nblocks, BLK, heads_here, HDIM)
    )
    key_feat = (
        jax.nn.silu(keys_quant.astype(jnp.float32))
        .astype(jnp.bfloat16)
        .reshape(nblocks, BLK, heads_here, HDIM)
    )
    decay_cum = jnp.cumsum(log_decay.reshape(heads_here, nblocks, BLK), axis=2)
    block_total = decay_cum[:, :, -1]
    scores = jnp.einsum("bihd,bjhd->hbij", query_feat, key_feat, preferred_element_type=jnp.float32)
    decay_gap = decay_cum[:, :, :, None] - decay_cum[:, :, None, :]
    causal_mask = jnp.arange(BLK)[:, None] >= jnp.arange(BLK)[None, :]
    decay_mask = jnp.where(causal_mask, jnp.exp(jnp.minimum(decay_gap, 0.0)), 0.0)
    block_probs = (scores * decay_mask).astype(jnp.bfloat16)
    within_block = jnp.einsum(
        "hbij,bjhd->bihd", block_probs, values, preferred_element_type=jnp.float32
    )
    weights = fake_quant(out_weight, weight_exponent[None, :])
    rows_w, cols_w = weights.shape
    piece = rows_w // n_mdl
    n_x = n_mdl // 2
    m_me = lax.axis_index("mdl")
    core = m_me % 2
    xi = m_me // 2
    d_idx = jnp.arange(n_x)[:, None]
    e_idx = jnp.arange(2)[None, :]
    mu_tab = 2 * ((xi - d_idx) % n_x) + jnp.where(e_idx == 0, core, 1 - core)
    w_perm = jnp.take(
        weights.reshape(n_mdl, piece, cols_w), mu_tab.reshape(-1), axis=0
    ).reshape(n_x, 2, piece, cols_w)
    within_block, w_perm = lax.optimization_barrier((within_block, w_perm))
    tail_decay = jnp.transpose(jnp.exp(block_total[:, :, None] - decay_cum), (1, 2, 0))
    weighted = (key_feat.astype(jnp.float32) * tail_decay[..., None]).astype(jnp.bfloat16)
    block_states = jnp.einsum(
        "bjhd,bjhe->bhde", weighted, values, preferred_element_type=jnp.float32
    )
    block_gain = jnp.exp(block_total).T

    def advance(carried, inputs):
        gain_here, state_here = inputs
        return (gain_here[:, None, None] * carried + state_here, carried)

    local_end, entry_local = lax.scan(
        advance, jnp.zeros((heads_here, HDIM, HDIM), jnp.float32), (block_gain, block_states)
    )
    device_log = jnp.sum(block_total, axis=1)
    log_hi = device_log.astype(jnp.bfloat16)
    log_lo = (device_log - log_hi.astype(jnp.float32)).astype(jnp.bfloat16)
    packed = jnp.concatenate(
        [
            local_end.astype(jnp.bfloat16).reshape(heads_here, HDIM * HDIM),
            jnp.broadcast_to(log_hi[:, None], (heads_here, HDIM)),
            jnp.broadcast_to(log_lo[:, None], (heads_here, HDIM)),
        ],
        axis=1,
    )
    gathered = lax.all_gather(packed, "seq", axis=0, tiled=False)
    gathered_states = (
        gathered[:, :, : HDIM * HDIM].astype(jnp.float32).reshape(n_seq, heads_here, HDIM, HDIM)
    )
    gathered_logs = gathered[:, :, HDIM * HDIM].astype(jnp.float32) + gathered[
        :, :, HDIM * HDIM + HDIM
    ].astype(jnp.float32)
    position = lax.axis_index("seq")
    end_offsets = jnp.cumsum(gathered_logs, axis=0)
    start_offsets = end_offsets - gathered_logs
    own_start = lax.dynamic_index_in_dim(start_offsets, position, 0, keepdims=False)
    earlier = jnp.arange(gathered_logs.shape[0])[:, None] < position
    state_weight = jnp.where(
        earlier, jnp.exp(jnp.minimum(own_start[None, :] - end_offsets, 0.0)), 0.0
    )
    incoming = jnp.einsum(
        "nh,nhde->hde", state_weight, gathered_states, precision=lax.Precision.HIGHEST
    )
    before = jnp.cumsum(block_total, axis=1) - block_total
    entry_state = entry_local + jnp.exp(before).T[:, :, None, None] * incoming[None]
    from_state = jnp.einsum(
        "bihd,bhde->bihe",
        query_feat.astype(jnp.float32),
        entry_state,
        precision=lax.Precision.HIGHEST,
    )
    position_decay = jnp.transpose(jnp.exp(decay_cum), (1, 2, 0))[..., None]
    attended = within_block + position_decay * from_state
    mean_square = jnp.mean(attended * attended, axis=-1, keepdims=True)
    normed = (attended * lax.rsqrt(mean_square + 1e-05)).reshape(tok_rows, heads_here * HDIM)
    attn = (normed * norm_gain[None, :] * jax.nn.sigmoid(gate_proj.astype(jnp.float32))).astype(
        jnp.bfloat16
    )

    blocks_here = feat_here // rows_w
    s_me = lax.axis_index("seq")
    received = []
    for k in range(n_seq):
        perm = []
        for s in range(n_seq):
            for m in range(n_mdl):
                j = (s + k) % n_seq
                f = m * blocks_here + j // n_mdl
                perm.append((s * n_mdl + m, f * n_mdl + j % n_mdl))
        j_send = (s_me + k) % n_seq
        chunk = lax.dynamic_slice_in_dim(attn, j_send * piece, piece, axis=1)
        received.append(lax.ppermute(chunk, ("seq", "mdl"), perm))
    received = jnp.stack(received)
    j_me = (s_me % blocks_here) * n_mdl + m_me
    x = jnp.take(received, (j_me - jnp.arange(n_seq)) % n_seq, axis=0)

    got = [x]
    for d in range(1, n_x):
        perm = [(mu, ((mu // 2 + d) % n_x) * 2 + mu % 2) for mu in range(n_mdl)]
        got.append(lax.ppermute(x, "mdl", perm))
    own = jnp.stack(got)
    other = lax.ppermute(own, "mdl", [(mu, mu ^ 1) for mu in range(n_mdl)])

    def partial_for(target):
        rows_own = lax.dynamic_index_in_dim(own, target, 1, keepdims=False)
        rows_other = lax.dynamic_index_in_dim(other, target, 1, keepdims=False)
        return jnp.einsum(
            "dti,dic->tc", rows_own, w_perm[:, 0], preferred_element_type=jnp.float32
        ) + jnp.einsum(
            "dti,dic->tc", rows_other, w_perm[:, 1], preferred_element_type=jnp.float32
        )

    recv_r = None
    recv_l = None
    for i in range(1, n_seq):
        t_r = jnp.clip(s_me + n_seq - i, 0, n_seq - 1)
        t_l = jnp.clip(s_me - n_seq + i, 0, n_seq - 1)
        send_r = partial_for(t_r)
        send_l = partial_for(t_l)
        if recv_r is not None:
            send_r = send_r + recv_r.astype(jnp.float32)
            send_l = send_l + recv_l.astype(jnp.float32)
        recv_r = lax.ppermute(
            send_r.astype(jnp.bfloat16), "seq", [(z, z + 1) for z in range(i)]
        )
        recv_l = lax.ppermute(
            send_l.astype(jnp.bfloat16), "seq", [(z, z - 1) for z in range(n_seq - i, n_seq)]
        )
    total = partial_for(s_me)
    if recv_r is not None:
        total = total + recv_r.astype(jnp.float32) + recv_l.astype(jnp.float32)
    return total.astype(jnp.bfloat16)


def solution(mesh):
    in_specs = (
        P(("grp", "seq"), "mdl"),
        P(("grp", "seq"), "mdl"),
        P(("grp", "seq"), "mdl"),
        P(("grp", "seq"), "mdl"),
        P("mdl", ("grp", "seq")),
        P(None, "mdl"),
        P("mdl"),
        P("seq", "mdl"),
        P("mdl"),
    )
    out_specs = P(("grp", "seq"), "mdl")
    n_seq = mesh.shape["seq"]
    n_mdl = mesh.shape["mdl"]

    def body(*args):
        return per_device(n_seq, n_mdl, *args)

    return jax.shard_map(
        body, mesh=mesh, in_specs=in_specs, out_specs=out_specs, check_vma=False
    )
```

```python
import jax
import jax.numpy as jnp
from jax import lax
from jax.sharding import PartitionSpec as P

HDIM = 128
BLK = 256


def power_two(exponent):
    result = jnp.zeros(exponent.shape, jnp.float32)
    for exponent_value in range(-16, 0):
        result = result + jnp.where(exponent == exponent_value, 2.0**exponent_value, 0.0)
    return result


def fake_quant(matrix, exponent):
    scale = power_two(exponent)
    levels = jnp.clip(jnp.floor(matrix.astype(jnp.float32) / scale + 0.5), -127.0, 127.0)
    return (levels * scale).astype(jnp.bfloat16)


def per_device(
    n_seq,
    n_mdl,
    query_proj,
    key_proj,
    value_proj,
    gate_proj,
    log_decay,
    act_exponent,
    norm_gain,
    out_weight,
    weight_exponent,
):
    weights = fake_quant(out_weight, weight_exponent[None, :])
    tok_rows = query_proj.shape[0]
    feat_here = query_proj.shape[1]
    heads_here = log_decay.shape[0]
    nblocks = tok_rows // BLK
    queries = fake_quant(query_proj, act_exponent[0][None, :])
    keys_quant = fake_quant(key_proj, act_exponent[1][None, :])
    values = fake_quant(value_proj, act_exponent[2][None, :]).reshape(
        nblocks, BLK, heads_here, HDIM
    )
    query_feat = (
        jax.nn.silu(queries.astype(jnp.float32))
        .astype(jnp.bfloat16)
        .reshape(nblocks, BLK, heads_here, HDIM)
    )
    key_feat = (
        jax.nn.silu(keys_quant.astype(jnp.float32))
        .astype(jnp.bfloat16)
        .reshape(nblocks, BLK, heads_here, HDIM)
    )
    decay_cum = jnp.cumsum(log_decay.reshape(heads_here, nblocks, BLK), axis=2)
    block_total = decay_cum[:, :, -1]
    scores = jnp.einsum("bihd,bjhd->hbij", query_feat, key_feat, preferred_element_type=jnp.float32)
    decay_gap = decay_cum[:, :, :, None] - decay_cum[:, :, None, :]
    causal_mask = jnp.arange(BLK)[:, None] >= jnp.arange(BLK)[None, :]
    decay_mask = jnp.where(causal_mask, jnp.exp(jnp.minimum(decay_gap, 0.0)), 0.0)
    block_probs = (scores * decay_mask).astype(jnp.bfloat16)
    within_block = jnp.einsum(
        "hbij,bjhd->bihd", block_probs, values, preferred_element_type=jnp.float32
    )
    tail_decay = jnp.transpose(jnp.exp(block_total[:, :, None] - decay_cum), (1, 2, 0))
    weighted = (key_feat.astype(jnp.float32) * tail_decay[..., None]).astype(jnp.bfloat16)
    block_states = jnp.einsum(
        "bjhd,bjhe->bhde", weighted, values, preferred_element_type=jnp.float32
    )
    block_gain = jnp.exp(block_total).T

    def advance(carried, inputs):
        gain_here, state_here = inputs
        return (gain_here[:, None, None] * carried + state_here, carried)

    local_end, entry_local = lax.scan(
        advance, jnp.zeros((heads_here, HDIM, HDIM), jnp.float32), (block_gain, block_states)
    )
    device_log = jnp.sum(block_total, axis=1)
    log_hi = device_log.astype(jnp.bfloat16)
    log_lo = (device_log - log_hi.astype(jnp.float32)).astype(jnp.bfloat16)
    packed = jnp.concatenate(
        [
            local_end.astype(jnp.bfloat16).reshape(heads_here, HDIM * HDIM),
            jnp.broadcast_to(log_hi[:, None], (heads_here, HDIM)),
            jnp.broadcast_to(log_lo[:, None], (heads_here, HDIM)),
        ],
        axis=1,
    )
    position = lax.axis_index("seq")
    incoming = jnp.zeros((heads_here, HDIM, HDIM), jnp.float32)
    gap = jnp.zeros((heads_here,), jnp.float32)
    for d in range(1, n_seq):
        came = lax.ppermute(packed, "seq", [(z, z + d) for z in range(n_seq - d)])
        came_state = came[:, : HDIM * HDIM].astype(jnp.float32).reshape(heads_here, HDIM, HDIM)
        came_log = came[:, HDIM * HDIM].astype(jnp.float32) + came[:, HDIM * HDIM + HDIM].astype(
            jnp.float32
        )
        weight = jnp.where(d <= position, jnp.exp(jnp.minimum(gap, 0.0)), 0.0)
        incoming = incoming + weight[:, None, None] * came_state
        gap = gap + came_log
    before = jnp.cumsum(block_total, axis=1) - block_total
    entry_state = entry_local + jnp.exp(before).T[:, :, None, None] * incoming[None]
    from_state = jnp.einsum(
        "bihd,bhde->bihe",
        query_feat.astype(jnp.float32),
        entry_state,
        precision=lax.Precision.HIGHEST,
    )
    position_decay = jnp.transpose(jnp.exp(decay_cum), (1, 2, 0))[..., None]
    attended = within_block + position_decay * from_state
    mean_square = jnp.mean(attended * attended, axis=-1, keepdims=True)
    normed = (attended * lax.rsqrt(mean_square + 1e-05)).reshape(tok_rows, heads_here * HDIM)
    attn = (normed * norm_gain[None, :] * jax.nn.sigmoid(gate_proj.astype(jnp.float32))).astype(
        jnp.bfloat16
    )

    rows_w, cols_w = weights.shape
    blocks_here = feat_here // rows_w
    piece = rows_w // n_mdl
    s_me = lax.axis_index("seq")
    m_me = lax.axis_index("mdl")
    received = []
    for k in range(n_seq):
        perm = []
        for s in range(n_seq):
            for m in range(n_mdl):
                j = (s + k) % n_seq
                f = m * blocks_here + j // n_mdl
                perm.append((s * n_mdl + m, f * n_mdl + j % n_mdl))
        j_send = (s_me + k) % n_seq
        chunk = lax.dynamic_slice_in_dim(attn, j_send * piece, piece, axis=1)
        received.append(lax.ppermute(chunk, ("seq", "mdl"), perm))
    received = jnp.stack(received)
    j_me = (s_me % blocks_here) * n_mdl + m_me
    x = jnp.take(received, (j_me - jnp.arange(n_seq)) % n_seq, axis=0)

    n_x = n_mdl // 2
    core = m_me % 2
    xi = m_me // 2
    got = [x]
    for d in range(1, n_x):
        perm = [(mu, ((mu // 2 + d) % n_x) * 2 + mu % 2) for mu in range(n_mdl)]
        got.append(lax.ppermute(x, "mdl", perm))
    own = jnp.stack(got)
    other = lax.ppermute(own, "mdl", [(mu, mu ^ 1) for mu in range(n_mdl)])
    gathered_x = jnp.stack([own, other], axis=1)
    d_idx = jnp.arange(n_x)[:, None]
    e_idx = jnp.arange(2)[None, :]
    mu_tab = 2 * ((xi - d_idx) % n_x) + jnp.where(e_idx == 0, core, 1 - core)
    w_perm = jnp.take(
        weights.reshape(n_mdl, piece, cols_w), mu_tab.reshape(-1), axis=0
    ).reshape(n_x, 2, piece, cols_w)

    def partial_for(target):
        rows = lax.dynamic_index_in_dim(gathered_x, target, 2, keepdims=False)
        return jnp.einsum(
            "deti,deic->tc", rows, w_perm, preferred_element_type=jnp.float32
        )

    halves = 2 if cols_w % 256 == 0 else 1
    width = cols_w // halves
    recv_r = [None] * halves
    recv_l = [None] * halves
    for i in range(1, n_seq):
        t_r = jnp.clip(s_me + n_seq - i, 0, n_seq - 1)
        t_l = jnp.clip(s_me - n_seq + i, 0, n_seq - 1)
        part_r = partial_for(t_r)
        part_l = partial_for(t_l)
        for h in range(halves):
            send_r = part_r[:, h * width : (h + 1) * width]
            send_l = part_l[:, h * width : (h + 1) * width]
            if recv_r[h] is not None:
                send_r = send_r + recv_r[h].astype(jnp.float32)
                send_l = send_l + recv_l[h].astype(jnp.float32)
            recv_r[h] = lax.ppermute(
                send_r.astype(jnp.bfloat16), "seq", [(z, z + 1) for z in range(i)]
            )
            recv_l[h] = lax.ppermute(
                send_l.astype(jnp.bfloat16), "seq", [(z, z - 1) for z in range(n_seq - i, n_seq)]
            )
    total = partial_for(s_me)
    if recv_r[0] is not None:
        total = total + jnp.concatenate(
            [recv_r[h].astype(jnp.float32) + recv_l[h].astype(jnp.float32) for h in range(halves)],
            axis=1,
        )
    return total.astype(jnp.bfloat16)


def solution(mesh):
    in_specs = (
        P(("grp", "seq"), "mdl"),
        P(("grp", "seq"), "mdl"),
        P(("grp", "seq"), "mdl"),
        P(("grp", "seq"), "mdl"),
        P("mdl", ("grp", "seq")),
        P(None, "mdl"),
        P("mdl"),
        P("seq", "mdl"),
        P("mdl"),
    )
    out_specs = P(("grp", "seq"), "mdl")
    n_seq = mesh.shape["seq"]
    n_mdl = mesh.shape["mdl"]

    def body(*args):
        return per_device(n_seq, n_mdl, *args)

    return jax.shard_map(
        body, mesh=mesh, in_specs=in_specs, out_specs=out_specs, check_vma=False
    )
```

```python
import jax
import jax.numpy as jnp
from jax import lax
from jax.sharding import PartitionSpec as P

HDIM = 128
BLK = 256


def power_two(exponent):
    result = jnp.zeros(exponent.shape, jnp.float32)
    for exponent_value in range(-16, 0):
        result = result + jnp.where(exponent == exponent_value, 2.0**exponent_value, 0.0)
    return result


def fake_quant(matrix, exponent):
    scale = power_two(exponent)
    levels = jnp.clip(jnp.floor(matrix.astype(jnp.float32) / scale + 0.5), -127.0, 127.0)
    return (levels * scale).astype(jnp.bfloat16)


def per_device(
    n_seq,
    n_mdl,
    query_proj,
    key_proj,
    value_proj,
    gate_proj,
    log_decay,
    act_exponent,
    norm_gain,
    out_weight,
    weight_exponent,
):
    weights = fake_quant(out_weight, weight_exponent[None, :])
    tok_rows = query_proj.shape[0]
    feat_here = query_proj.shape[1]
    heads_here = log_decay.shape[0]
    nblocks = tok_rows // BLK
    queries = fake_quant(query_proj, act_exponent[0][None, :])
    keys_quant = fake_quant(key_proj, act_exponent[1][None, :])
    values = fake_quant(value_proj, act_exponent[2][None, :]).reshape(
        nblocks, BLK, heads_here, HDIM
    )
    query_feat = (
        jax.nn.silu(queries.astype(jnp.float32))
        .astype(jnp.bfloat16)
        .reshape(nblocks, BLK, heads_here, HDIM)
    )
    key_feat = (
        jax.nn.silu(keys_quant.astype(jnp.float32))
        .astype(jnp.bfloat16)
        .reshape(nblocks, BLK, heads_here, HDIM)
    )
    decay_cum = jnp.cumsum(log_decay.reshape(heads_here, nblocks, BLK), axis=2)
    block_total = decay_cum[:, :, -1]
    scores = jnp.einsum("bihd,bjhd->hbij", query_feat, key_feat, preferred_element_type=jnp.float32)
    decay_gap = decay_cum[:, :, :, None] - decay_cum[:, :, None, :]
    causal_mask = jnp.arange(BLK)[:, None] >= jnp.arange(BLK)[None, :]
    decay_mask = jnp.where(causal_mask, jnp.exp(jnp.minimum(decay_gap, 0.0)), 0.0)
    block_probs = (scores * decay_mask).astype(jnp.bfloat16)
    within_block = jnp.einsum(
        "hbij,bjhd->bihd", block_probs, values, preferred_element_type=jnp.float32
    )
    tail_decay = jnp.transpose(jnp.exp(block_total[:, :, None] - decay_cum), (1, 2, 0))
    weighted = (key_feat.astype(jnp.float32) * tail_decay[..., None]).astype(jnp.bfloat16)
    block_states = jnp.einsum(
        "bjhd,bjhe->bhde", weighted, values, preferred_element_type=jnp.float32
    )
    block_gain = jnp.exp(block_total).T

    def advance(carried, inputs):
        gain_here, state_here = inputs
        return (gain_here[:, None, None] * carried + state_here, carried)

    local_end, entry_local = lax.scan(
        advance, jnp.zeros((heads_here, HDIM, HDIM), jnp.float32), (block_gain, block_states)
    )
    device_log = jnp.sum(block_total, axis=1)
    log_hi = device_log.astype(jnp.bfloat16)
    log_lo = (device_log - log_hi.astype(jnp.float32)).astype(jnp.bfloat16)
    packed = jnp.concatenate(
        [
            local_end.astype(jnp.bfloat16).reshape(heads_here, HDIM * HDIM),
            jnp.broadcast_to(log_hi[:, None], (heads_here, HDIM)),
            jnp.broadcast_to(log_lo[:, None], (heads_here, HDIM)),
        ],
        axis=1,
    )
    position = lax.axis_index("seq")
    incoming = jnp.zeros((heads_here, HDIM, HDIM), jnp.float32)
    gap = jnp.zeros((heads_here,), jnp.float32)
    for d in range(1, n_seq):
        came = lax.ppermute(packed, "seq", [(z, z + d) for z in range(n_seq - d)])
        came_state = came[:, : HDIM * HDIM].astype(jnp.float32).reshape(heads_here, HDIM, HDIM)
        came_log = came[:, HDIM * HDIM].astype(jnp.float32) + came[:, HDIM * HDIM + HDIM].astype(
            jnp.float32
        )
        weight = jnp.where(d <= position, jnp.exp(jnp.minimum(gap, 0.0)), 0.0)
        incoming = incoming + weight[:, None, None] * came_state
        gap = gap + came_log
    before = jnp.cumsum(block_total, axis=1) - block_total
    entry_state = entry_local + jnp.exp(before).T[:, :, None, None] * incoming[None]
    from_state = jnp.einsum(
        "bihd,bhde->bihe",
        query_feat.astype(jnp.float32),
        entry_state,
        precision=lax.Precision.HIGHEST,
    )
    position_decay = jnp.transpose(jnp.exp(decay_cum), (1, 2, 0))[..., None]
    attended = within_block + position_decay * from_state
    mean_square = jnp.mean(attended * attended, axis=-1, keepdims=True)
    normed = (attended * lax.rsqrt(mean_square + 1e-05)).reshape(tok_rows, heads_here * HDIM)
    attn = (normed * norm_gain[None, :] * jax.nn.sigmoid(gate_proj.astype(jnp.float32))).astype(
        jnp.bfloat16
    )

    rows_w, cols_w = weights.shape
    blocks_here = feat_here // rows_w
    piece = rows_w // n_mdl
    s_me = lax.axis_index("seq")
    m_me = lax.axis_index("mdl")
    if n_seq == 4 and n_mdl == 4:
        x_me = m_me // 2
        own_pieces = attn.reshape(tok_rows, n_mdl, piece)
        keep = lax.dynamic_slice_in_dim(own_pieces, 2 * x_me, 2, axis=1)
        away = lax.dynamic_slice_in_dim(own_pieces, 2 * (1 - x_me), 2, axis=1)
        came = lax.ppermute(away, "mdl", [(mu, mu ^ 2) for mu in range(n_mdl)])
        items = jnp.transpose(jnp.concatenate([keep, came], axis=1), (1, 0, 2))
        received = []
        for k in range(n_seq):
            perm = []
            for s in range(n_seq):
                for mu in range(n_mdl):
                    r = (s + k) % n_seq
                    f = mu if r // 2 == 0 else mu ^ 2
                    perm.append((s * n_mdl + mu, f * n_mdl + 2 * (mu // 2) + r % 2))
            item = lax.dynamic_index_in_dim(items, (s_me + k) % n_seq, 0, keepdims=False)
            received.append(lax.ppermute(item, ("seq", "mdl"), perm))
        received = jnp.stack(received)
        r_me = 2 * ((s_me // 2) != (m_me // 2)).astype(jnp.int32) + m_me % 2
        x = jnp.take(received, (r_me - jnp.arange(n_seq)) % n_seq, axis=0)
    else:
        received = []
        for k in range(n_seq):
            perm = []
            for s in range(n_seq):
                for m in range(n_mdl):
                    j = (s + k) % n_seq
                    f = m * blocks_here + j // n_mdl
                    perm.append((s * n_mdl + m, f * n_mdl + j % n_mdl))
            j_send = (s_me + k) % n_seq
            chunk = lax.dynamic_slice_in_dim(attn, j_send * piece, piece, axis=1)
            received.append(lax.ppermute(chunk, ("seq", "mdl"), perm))
        received = jnp.stack(received)
        j_me = (s_me % blocks_here) * n_mdl + m_me
        x = jnp.take(received, (j_me - jnp.arange(n_seq)) % n_seq, axis=0)

    n_x = n_mdl // 2
    core = m_me % 2
    xi = m_me // 2
    got = [x]
    for d in range(1, n_x):
        perm = [(mu, ((mu // 2 + d) % n_x) * 2 + mu % 2) for mu in range(n_mdl)]
        got.append(lax.ppermute(x, "mdl", perm))
    own = jnp.stack(got)
    other = lax.ppermute(own, "mdl", [(mu, mu ^ 1) for mu in range(n_mdl)])
    gathered_x = jnp.stack([own, other], axis=1)
    d_idx = jnp.arange(n_x)[:, None]
    e_idx = jnp.arange(2)[None, :]
    mu_tab = 2 * ((xi - d_idx) % n_x) + jnp.where(e_idx == 0, core, 1 - core)
    w_perm = jnp.take(
        weights.reshape(n_mdl, piece, cols_w), mu_tab.reshape(-1), axis=0
    ).reshape(n_x, 2, piece, cols_w)

    def partial_for(target):
        rows = lax.dynamic_index_in_dim(gathered_x, target, 2, keepdims=False)
        return jnp.einsum(
            "deti,deic->tc", rows, w_perm, preferred_element_type=jnp.float32
        )

    halves = 2 if cols_w % 256 == 0 else 1
    width = cols_w // halves
    recv_r = [None] * halves
    recv_l = [None] * halves
    for i in range(1, n_seq):
        t_r = jnp.clip(s_me + n_seq - i, 0, n_seq - 1)
        t_l = jnp.clip(s_me - n_seq + i, 0, n_seq - 1)
        part_r = partial_for(t_r)
        part_l = partial_for(t_l)
        for h in range(halves):
            send_r = part_r[:, h * width : (h + 1) * width]
            send_l = part_l[:, h * width : (h + 1) * width]
            if recv_r[h] is not None:
                send_r = send_r + recv_r[h].astype(jnp.float32)
                send_l = send_l + recv_l[h].astype(jnp.float32)
            recv_r[h] = lax.ppermute(
                send_r.astype(jnp.bfloat16), "seq", [(z, z + 1) for z in range(i)]
            )
            recv_l[h] = lax.ppermute(
                send_l.astype(jnp.bfloat16), "seq", [(z, z - 1) for z in range(n_seq - i, n_seq)]
            )
    total = partial_for(s_me)
    if recv_r[0] is not None:
        total = total + jnp.concatenate(
            [recv_r[h].astype(jnp.float32) + recv_l[h].astype(jnp.float32) for h in range(halves)],
            axis=1,
        )
    return total.astype(jnp.bfloat16)


def solution(mesh):
    in_specs = (
        P(("grp", "seq"), "mdl"),
        P(("grp", "seq"), "mdl"),
        P(("grp", "seq"), "mdl"),
        P(("grp", "seq"), "mdl"),
        P("mdl", ("grp", "seq")),
        P(None, "mdl"),
        P("mdl"),
        P("seq", "mdl"),
        P("mdl"),
    )
    out_specs = P(("grp", "seq"), "mdl")
    n_seq = mesh.shape["seq"]
    n_mdl = mesh.shape["mdl"]

    def body(*args):
        return per_device(n_seq, n_mdl, *args)

    return jax.shard_map(
        body, mesh=mesh, in_specs=in_specs, out_specs=out_specs, check_vma=False
    )
```

```python
import jax
import jax.numpy as jnp
from jax import lax
from jax.sharding import PartitionSpec as P

HDIM = 128
BLK = 256


def power_two(exponent):
    result = jnp.zeros(exponent.shape, jnp.float32)
    for exponent_value in range(-16, 0):
        result = result + jnp.where(exponent == exponent_value, 2.0**exponent_value, 0.0)
    return result


def fake_quant(matrix, exponent):
    scale = power_two(exponent)
    levels = jnp.clip(jnp.floor(matrix.astype(jnp.float32) / scale + 0.5), -127.0, 127.0)
    return (levels * scale).astype(jnp.bfloat16)


def per_device(
    n_seq,
    n_mdl,
    query_proj,
    key_proj,
    value_proj,
    gate_proj,
    log_decay,
    act_exponent,
    norm_gain,
    out_weight,
    weight_exponent,
):
    tok_rows = query_proj.shape[0]
    feat_here = query_proj.shape[1]
    heads_here = log_decay.shape[0]
    nblocks = tok_rows // BLK
    queries = fake_quant(query_proj, act_exponent[0][None, :])
    keys_quant = fake_quant(key_proj, act_exponent[1][None, :])
    values = fake_quant(value_proj, act_exponent[2][None, :]).reshape(
        nblocks, BLK, heads_here, HDIM
    )
    query_feat = (
        jax.nn.silu(queries.astype(jnp.float32))
        .astype(jnp.bfloat16)
        .reshape(nblocks, BLK, heads_here, HDIM)
    )
    key_feat = (
        jax.nn.silu(keys_quant.astype(jnp.float32))
        .astype(jnp.bfloat16)
        .reshape(nblocks, BLK, heads_here, HDIM)
    )
    decay_cum = jnp.cumsum(log_decay.reshape(heads_here, nblocks, BLK), axis=2)
    block_total = decay_cum[:, :, -1]
    scores = jnp.einsum("bihd,bjhd->hbij", query_feat, key_feat, preferred_element_type=jnp.float32)
    decay_gap = decay_cum[:, :, :, None] - decay_cum[:, :, None, :]
    causal_mask = jnp.arange(BLK)[:, None] >= jnp.arange(BLK)[None, :]
    decay_mask = jnp.where(causal_mask, jnp.exp(jnp.minimum(decay_gap, 0.0)), 0.0)
    block_probs = (scores * decay_mask).astype(jnp.bfloat16)
    within_block = jnp.einsum(
        "hbij,bjhd->bihd", block_probs, values, preferred_element_type=jnp.float32
    )
    tail_decay = jnp.transpose(jnp.exp(block_total[:, :, None] - decay_cum), (1, 2, 0))
    weighted = (key_feat.astype(jnp.float32) * tail_decay[..., None]).astype(jnp.bfloat16)
    block_states = jnp.einsum(
        "bjhd,bjhe->bhde", weighted, values, preferred_element_type=jnp.float32
    )
    block_gain = jnp.exp(block_total).T

    def advance(carried, inputs):
        gain_here, state_here = inputs
        return (gain_here[:, None, None] * carried + state_here, carried)

    local_end, entry_local = lax.scan(
        advance, jnp.zeros((heads_here, HDIM, HDIM), jnp.float32), (block_gain, block_states)
    )
    device_log = jnp.sum(block_total, axis=1)
    weights = fake_quant(out_weight, weight_exponent[None, :])
    rows_w, cols_w = weights.shape
    piece = rows_w // n_mdl
    n_x = n_mdl // 2
    m_me = lax.axis_index("mdl")
    core = m_me % 2
    xi = m_me // 2
    d_idx = jnp.arange(n_x)[:, None]
    e_idx = jnp.arange(2)[None, :]
    mu_tab = 2 * ((xi - d_idx) % n_x) + jnp.where(e_idx == 0, core, 1 - core)
    w_perm = jnp.take(
        weights.reshape(n_mdl, piece, cols_w), mu_tab.reshape(-1), axis=0
    ).reshape(n_x, 2, piece, cols_w)
    log_hi = device_log.astype(jnp.bfloat16)
    log_lo = (device_log - log_hi.astype(jnp.float32)).astype(jnp.bfloat16)
    packed = jnp.concatenate(
        [
            local_end.astype(jnp.bfloat16).reshape(heads_here, HDIM * HDIM),
            jnp.broadcast_to(log_hi[:, None], (heads_here, HDIM)),
            jnp.broadcast_to(log_lo[:, None], (heads_here, HDIM)),
        ],
        axis=1,
    )
    position = lax.axis_index("seq")
    incoming = jnp.zeros((heads_here, HDIM, HDIM), jnp.float32)
    gap = jnp.zeros((heads_here,), jnp.float32)
    for d in range(1, n_seq):
        came = lax.ppermute(packed, "seq", [(z, z + d) for z in range(n_seq - d)])
        if d == 1:
            came, w_perm = lax.optimization_barrier((came, w_perm))
        came_state = came[:, : HDIM * HDIM].astype(jnp.float32).reshape(heads_here, HDIM, HDIM)
        came_log = came[:, HDIM * HDIM].astype(jnp.float32) + came[:, HDIM * HDIM + HDIM].astype(
            jnp.float32
        )
        weight = jnp.where(d <= position, jnp.exp(jnp.minimum(gap, 0.0)), 0.0)
        incoming = incoming + weight[:, None, None] * came_state
        gap = gap + came_log
    before = jnp.cumsum(block_total, axis=1) - block_total
    entry_state = entry_local + jnp.exp(before).T[:, :, None, None] * incoming[None]
    from_state = jnp.einsum(
        "bihd,bhde->bihe",
        query_feat.astype(jnp.float32),
        entry_state,
        precision=lax.Precision.HIGHEST,
    )
    position_decay = jnp.transpose(jnp.exp(decay_cum), (1, 2, 0))[..., None]
    attended = within_block + position_decay * from_state
    mean_square = jnp.mean(attended * attended, axis=-1, keepdims=True)
    normed = (attended * lax.rsqrt(mean_square + 1e-05)).reshape(tok_rows, heads_here * HDIM)
    attn = (normed * norm_gain[None, :] * jax.nn.sigmoid(gate_proj.astype(jnp.float32))).astype(
        jnp.bfloat16
    )

    blocks_here = feat_here // rows_w
    s_me = lax.axis_index("seq")
    if n_seq == 4 and n_mdl == 4:
        x_me = m_me // 2
        own_pieces = attn.reshape(tok_rows, n_mdl, piece)
        keep = lax.dynamic_slice_in_dim(own_pieces, 2 * x_me, 2, axis=1)
        away = lax.dynamic_slice_in_dim(own_pieces, 2 * (1 - x_me), 2, axis=1)
        came = lax.ppermute(away, "mdl", [(mu, mu ^ 2) for mu in range(n_mdl)])
        items = jnp.transpose(jnp.concatenate([keep, came], axis=1), (1, 0, 2))
        received = []
        for k in range(n_seq):
            perm = []
            for s in range(n_seq):
                for mu in range(n_mdl):
                    r = (s + k) % n_seq
                    f = mu if r // 2 == 0 else mu ^ 2
                    perm.append((s * n_mdl + mu, f * n_mdl + 2 * (mu // 2) + r % 2))
            item = lax.dynamic_index_in_dim(items, (s_me + k) % n_seq, 0, keepdims=False)
            received.append(lax.ppermute(item, ("seq", "mdl"), perm))
        received = jnp.stack(received)
        r_me = 2 * ((s_me // 2) != (m_me // 2)).astype(jnp.int32) + m_me % 2
        x = jnp.take(received, (r_me - jnp.arange(n_seq)) % n_seq, axis=0)
    else:
        received = []
        for k in range(n_seq):
            perm = []
            for s in range(n_seq):
                for m in range(n_mdl):
                    j = (s + k) % n_seq
                    f = m * blocks_here + j // n_mdl
                    perm.append((s * n_mdl + m, f * n_mdl + j % n_mdl))
            j_send = (s_me + k) % n_seq
            chunk = lax.dynamic_slice_in_dim(attn, j_send * piece, piece, axis=1)
            received.append(lax.ppermute(chunk, ("seq", "mdl"), perm))
        received = jnp.stack(received)
        j_me = (s_me % blocks_here) * n_mdl + m_me
        x = jnp.take(received, (j_me - jnp.arange(n_seq)) % n_seq, axis=0)

    n_x = n_mdl // 2
    core = m_me % 2
    xi = m_me // 2
    got = [x]
    for d in range(1, n_x):
        perm = [(mu, ((mu // 2 + d) % n_x) * 2 + mu % 2) for mu in range(n_mdl)]
        got.append(lax.ppermute(x, "mdl", perm))
    own = jnp.stack(got)
    other = lax.ppermute(own, "mdl", [(mu, mu ^ 1) for mu in range(n_mdl)])
    gathered_x = jnp.stack([own, other], axis=1)
    def partial_for(target):
        rows = lax.dynamic_index_in_dim(gathered_x, target, 2, keepdims=False)
        return jnp.einsum(
            "deti,deic->tc", rows, w_perm, preferred_element_type=jnp.float32
        )

    halves = 2 if cols_w % 256 == 0 else 1
    width = cols_w // halves
    recv_r = [None] * halves
    recv_l = [None] * halves
    for i in range(1, n_seq):
        t_r = jnp.clip(s_me + n_seq - i, 0, n_seq - 1)
        t_l = jnp.clip(s_me - n_seq + i, 0, n_seq - 1)
        part_r = partial_for(t_r)
        part_l = partial_for(t_l)
        for h in range(halves):
            send_r = part_r[:, h * width : (h + 1) * width]
            send_l = part_l[:, h * width : (h + 1) * width]
            if recv_r[h] is not None:
                send_r = send_r + recv_r[h].astype(jnp.float32)
                send_l = send_l + recv_l[h].astype(jnp.float32)
            recv_r[h] = lax.ppermute(
                send_r.astype(jnp.bfloat16), "seq", [(z, z + 1) for z in range(i)]
            )
            recv_l[h] = lax.ppermute(
                send_l.astype(jnp.bfloat16), "seq", [(z, z - 1) for z in range(n_seq - i, n_seq)]
            )
    total = partial_for(s_me)
    if recv_r[0] is not None:
        total = total + jnp.concatenate(
            [recv_r[h].astype(jnp.float32) + recv_l[h].astype(jnp.float32) for h in range(halves)],
            axis=1,
        )
    return total.astype(jnp.bfloat16)


def solution(mesh):
    in_specs = (
        P(("grp", "seq"), "mdl"),
        P(("grp", "seq"), "mdl"),
        P(("grp", "seq"), "mdl"),
        P(("grp", "seq"), "mdl"),
        P("mdl", ("grp", "seq")),
        P(None, "mdl"),
        P("mdl"),
        P("seq", "mdl"),
        P("mdl"),
    )
    out_specs = P(("grp", "seq"), "mdl")
    n_seq = mesh.shape["seq"]
    n_mdl = mesh.shape["mdl"]

    def body(*args):
        return per_device(n_seq, n_mdl, *args)

    return jax.shard_map(
        body, mesh=mesh, in_specs=in_specs, out_specs=out_specs, check_vma=False
    )
```

```python
import jax
import jax.numpy as jnp
from jax import lax
from jax.sharding import PartitionSpec as P

HDIM = 128
BLK = 256


def power_two(exponent):
    result = jnp.zeros(exponent.shape, jnp.float32)
    for exponent_value in range(-16, 0):
        result = result + jnp.where(exponent == exponent_value, 2.0**exponent_value, 0.0)
    return result


def fake_quant(matrix, exponent):
    scale = power_two(exponent)
    levels = jnp.clip(jnp.floor(matrix.astype(jnp.float32) / scale + 0.5), -127.0, 127.0)
    return (levels * scale).astype(jnp.bfloat16)


def per_device(
    n_seq,
    n_mdl,
    query_proj,
    key_proj,
    value_proj,
    gate_proj,
    log_decay,
    act_exponent,
    norm_gain,
    out_weight,
    weight_exponent,
):
    weights = fake_quant(out_weight, weight_exponent[None, :])
    tok_rows = query_proj.shape[0]
    feat_here = query_proj.shape[1]
    heads_here = log_decay.shape[0]
    nblocks = tok_rows // BLK
    queries = fake_quant(query_proj, act_exponent[0][None, :])
    keys_quant = fake_quant(key_proj, act_exponent[1][None, :])
    values = fake_quant(value_proj, act_exponent[2][None, :]).reshape(
        nblocks, BLK, heads_here, HDIM
    )
    query_feat = (
        jax.nn.silu(queries.astype(jnp.float32))
        .astype(jnp.bfloat16)
        .reshape(nblocks, BLK, heads_here, HDIM)
    )
    key_feat = (
        jax.nn.silu(keys_quant.astype(jnp.float32))
        .astype(jnp.bfloat16)
        .reshape(nblocks, BLK, heads_here, HDIM)
    )
    decay_cum = jnp.cumsum(log_decay.reshape(heads_here, nblocks, BLK), axis=2)
    block_total = decay_cum[:, :, -1]
    scores = jnp.einsum("bihd,bjhd->hbij", query_feat, key_feat, preferred_element_type=jnp.float32)
    decay_gap = decay_cum[:, :, :, None] - decay_cum[:, :, None, :]
    causal_mask = jnp.arange(BLK)[:, None] >= jnp.arange(BLK)[None, :]
    decay_mask = jnp.where(causal_mask, jnp.exp(jnp.minimum(decay_gap, 0.0)), 0.0)
    block_probs = (scores * decay_mask).astype(jnp.bfloat16)
    within_block = jnp.einsum(
        "hbij,bjhd->bihd", block_probs, values, preferred_element_type=jnp.float32
    )
    tail_decay = jnp.transpose(jnp.exp(block_total[:, :, None] - decay_cum), (1, 2, 0))
    weighted = (key_feat.astype(jnp.float32) * tail_decay[..., None]).astype(jnp.bfloat16)
    block_states = jnp.einsum(
        "bjhd,bjhe->bhde", weighted, values, preferred_element_type=jnp.float32
    )
    block_gain = jnp.exp(block_total).T

    def advance(carried, inputs):
        gain_here, state_here = inputs
        return (gain_here[:, None, None] * carried + state_here, carried)

    local_end, entry_local = lax.scan(
        advance, jnp.zeros((heads_here, HDIM, HDIM), jnp.float32), (block_gain, block_states)
    )
    device_log = jnp.sum(block_total, axis=1)
    log_hi = device_log.astype(jnp.bfloat16)
    log_lo = (device_log - log_hi.astype(jnp.float32)).astype(jnp.bfloat16)
    packed = jnp.concatenate(
        [
            local_end.astype(jnp.bfloat16).reshape(heads_here, HDIM * HDIM),
            jnp.broadcast_to(log_hi[:, None], (heads_here, HDIM)),
            jnp.broadcast_to(log_lo[:, None], (heads_here, HDIM)),
        ],
        axis=1,
    )
    position = lax.axis_index("seq")
    incoming = jnp.zeros((heads_here, HDIM, HDIM), jnp.float32)
    gap = jnp.zeros((heads_here,), jnp.float32)
    for d in range(1, n_seq):
        came = lax.ppermute(packed, "seq", [(z, z + d) for z in range(n_seq - d)])
        came_state = came[:, : HDIM * HDIM].astype(jnp.float32).reshape(heads_here, HDIM, HDIM)
        came_log = came[:, HDIM * HDIM].astype(jnp.float32) + came[:, HDIM * HDIM + HDIM].astype(
            jnp.float32
        )
        weight = jnp.where(d <= position, jnp.exp(jnp.minimum(gap, 0.0)), 0.0)
        incoming = incoming + weight[:, None, None] * came_state
        gap = gap + came_log
    before = jnp.cumsum(block_total, axis=1) - block_total
    entry_state = entry_local + jnp.exp(before).T[:, :, None, None] * incoming[None]
    from_state = jnp.einsum(
        "bihd,bhde->bihe",
        query_feat.astype(jnp.float32),
        entry_state,
        precision=lax.Precision.HIGHEST,
    )
    position_decay = jnp.transpose(jnp.exp(decay_cum), (1, 2, 0))[..., None]
    attended = within_block + position_decay * from_state
    mean_square = jnp.mean(attended * attended, axis=-1, keepdims=True)
    normed = (attended * lax.rsqrt(mean_square + 1e-05)).reshape(tok_rows, heads_here * HDIM)
    attn = (normed * norm_gain[None, :] * jax.nn.sigmoid(gate_proj.astype(jnp.float32))).astype(
        jnp.bfloat16
    )

    rows_w, cols_w = weights.shape
    blocks_here = feat_here // rows_w
    piece = rows_w // n_mdl
    s_me = lax.axis_index("seq")
    m_me = lax.axis_index("mdl")
    if n_seq == 4 and n_mdl == 4:
        x_me = m_me // 2
        own_pieces = attn.reshape(tok_rows, n_mdl, piece)
        keep = lax.dynamic_slice_in_dim(own_pieces, 2 * x_me, 2, axis=1)
        away = lax.dynamic_slice_in_dim(own_pieces, 2 * (1 - x_me), 2, axis=1)
        came = lax.ppermute(away, "mdl", [(mu, mu ^ 2) for mu in range(n_mdl)])
        items = jnp.transpose(jnp.concatenate([keep, came], axis=1), (1, 0, 2))
        received = []
        for k in range(n_seq):
            perm = []
            for s in range(n_seq):
                for mu in range(n_mdl):
                    r = (s + k) % n_seq
                    f = mu if r // 2 == 0 else mu ^ 2
                    perm.append((s * n_mdl + mu, f * n_mdl + 2 * (mu // 2) + r % 2))
            item = lax.dynamic_index_in_dim(items, (s_me + k) % n_seq, 0, keepdims=False)
            received.append(lax.ppermute(item, ("seq", "mdl"), perm))
        received = jnp.stack(received)
        r_me = 2 * ((s_me // 2) != (m_me // 2)).astype(jnp.int32) + m_me % 2
        x = jnp.take(received, (r_me - jnp.arange(n_seq)) % n_seq, axis=0)
    else:
        received = []
        for k in range(n_seq):
            perm = []
            for s in range(n_seq):
                for m in range(n_mdl):
                    j = (s + k) % n_seq
                    f = m * blocks_here + j // n_mdl
                    perm.append((s * n_mdl + m, f * n_mdl + j % n_mdl))
            j_send = (s_me + k) % n_seq
            chunk = lax.dynamic_slice_in_dim(attn, j_send * piece, piece, axis=1)
            received.append(lax.ppermute(chunk, ("seq", "mdl"), perm))
        received = jnp.stack(received)
        j_me = (s_me % blocks_here) * n_mdl + m_me
        x = jnp.take(received, (j_me - jnp.arange(n_seq)) % n_seq, axis=0)

    n_x = n_mdl // 2
    core = m_me % 2
    xi = m_me // 2
    got = [x]
    for d in range(1, n_x):
        perm = [(mu, ((mu // 2 + d) % n_x) * 2 + mu % 2) for mu in range(n_mdl)]
        got.append(lax.ppermute(x, "mdl", perm))
    own = jnp.stack(got)
    other = lax.ppermute(own, "mdl", [(mu, mu ^ 1) for mu in range(n_mdl)])
    gathered_x = jnp.stack([own, other], axis=1)
    d_idx = jnp.arange(n_x)[:, None]
    e_idx = jnp.arange(2)[None, :]
    mu_tab = 2 * ((xi - d_idx) % n_x) + jnp.where(e_idx == 0, core, 1 - core)
    w_perm = jnp.take(
        weights.reshape(n_mdl, piece, cols_w), mu_tab.reshape(-1), axis=0
    ).reshape(n_x, 2, piece, cols_w)

    def partial_for(target):
        rows = lax.dynamic_index_in_dim(gathered_x, target, 2, keepdims=False)
        return jnp.einsum(
            "deti,deic->tc", rows, w_perm, preferred_element_type=jnp.float32
        )

    if n_seq == 4:
        def bf(v):
            return v.astype(jnp.bfloat16)

        near_r = lax.ppermute(
            bf(partial_for(jnp.clip(s_me + 2, 0, 3))), "seq", [(0, 1), (1, 2)]
        )
        far_r = lax.ppermute(bf(partial_for(jnp.int32(3))), "seq", [(0, 3)])
        near_l = lax.ppermute(
            bf(partial_for(jnp.clip(s_me - 2, 0, 3))), "seq", [(3, 2), (2, 1)]
        )
        far_l = lax.ppermute(bf(partial_for(jnp.int32(0))), "seq", [(3, 0)])
        last_r = lax.ppermute(
            bf(partial_for(jnp.clip(s_me + 1, 0, 3)) + near_r.astype(jnp.float32)),
            "seq",
            [(0, 1), (1, 2), (2, 3)],
        )
        last_l = lax.ppermute(
            bf(partial_for(jnp.clip(s_me - 1, 0, 3)) + near_l.astype(jnp.float32)),
            "seq",
            [(3, 2), (2, 1), (1, 0)],
        )
        total = partial_for(s_me)
        for came in (last_r, far_r, last_l, far_l):
            total = total + came.astype(jnp.float32)
        return total.astype(jnp.bfloat16)

    halves = 2 if cols_w % 256 == 0 else 1
    width = cols_w // halves
    recv_r = [None] * halves
    recv_l = [None] * halves
    for i in range(1, n_seq):
        t_r = jnp.clip(s_me + n_seq - i, 0, n_seq - 1)
        t_l = jnp.clip(s_me - n_seq + i, 0, n_seq - 1)
        part_r = partial_for(t_r)
        part_l = partial_for(t_l)
        for h in range(halves):
            send_r = part_r[:, h * width : (h + 1) * width]
            send_l = part_l[:, h * width : (h + 1) * width]
            if recv_r[h] is not None:
                send_r = send_r + recv_r[h].astype(jnp.float32)
                send_l = send_l + recv_l[h].astype(jnp.float32)
            recv_r[h] = lax.ppermute(
                send_r.astype(jnp.bfloat16), "seq", [(z, z + 1) for z in range(i)]
            )
            recv_l[h] = lax.ppermute(
                send_l.astype(jnp.bfloat16), "seq", [(z, z - 1) for z in range(n_seq - i, n_seq)]
            )
    total = partial_for(s_me)
    if recv_r[0] is not None:
        total = total + jnp.concatenate(
            [recv_r[h].astype(jnp.float32) + recv_l[h].astype(jnp.float32) for h in range(halves)],
            axis=1,
        )
    return total.astype(jnp.bfloat16)


def solution(mesh):
    in_specs = (
        P(("grp", "seq"), "mdl"),
        P(("grp", "seq"), "mdl"),
        P(("grp", "seq"), "mdl"),
        P(("grp", "seq"), "mdl"),
        P("mdl", ("grp", "seq")),
        P(None, "mdl"),
        P("mdl"),
        P("seq", "mdl"),
        P("mdl"),
    )
    out_specs = P(("grp", "seq"), "mdl")
    n_seq = mesh.shape["seq"]
    n_mdl = mesh.shape["mdl"]

    def body(*args):
        return per_device(n_seq, n_mdl, *args)

    return jax.shard_map(
        body, mesh=mesh, in_specs=in_specs, out_specs=out_specs, check_vma=False
    )
```

```python
import jax
import jax.numpy as jnp
from jax import lax
from jax.sharding import PartitionSpec as P

HDIM = 128
BLK = 256


def power_two(exponent):
    result = jnp.zeros(exponent.shape, jnp.float32)
    for exponent_value in range(-16, 0):
        result = result + jnp.where(exponent == exponent_value, 2.0**exponent_value, 0.0)
    return result


def fake_quant(matrix, exponent):
    scale = power_two(exponent)
    levels = jnp.clip(jnp.floor(matrix.astype(jnp.float32) / scale + 0.5), -127.0, 127.0)
    return (levels * scale).astype(jnp.bfloat16)


def per_device(
    n_seq,
    n_mdl,
    query_proj,
    key_proj,
    value_proj,
    gate_proj,
    log_decay,
    act_exponent,
    norm_gain,
    out_weight,
    weight_exponent,
):
    weights = fake_quant(out_weight, weight_exponent[None, :])
    tok_rows = query_proj.shape[0]
    feat_here = query_proj.shape[1]
    heads_here = log_decay.shape[0]
    nblocks = tok_rows // BLK
    queries = fake_quant(query_proj, act_exponent[0][None, :])
    keys_quant = fake_quant(key_proj, act_exponent[1][None, :])
    values = fake_quant(value_proj, act_exponent[2][None, :]).reshape(
        nblocks, BLK, heads_here, HDIM
    )
    query_feat = (
        jax.nn.silu(queries.astype(jnp.float32))
        .astype(jnp.bfloat16)
        .reshape(nblocks, BLK, heads_here, HDIM)
    )
    key_feat = (
        jax.nn.silu(keys_quant.astype(jnp.float32))
        .astype(jnp.bfloat16)
        .reshape(nblocks, BLK, heads_here, HDIM)
    )
    decay_cum = jnp.cumsum(log_decay.reshape(heads_here, nblocks, BLK), axis=2)
    block_total = decay_cum[:, :, -1]
    scores = jnp.einsum("bihd,bjhd->hbij", query_feat, key_feat, preferred_element_type=jnp.float32)
    decay_gap = decay_cum[:, :, :, None] - decay_cum[:, :, None, :]
    causal_mask = jnp.arange(BLK)[:, None] >= jnp.arange(BLK)[None, :]
    decay_mask = jnp.where(causal_mask, jnp.exp(jnp.minimum(decay_gap, 0.0)), 0.0)
    block_probs = (scores * decay_mask).astype(jnp.bfloat16)
    within_block = jnp.einsum(
        "hbij,bjhd->bihd", block_probs, values, preferred_element_type=jnp.float32
    )
    tail_decay = jnp.transpose(jnp.exp(block_total[:, :, None] - decay_cum), (1, 2, 0))
    weighted = (key_feat.astype(jnp.float32) * tail_decay[..., None]).astype(jnp.bfloat16)
    block_states = jnp.einsum(
        "bjhd,bjhe->bhde", weighted, values, preferred_element_type=jnp.float32
    )
    block_gain = jnp.exp(block_total).T

    def advance(carried, inputs):
        gain_here, state_here = inputs
        return (gain_here[:, None, None] * carried + state_here, carried)

    local_end, entry_local = lax.scan(
        advance, jnp.zeros((heads_here, HDIM, HDIM), jnp.float32), (block_gain, block_states)
    )
    device_log = jnp.sum(block_total, axis=1)
    log_hi = device_log.astype(jnp.bfloat16)
    log_lo = (device_log - log_hi.astype(jnp.float32)).astype(jnp.bfloat16)
    packed = jnp.concatenate(
        [
            local_end.astype(jnp.bfloat16).reshape(heads_here, HDIM * HDIM),
            jnp.broadcast_to(log_hi[:, None], (heads_here, HDIM)),
            jnp.broadcast_to(log_lo[:, None], (heads_here, HDIM)),
        ],
        axis=1,
    )
    position = lax.axis_index("seq")
    incoming = jnp.zeros((heads_here, HDIM, HDIM), jnp.float32)
    gap = jnp.zeros((heads_here,), jnp.float32)
    for d in range(1, n_seq):
        came = lax.ppermute(packed, "seq", [(z, z + d) for z in range(n_seq - d)])
        came_state = came[:, : HDIM * HDIM].astype(jnp.float32).reshape(heads_here, HDIM, HDIM)
        came_log = came[:, HDIM * HDIM].astype(jnp.float32) + came[:, HDIM * HDIM + HDIM].astype(
            jnp.float32
        )
        weight = jnp.where(d <= position, jnp.exp(jnp.minimum(gap, 0.0)), 0.0)
        incoming = incoming + weight[:, None, None] * came_state
        gap = gap + came_log
    before = jnp.cumsum(block_total, axis=1) - block_total
    entry_state = entry_local + jnp.exp(before).T[:, :, None, None] * incoming[None]
    from_state = jnp.einsum(
        "bihd,bhde->bihe",
        query_feat.astype(jnp.float32),
        entry_state,
        precision=lax.Precision.HIGHEST,
    )
    position_decay = jnp.transpose(jnp.exp(decay_cum), (1, 2, 0))[..., None]
    attended = within_block + position_decay * from_state
    mean_square = jnp.mean(attended * attended, axis=-1, keepdims=True)
    normed = (attended * lax.rsqrt(mean_square + 1e-05)).reshape(tok_rows, heads_here * HDIM)
    attn = (normed * norm_gain[None, :] * jax.nn.sigmoid(gate_proj.astype(jnp.float32))).astype(
        jnp.bfloat16
    )

    rows_w, cols_w = weights.shape
    blocks_here = feat_here // rows_w
    piece = rows_w // n_mdl
    s_me = lax.axis_index("seq")
    m_me = lax.axis_index("mdl")
    if n_seq == 4 and n_mdl == 4:
        x_me = m_me // 2
        own_pieces = attn.reshape(tok_rows, n_mdl, piece)
        keep = lax.dynamic_slice_in_dim(own_pieces, 2 * x_me, 2, axis=1)
        away = lax.dynamic_slice_in_dim(own_pieces, 2 * (1 - x_me), 2, axis=1)
        came = lax.ppermute(away, "mdl", [(mu, mu ^ 2) for mu in range(n_mdl)])
        items = jnp.transpose(jnp.concatenate([keep, came], axis=1), (1, 0, 2))
        received = []
        for k in range(n_seq):
            perm = []
            for s in range(n_seq):
                for mu in range(n_mdl):
                    r = (s + k) % n_seq
                    f = mu if r // 2 == 0 else mu ^ 2
                    perm.append((s * n_mdl + mu, f * n_mdl + 2 * (mu // 2) + r % 2))
            item = lax.dynamic_index_in_dim(items, (s_me + k) % n_seq, 0, keepdims=False)
            received.append(lax.ppermute(item, ("seq", "mdl"), perm))
        received = jnp.stack(received)
        r_me = 2 * ((s_me // 2) != (m_me // 2)).astype(jnp.int32) + m_me % 2
        x = jnp.take(received, (r_me - jnp.arange(n_seq)) % n_seq, axis=0)
    else:
        received = []
        for k in range(n_seq):
            perm = []
            for s in range(n_seq):
                for m in range(n_mdl):
                    j = (s + k) % n_seq
                    f = m * blocks_here + j // n_mdl
                    perm.append((s * n_mdl + m, f * n_mdl + j % n_mdl))
            j_send = (s_me + k) % n_seq
            chunk = lax.dynamic_slice_in_dim(attn, j_send * piece, piece, axis=1)
            received.append(lax.ppermute(chunk, ("seq", "mdl"), perm))
        received = jnp.stack(received)
        j_me = (s_me % blocks_here) * n_mdl + m_me
        x = jnp.take(received, (j_me - jnp.arange(n_seq)) % n_seq, axis=0)

    n_x = n_mdl // 2
    core = m_me % 2
    xi = m_me // 2
    got = [x]
    for d in range(1, n_x):
        perm = [(mu, ((mu // 2 + d) % n_x) * 2 + mu % 2) for mu in range(n_mdl)]
        got.append(lax.ppermute(x, "mdl", perm))
    own = jnp.stack(got)
    other = lax.ppermute(own, "mdl", [(mu, mu ^ 1) for mu in range(n_mdl)])
    gathered_x = jnp.stack([own, other], axis=1)
    d_idx = jnp.arange(n_x)[:, None]
    e_idx = jnp.arange(2)[None, :]
    mu_tab = 2 * ((xi - d_idx) % n_x) + jnp.where(e_idx == 0, core, 1 - core)
    w_perm = jnp.take(
        weights.reshape(n_mdl, piece, cols_w), mu_tab.reshape(-1), axis=0
    ).reshape(n_x, 2, piece, cols_w)

    if n_seq == 4:
        all_partials = jnp.einsum(
            "desti,deic->stc", gathered_x, w_perm, preferred_element_type=jnp.float32
        )

        def partial_for(target):
            return lax.dynamic_index_in_dim(all_partials, target, 0, keepdims=False)

    else:

        def partial_for(target):
            rows = lax.dynamic_index_in_dim(gathered_x, target, 2, keepdims=False)
            return jnp.einsum(
                "deti,deic->tc", rows, w_perm, preferred_element_type=jnp.float32
            )

    if n_seq == 4:
        def bf(v):
            return v.astype(jnp.bfloat16)

        near_r = lax.ppermute(
            bf(partial_for(jnp.clip(s_me + 2, 0, 3))), "seq", [(0, 1), (1, 2)]
        )
        far_r = lax.ppermute(bf(partial_for(jnp.int32(3))), "seq", [(0, 3)])
        near_l = lax.ppermute(
            bf(partial_for(jnp.clip(s_me - 2, 0, 3))), "seq", [(3, 2), (2, 1)]
        )
        far_l = lax.ppermute(bf(partial_for(jnp.int32(0))), "seq", [(3, 0)])
        last_r = lax.ppermute(
            bf(partial_for(jnp.clip(s_me + 1, 0, 3)) + near_r.astype(jnp.float32)),
            "seq",
            [(0, 1), (1, 2), (2, 3)],
        )
        last_l = lax.ppermute(
            bf(partial_for(jnp.clip(s_me - 1, 0, 3)) + near_l.astype(jnp.float32)),
            "seq",
            [(3, 2), (2, 1), (1, 0)],
        )
        total = partial_for(s_me)
        for came in (last_r, far_r, last_l, far_l):
            total = total + came.astype(jnp.float32)
        return total.astype(jnp.bfloat16)

    halves = 2 if cols_w % 256 == 0 else 1
    width = cols_w // halves
    recv_r = [None] * halves
    recv_l = [None] * halves
    for i in range(1, n_seq):
        t_r = jnp.clip(s_me + n_seq - i, 0, n_seq - 1)
        t_l = jnp.clip(s_me - n_seq + i, 0, n_seq - 1)
        part_r = partial_for(t_r)
        part_l = partial_for(t_l)
        for h in range(halves):
            send_r = part_r[:, h * width : (h + 1) * width]
            send_l = part_l[:, h * width : (h + 1) * width]
            if recv_r[h] is not None:
                send_r = send_r + recv_r[h].astype(jnp.float32)
                send_l = send_l + recv_l[h].astype(jnp.float32)
            recv_r[h] = lax.ppermute(
                send_r.astype(jnp.bfloat16), "seq", [(z, z + 1) for z in range(i)]
            )
            recv_l[h] = lax.ppermute(
                send_l.astype(jnp.bfloat16), "seq", [(z, z - 1) for z in range(n_seq - i, n_seq)]
            )
    total = partial_for(s_me)
    if recv_r[0] is not None:
        total = total + jnp.concatenate(
            [recv_r[h].astype(jnp.float32) + recv_l[h].astype(jnp.float32) for h in range(halves)],
            axis=1,
        )
    return total.astype(jnp.bfloat16)


def solution(mesh):
    in_specs = (
        P(("grp", "seq"), "mdl"),
        P(("grp", "seq"), "mdl"),
        P(("grp", "seq"), "mdl"),
        P(("grp", "seq"), "mdl"),
        P("mdl", ("grp", "seq")),
        P(None, "mdl"),
        P("mdl"),
        P("seq", "mdl"),
        P("mdl"),
    )
    out_specs = P(("grp", "seq"), "mdl")
    n_seq = mesh.shape["seq"]
    n_mdl = mesh.shape["mdl"]

    def body(*args):
        return per_device(n_seq, n_mdl, *args)

    return jax.shard_map(
        body, mesh=mesh, in_specs=in_specs, out_specs=out_specs, check_vma=False
    )
```

```python
import jax
import jax.numpy as jnp
from jax import lax
from jax.sharding import PartitionSpec as P

HDIM = 128
BLK = 256


def power_two(exponent):
    result = jnp.zeros(exponent.shape, jnp.float32)
    for exponent_value in range(-16, 0):
        result = result + jnp.where(exponent == exponent_value, 2.0**exponent_value, 0.0)
    return result


def fake_quant(matrix, exponent):
    scale = power_two(exponent)
    levels = jnp.clip(jnp.floor(matrix.astype(jnp.float32) / scale + 0.5), -127.0, 127.0)
    return (levels * scale).astype(jnp.bfloat16)


def per_device(
    n_seq,
    n_mdl,
    query_proj,
    key_proj,
    value_proj,
    gate_proj,
    log_decay,
    act_exponent,
    norm_gain,
    out_weight,
    weight_exponent,
):
    weights = fake_quant(out_weight, weight_exponent[None, :])
    tok_rows = query_proj.shape[0]
    feat_here = query_proj.shape[1]
    heads_here = log_decay.shape[0]
    nblocks = tok_rows // BLK
    queries = fake_quant(query_proj, act_exponent[0][None, :])
    keys_quant = fake_quant(key_proj, act_exponent[1][None, :])
    values = fake_quant(value_proj, act_exponent[2][None, :]).reshape(
        nblocks, BLK, heads_here, HDIM
    )
    query_feat = (
        jax.nn.silu(queries.astype(jnp.float32))
        .astype(jnp.bfloat16)
        .reshape(nblocks, BLK, heads_here, HDIM)
    )
    key_feat = (
        jax.nn.silu(keys_quant.astype(jnp.float32))
        .astype(jnp.bfloat16)
        .reshape(nblocks, BLK, heads_here, HDIM)
    )
    decay_cum = jnp.cumsum(log_decay.reshape(heads_here, nblocks, BLK), axis=2)
    block_total = decay_cum[:, :, -1]
    scores = jnp.einsum("bihd,bjhd->hbij", query_feat, key_feat, preferred_element_type=jnp.float32)
    decay_gap = decay_cum[:, :, :, None] - decay_cum[:, :, None, :]
    causal_mask = jnp.arange(BLK)[:, None] >= jnp.arange(BLK)[None, :]
    decay_mask = jnp.where(causal_mask, jnp.exp(jnp.minimum(decay_gap, 0.0)), 0.0)
    block_probs = (scores * decay_mask).astype(jnp.bfloat16)
    within_block = jnp.einsum(
        "hbij,bjhd->bihd", block_probs, values, preferred_element_type=jnp.float32
    )
    tail_decay = jnp.transpose(jnp.exp(block_total[:, :, None] - decay_cum), (1, 2, 0))
    weighted = (key_feat.astype(jnp.float32) * tail_decay[..., None]).astype(jnp.bfloat16)
    block_states = jnp.einsum(
        "bjhd,bjhe->bhde", weighted, values, preferred_element_type=jnp.float32
    )
    block_gain = jnp.exp(block_total).T

    def advance(carried, inputs):
        gain_here, state_here = inputs
        return (gain_here[:, None, None] * carried + state_here, carried)

    local_end, entry_local = lax.scan(
        advance, jnp.zeros((heads_here, HDIM, HDIM), jnp.float32), (block_gain, block_states)
    )
    device_log = jnp.sum(block_total, axis=1)
    log_hi = device_log.astype(jnp.bfloat16)
    log_lo = (device_log - log_hi.astype(jnp.float32)).astype(jnp.bfloat16)
    packed = jnp.concatenate(
        [
            local_end.astype(jnp.bfloat16).reshape(heads_here, HDIM * HDIM),
            jnp.broadcast_to(log_hi[:, None], (heads_here, HDIM)),
            jnp.broadcast_to(log_lo[:, None], (heads_here, HDIM)),
        ],
        axis=1,
    )
    position = lax.axis_index("seq")
    incoming = jnp.zeros((heads_here, HDIM, HDIM), jnp.float32)
    gap = jnp.zeros((heads_here,), jnp.float32)
    for d in range(1, n_seq):
        came = lax.ppermute(packed, "seq", [(z, z + d) for z in range(n_seq - d)])
        came_state = came[:, : HDIM * HDIM].astype(jnp.float32).reshape(heads_here, HDIM, HDIM)
        came_log = came[:, HDIM * HDIM].astype(jnp.float32) + came[:, HDIM * HDIM + HDIM].astype(
            jnp.float32
        )
        weight = jnp.where(d <= position, jnp.exp(jnp.minimum(gap, 0.0)), 0.0)
        incoming = incoming + weight[:, None, None] * came_state
        gap = gap + came_log
    before = jnp.cumsum(block_total, axis=1) - block_total
    entry_state = entry_local + jnp.exp(before).T[:, :, None, None] * incoming[None]
    from_state = jnp.einsum(
        "bihd,bhde->bihe",
        query_feat.astype(jnp.float32),
        entry_state,
        precision=lax.Precision.HIGHEST,
    )
    position_decay = jnp.transpose(jnp.exp(decay_cum), (1, 2, 0))[..., None]
    attended = within_block + position_decay * from_state
    mean_square = jnp.mean(attended * attended, axis=-1, keepdims=True)
    normed = (attended * lax.rsqrt(mean_square + 1e-05)).reshape(tok_rows, heads_here * HDIM)
    attn = (normed * norm_gain[None, :] * jax.nn.sigmoid(gate_proj.astype(jnp.float32))).astype(
        jnp.bfloat16
    )

    rows_w, cols_w = weights.shape
    blocks_here = feat_here // rows_w
    piece = rows_w // n_mdl
    s_me = lax.axis_index("seq")
    m_me = lax.axis_index("mdl")
    if n_seq == 4 and n_mdl == 4:
        b_me = m_me % 2
        partner_attn = lax.ppermute(attn, "mdl", [(mu, mu ^ 2) for mu in range(n_mdl)])
        pair = 2 * piece
        items = []
        for blk in (attn, partner_attn):
            halves_of = blk.reshape(tok_rows, 2, pair)
            items.append(jnp.transpose(halves_of, (1, 0, 2)))
        items = jnp.concatenate(items, axis=0)
        received = []
        for k in range(n_seq):
            perm = []
            for s in range(n_seq):
                for mu in range(n_mdl):
                    r = (s + k) % n_seq
                    f = mu if r // 2 == 0 else mu ^ 2
                    perm.append((s * n_mdl + mu, f * n_mdl + 2 * (mu // 2) + r % 2))
            item = lax.dynamic_index_in_dim(items, (s_me + k) % n_seq, 0, keepdims=False)
            received.append(lax.ppermute(item, ("seq", "mdl"), perm))
        received = jnp.stack(received)
        r_me = 2 * ((s_me // 2) != (m_me // 2)).astype(jnp.int32) + b_me
        mine = jnp.take(received, (r_me - jnp.arange(n_seq)) % n_seq, axis=0)
        theirs = lax.ppermute(mine, "mdl", [(mu, mu ^ 1) for mu in range(n_mdl)])
        w_mine = lax.dynamic_slice_in_dim(weights, b_me * pair, pair, axis=0)
        w_theirs = lax.dynamic_slice_in_dim(weights, (1 - b_me) * pair, pair, axis=0)

        def partial_for(target):
            rows_mine = lax.dynamic_index_in_dim(mine, target, 0, keepdims=False)
            rows_theirs = lax.dynamic_index_in_dim(theirs, target, 0, keepdims=False)
            return jnp.dot(rows_mine, w_mine, preferred_element_type=jnp.float32) + jnp.dot(
                rows_theirs, w_theirs, preferred_element_type=jnp.float32
            )

    else:
        received = []
        for k in range(n_seq):
            perm = []
            for s in range(n_seq):
                for m in range(n_mdl):
                    j = (s + k) % n_seq
                    f = m * blocks_here + j // n_mdl
                    perm.append((s * n_mdl + m, f * n_mdl + j % n_mdl))
            j_send = (s_me + k) % n_seq
            chunk = lax.dynamic_slice_in_dim(attn, j_send * piece, piece, axis=1)
            received.append(lax.ppermute(chunk, ("seq", "mdl"), perm))
        received = jnp.stack(received)
        j_me = (s_me % blocks_here) * n_mdl + m_me
        x = jnp.take(received, (j_me - jnp.arange(n_seq)) % n_seq, axis=0)

        n_x = n_mdl // 2
        core = m_me % 2
        xi = m_me // 2
        got = [x]
        for d in range(1, n_x):
            perm = [(mu, ((mu // 2 + d) % n_x) * 2 + mu % 2) for mu in range(n_mdl)]
            got.append(lax.ppermute(x, "mdl", perm))
        own = jnp.stack(got)
        other = lax.ppermute(own, "mdl", [(mu, mu ^ 1) for mu in range(n_mdl)])
        gathered_x = jnp.stack([own, other], axis=1)
        d_idx = jnp.arange(n_x)[:, None]
        e_idx = jnp.arange(2)[None, :]
        mu_tab = 2 * ((xi - d_idx) % n_x) + jnp.where(e_idx == 0, core, 1 - core)
        w_perm = jnp.take(
            weights.reshape(n_mdl, piece, cols_w), mu_tab.reshape(-1), axis=0
        ).reshape(n_x, 2, piece, cols_w)

        def partial_for(target):
            rows = lax.dynamic_index_in_dim(gathered_x, target, 2, keepdims=False)
            return jnp.einsum(
                "deti,deic->tc", rows, w_perm, preferred_element_type=jnp.float32
            )

    if n_seq == 4:
        def bf(v):
            return v.astype(jnp.bfloat16)

        near_r = lax.ppermute(
            bf(partial_for(jnp.clip(s_me + 2, 0, 3))), "seq", [(0, 1), (1, 2)]
        )
        far_r = lax.ppermute(bf(partial_for(jnp.int32(3))), "seq", [(0, 3)])
        near_l = lax.ppermute(
            bf(partial_for(jnp.clip(s_me - 2, 0, 3))), "seq", [(3, 2), (2, 1)]
        )
        far_l = lax.ppermute(bf(partial_for(jnp.int32(0))), "seq", [(3, 0)])
        last_r = lax.ppermute(
            bf(partial_for(jnp.clip(s_me + 1, 0, 3)) + near_r.astype(jnp.float32)),
            "seq",
            [(0, 1), (1, 2), (2, 3)],
        )
        last_l = lax.ppermute(
            bf(partial_for(jnp.clip(s_me - 1, 0, 3)) + near_l.astype(jnp.float32)),
            "seq",
            [(3, 2), (2, 1), (1, 0)],
        )
        total = partial_for(s_me)
        for came in (last_r, far_r, last_l, far_l):
            total = total + came.astype(jnp.float32)
        return total.astype(jnp.bfloat16)

    halves = 2 if cols_w % 256 == 0 else 1
    width = cols_w // halves
    recv_r = [None] * halves
    recv_l = [None] * halves
    for i in range(1, n_seq):
        t_r = jnp.clip(s_me + n_seq - i, 0, n_seq - 1)
        t_l = jnp.clip(s_me - n_seq + i, 0, n_seq - 1)
        part_r = partial_for(t_r)
        part_l = partial_for(t_l)
        for h in range(halves):
            send_r = part_r[:, h * width : (h + 1) * width]
            send_l = part_l[:, h * width : (h + 1) * width]
            if recv_r[h] is not None:
                send_r = send_r + recv_r[h].astype(jnp.float32)
                send_l = send_l + recv_l[h].astype(jnp.float32)
            recv_r[h] = lax.ppermute(
                send_r.astype(jnp.bfloat16), "seq", [(z, z + 1) for z in range(i)]
            )
            recv_l[h] = lax.ppermute(
                send_l.astype(jnp.bfloat16), "seq", [(z, z - 1) for z in range(n_seq - i, n_seq)]
            )
    total = partial_for(s_me)
    if recv_r[0] is not None:
        total = total + jnp.concatenate(
            [recv_r[h].astype(jnp.float32) + recv_l[h].astype(jnp.float32) for h in range(halves)],
            axis=1,
        )
    return total.astype(jnp.bfloat16)


def solution(mesh):
    in_specs = (
        P(("grp", "seq"), "mdl"),
        P(("grp", "seq"), "mdl"),
        P(("grp", "seq"), "mdl"),
        P(("grp", "seq"), "mdl"),
        P("mdl", ("grp", "seq")),
        P(None, "mdl"),
        P("mdl"),
        P("seq", "mdl"),
        P("mdl"),
    )
    out_specs = P(("grp", "seq"), "mdl")
    n_seq = mesh.shape["seq"]
    n_mdl = mesh.shape["mdl"]

    def body(*args):
        return per_device(n_seq, n_mdl, *args)

    return jax.shard_map(
        body, mesh=mesh, in_specs=in_specs, out_specs=out_specs, check_vma=False
    )
```

```python
import jax
import jax.numpy as jnp
from jax import lax
from jax.sharding import PartitionSpec as P

HDIM = 128
BLK = 256


def power_two(exponent):
    result = jnp.zeros(exponent.shape, jnp.float32)
    for exponent_value in range(-16, 0):
        result = result + jnp.where(exponent == exponent_value, 2.0**exponent_value, 0.0)
    return result


def fake_quant(matrix, exponent):
    scale = power_two(exponent)
    levels = jnp.clip(jnp.floor(matrix.astype(jnp.float32) / scale + 0.5), -127.0, 127.0)
    return (levels * scale).astype(jnp.bfloat16)


def per_device(
    n_seq,
    n_mdl,
    query_proj,
    key_proj,
    value_proj,
    gate_proj,
    log_decay,
    act_exponent,
    norm_gain,
    out_weight,
    weight_exponent,
):
    weights = fake_quant(out_weight, weight_exponent[None, :])
    tok_rows = query_proj.shape[0]
    feat_here = query_proj.shape[1]
    heads_here = log_decay.shape[0]
    nblocks = tok_rows // BLK
    queries = fake_quant(query_proj, act_exponent[0][None, :])
    keys_quant = fake_quant(key_proj, act_exponent[1][None, :])
    values = fake_quant(value_proj, act_exponent[2][None, :]).reshape(
        nblocks, BLK, heads_here, HDIM
    )
    query_feat = (
        jax.nn.silu(queries.astype(jnp.float32))
        .astype(jnp.bfloat16)
        .reshape(nblocks, BLK, heads_here, HDIM)
    )
    key_feat = (
        jax.nn.silu(keys_quant.astype(jnp.float32))
        .astype(jnp.bfloat16)
        .reshape(nblocks, BLK, heads_here, HDIM)
    )
    decay_cum = jnp.cumsum(log_decay.reshape(heads_here, nblocks, BLK), axis=2)
    block_total = decay_cum[:, :, -1]
    scores = jnp.einsum("bihd,bjhd->hbij", query_feat, key_feat, preferred_element_type=jnp.float32)
    decay_gap = decay_cum[:, :, :, None] - decay_cum[:, :, None, :]
    causal_mask = jnp.arange(BLK)[:, None] >= jnp.arange(BLK)[None, :]
    decay_mask = jnp.where(causal_mask, jnp.exp(jnp.minimum(decay_gap, 0.0)), 0.0)
    block_probs = (scores * decay_mask).astype(jnp.bfloat16)
    within_block = jnp.einsum(
        "hbij,bjhd->bihd", block_probs, values, preferred_element_type=jnp.float32
    )
    tail_decay = jnp.transpose(jnp.exp(block_total[:, :, None] - decay_cum), (1, 2, 0))
    weighted = (key_feat.astype(jnp.float32) * tail_decay[..., None]).astype(jnp.bfloat16)
    block_states = jnp.einsum(
        "bjhd,bjhe->bhde", weighted, values, preferred_element_type=jnp.float32
    )
    block_gain = jnp.exp(block_total).T

    def advance(carried, inputs):
        gain_here, state_here = inputs
        return (gain_here[:, None, None] * carried + state_here, carried)

    local_end, entry_local = lax.scan(
        advance, jnp.zeros((heads_here, HDIM, HDIM), jnp.float32), (block_gain, block_states)
    )
    device_log = jnp.sum(block_total, axis=1)
    log_hi = device_log.astype(jnp.bfloat16)
    log_lo = (device_log - log_hi.astype(jnp.float32)).astype(jnp.bfloat16)
    packed = jnp.concatenate(
        [
            local_end.astype(jnp.bfloat16).reshape(heads_here, HDIM * HDIM),
            jnp.broadcast_to(log_hi[:, None], (heads_here, HDIM)),
            jnp.broadcast_to(log_lo[:, None], (heads_here, HDIM)),
        ],
        axis=1,
    )
    position = lax.axis_index("seq")
    incoming = jnp.zeros((heads_here, HDIM, HDIM), jnp.float32)
    gap = jnp.zeros((heads_here,), jnp.float32)
    for d in range(1, n_seq):
        came = lax.ppermute(packed, "seq", [(z, z + d) for z in range(n_seq - d)])
        came_state = came[:, : HDIM * HDIM].astype(jnp.float32).reshape(heads_here, HDIM, HDIM)
        came_log = came[:, HDIM * HDIM].astype(jnp.float32) + came[:, HDIM * HDIM + HDIM].astype(
            jnp.float32
        )
        weight = jnp.where(d <= position, jnp.exp(jnp.minimum(gap, 0.0)), 0.0)
        incoming = incoming + weight[:, None, None] * came_state
        gap = gap + came_log
    before = jnp.cumsum(block_total, axis=1) - block_total
    entry_state = entry_local + jnp.exp(before).T[:, :, None, None] * incoming[None]
    from_state = jnp.einsum(
        "bihd,bhde->bihe",
        query_feat.astype(jnp.float32),
        entry_state,
        precision=lax.Precision.HIGHEST,
    )
    position_decay = jnp.transpose(jnp.exp(decay_cum), (1, 2, 0))[..., None]
    attended = within_block + position_decay * from_state
    mean_square = jnp.mean(attended * attended, axis=-1, keepdims=True)
    normed = (attended * lax.rsqrt(mean_square + 1e-05)).reshape(tok_rows, heads_here * HDIM)
    attn = (normed * norm_gain[None, :] * jax.nn.sigmoid(gate_proj.astype(jnp.float32))).astype(
        jnp.bfloat16
    )

    rows_w, cols_w = weights.shape
    blocks_here = feat_here // rows_w
    piece = rows_w // n_mdl
    s_me = lax.axis_index("seq")
    m_me = lax.axis_index("mdl")
    if n_seq == 4 and n_mdl == 4:
        x_me = m_me // 2
        own_pieces = attn.reshape(tok_rows, n_mdl, piece)
        keep = lax.dynamic_slice_in_dim(own_pieces, 2 * x_me, 2, axis=1)
        away = lax.dynamic_slice_in_dim(own_pieces, 2 * (1 - x_me), 2, axis=1)
        came = lax.ppermute(away, "mdl", [(mu, mu ^ 2) for mu in range(n_mdl)])
        items = jnp.transpose(jnp.concatenate([keep, came], axis=1), (1, 0, 2))
        received = []
        for k in range(n_seq):
            perm = []
            for s in range(n_seq):
                for mu in range(n_mdl):
                    r = (s + k) % n_seq
                    f = mu if r // 2 == 0 else mu ^ 2
                    perm.append((s * n_mdl + mu, f * n_mdl + 2 * (mu // 2) + r % 2))
            item = lax.dynamic_index_in_dim(items, (s_me + k) % n_seq, 0, keepdims=False)
            received.append(lax.ppermute(item, ("seq", "mdl"), perm))
        received = jnp.stack(received)
        r_me = 2 * ((s_me // 2) != (m_me // 2)).astype(jnp.int32) + m_me % 2
        x = jnp.take(received, (r_me - jnp.arange(n_seq)) % n_seq, axis=0)
    else:
        received = []
        for k in range(n_seq):
            perm = []
            for s in range(n_seq):
                for m in range(n_mdl):
                    j = (s + k) % n_seq
                    f = m * blocks_here + j // n_mdl
                    perm.append((s * n_mdl + m, f * n_mdl + j % n_mdl))
            j_send = (s_me + k) % n_seq
            chunk = lax.dynamic_slice_in_dim(attn, j_send * piece, piece, axis=1)
            received.append(lax.ppermute(chunk, ("seq", "mdl"), perm))
        received = jnp.stack(received)
        j_me = (s_me % blocks_here) * n_mdl + m_me
        x = jnp.take(received, (j_me - jnp.arange(n_seq)) % n_seq, axis=0)

    n_x = n_mdl // 2
    core = m_me % 2
    xi = m_me // 2
    got = [x]
    for d in range(1, n_x):
        perm = [(mu, ((mu // 2 + d) % n_x) * 2 + mu % 2) for mu in range(n_mdl)]
        got.append(lax.ppermute(x, "mdl", perm))
    own = jnp.stack(got)
    other = lax.ppermute(own, "mdl", [(mu, mu ^ 1) for mu in range(n_mdl)])
    gathered_x = jnp.stack([own, other], axis=1)
    d_idx = jnp.arange(n_x)[:, None]
    e_idx = jnp.arange(2)[None, :]
    mu_tab = 2 * ((xi - d_idx) % n_x) + jnp.where(e_idx == 0, core, 1 - core)
    w_perm = jnp.take(
        weights.reshape(n_mdl, piece, cols_w), mu_tab.reshape(-1), axis=0
    ).reshape(n_x, 2, piece, cols_w)

    def partial_for(target):
        rows = lax.dynamic_index_in_dim(gathered_x, target, 2, keepdims=False)
        return jnp.einsum(
            "deti,deic->tc", rows, w_perm, preferred_element_type=jnp.float32
        )

    if n_seq == 4:
        def bf(v):
            return v.astype(jnp.bfloat16)

        near_r = lax.ppermute(
            bf(partial_for(jnp.clip(s_me + 2, 0, 3))), "seq", [(0, 1), (1, 2)]
        )
        near_l = lax.ppermute(
            bf(partial_for(jnp.clip(s_me - 2, 0, 3))), "seq", [(3, 2), (2, 1)]
        )
        far_r = lax.ppermute(
            bf(partial_for(jnp.int32(3))) + near_r * jnp.bfloat16(0), "seq", [(0, 3)]
        )
        far_l = lax.ppermute(
            bf(partial_for(jnp.int32(0))) + near_l * jnp.bfloat16(0), "seq", [(3, 0)]
        )
        last_r = lax.ppermute(
            bf(partial_for(jnp.clip(s_me + 1, 0, 3)) + near_r.astype(jnp.float32)),
            "seq",
            [(0, 1), (1, 2), (2, 3)],
        )
        last_l = lax.ppermute(
            bf(partial_for(jnp.clip(s_me - 1, 0, 3)) + near_l.astype(jnp.float32)),
            "seq",
            [(3, 2), (2, 1), (1, 0)],
        )
        total = partial_for(s_me)
        for came in (last_r, far_r, last_l, far_l):
            total = total + came.astype(jnp.float32)
        return total.astype(jnp.bfloat16)

    halves = 2 if cols_w % 256 == 0 else 1
    width = cols_w // halves
    recv_r = [None] * halves
    recv_l = [None] * halves
    for i in range(1, n_seq):
        t_r = jnp.clip(s_me + n_seq - i, 0, n_seq - 1)
        t_l = jnp.clip(s_me - n_seq + i, 0, n_seq - 1)
        part_r = partial_for(t_r)
        part_l = partial_for(t_l)
        for h in range(halves):
            send_r = part_r[:, h * width : (h + 1) * width]
            send_l = part_l[:, h * width : (h + 1) * width]
            if recv_r[h] is not None:
                send_r = send_r + recv_r[h].astype(jnp.float32)
                send_l = send_l + recv_l[h].astype(jnp.float32)
            recv_r[h] = lax.ppermute(
                send_r.astype(jnp.bfloat16), "seq", [(z, z + 1) for z in range(i)]
            )
            recv_l[h] = lax.ppermute(
                send_l.astype(jnp.bfloat16), "seq", [(z, z - 1) for z in range(n_seq - i, n_seq)]
            )
    total = partial_for(s_me)
    if recv_r[0] is not None:
        total = total + jnp.concatenate(
            [recv_r[h].astype(jnp.float32) + recv_l[h].astype(jnp.float32) for h in range(halves)],
            axis=1,
        )
    return total.astype(jnp.bfloat16)


def solution(mesh):
    in_specs = (
        P(("grp", "seq"), "mdl"),
        P(("grp", "seq"), "mdl"),
        P(("grp", "seq"), "mdl"),
        P(("grp", "seq"), "mdl"),
        P("mdl", ("grp", "seq")),
        P(None, "mdl"),
        P("mdl"),
        P("seq", "mdl"),
        P("mdl"),
    )
    out_specs = P(("grp", "seq"), "mdl")
    n_seq = mesh.shape["seq"]
    n_mdl = mesh.shape["mdl"]

    def body(*args):
        return per_device(n_seq, n_mdl, *args)

    return jax.shard_map(
        body, mesh=mesh, in_specs=in_specs, out_specs=out_specs, check_vma=False
    )
```

```python
import jax
import jax.numpy as jnp
from jax import lax
from jax.sharding import PartitionSpec as P

HDIM = 128
BLK = 256


def power_two(exponent):
    result = jnp.zeros(exponent.shape, jnp.float32)
    for exponent_value in range(-16, 0):
        result = result + jnp.where(exponent == exponent_value, 2.0**exponent_value, 0.0)
    return result


def fake_quant(matrix, exponent):
    scale = power_two(exponent)
    levels = jnp.clip(jnp.floor(matrix.astype(jnp.float32) / scale + 0.5), -127.0, 127.0)
    return (levels * scale).astype(jnp.bfloat16)


def per_device(
    n_seq,
    n_mdl,
    query_proj,
    key_proj,
    value_proj,
    gate_proj,
    log_decay,
    act_exponent,
    norm_gain,
    out_weight,
    weight_exponent,
):
    weights = fake_quant(out_weight, weight_exponent[None, :])
    tok_rows = query_proj.shape[0]
    feat_here = query_proj.shape[1]
    heads_here = log_decay.shape[0]
    nblocks = tok_rows // BLK
    queries = fake_quant(query_proj, act_exponent[0][None, :])
    keys_quant = fake_quant(key_proj, act_exponent[1][None, :])
    values = fake_quant(value_proj, act_exponent[2][None, :]).reshape(
        nblocks, BLK, heads_here, HDIM
    )
    query_feat = (
        jax.nn.silu(queries.astype(jnp.float32))
        .astype(jnp.bfloat16)
        .reshape(nblocks, BLK, heads_here, HDIM)
    )
    key_feat = (
        jax.nn.silu(keys_quant.astype(jnp.float32))
        .astype(jnp.bfloat16)
        .reshape(nblocks, BLK, heads_here, HDIM)
    )
    decay_cum = jnp.cumsum(log_decay.reshape(heads_here, nblocks, BLK), axis=2)
    block_total = decay_cum[:, :, -1]
    scores = jnp.einsum("bihd,bjhd->hbij", query_feat, key_feat, preferred_element_type=jnp.float32)
    decay_gap = decay_cum[:, :, :, None] - decay_cum[:, :, None, :]
    causal_mask = jnp.arange(BLK)[:, None] >= jnp.arange(BLK)[None, :]
    decay_mask = jnp.where(causal_mask, jnp.exp(jnp.minimum(decay_gap, 0.0)), 0.0)
    block_probs = (scores * decay_mask).astype(jnp.bfloat16)
    within_block = jnp.einsum(
        "hbij,bjhd->bihd", block_probs, values, preferred_element_type=jnp.float32
    )
    tail_decay = jnp.transpose(jnp.exp(block_total[:, :, None] - decay_cum), (1, 2, 0))
    weighted = (key_feat.astype(jnp.float32) * tail_decay[..., None]).astype(jnp.bfloat16)
    block_states = jnp.einsum(
        "bjhd,bjhe->bhde", weighted, values, preferred_element_type=jnp.float32
    )
    block_gain = jnp.exp(block_total).T

    def advance(carried, inputs):
        gain_here, state_here = inputs
        return (gain_here[:, None, None] * carried + state_here, carried)

    local_end, entry_local = lax.scan(
        advance, jnp.zeros((heads_here, HDIM, HDIM), jnp.float32), (block_gain, block_states)
    )
    device_log = jnp.sum(block_total, axis=1)
    log_hi = device_log.astype(jnp.bfloat16)
    log_lo = (device_log - log_hi.astype(jnp.float32)).astype(jnp.bfloat16)
    packed = jnp.concatenate(
        [
            local_end.astype(jnp.bfloat16).reshape(heads_here, HDIM * HDIM),
            jnp.broadcast_to(log_hi[:, None], (heads_here, HDIM)),
            jnp.broadcast_to(log_lo[:, None], (heads_here, HDIM)),
        ],
        axis=1,
    )
    position = lax.axis_index("seq")
    incoming = jnp.zeros((heads_here, HDIM, HDIM), jnp.float32)
    gap = jnp.zeros((heads_here,), jnp.float32)
    for d in range(1, n_seq):
        came = lax.ppermute(packed, "seq", [(z, z + d) for z in range(n_seq - d)])
        came_state = came[:, : HDIM * HDIM].astype(jnp.float32).reshape(heads_here, HDIM, HDIM)
        came_log = came[:, HDIM * HDIM].astype(jnp.float32) + came[:, HDIM * HDIM + HDIM].astype(
            jnp.float32
        )
        weight = jnp.where(d <= position, jnp.exp(jnp.minimum(gap, 0.0)), 0.0)
        incoming = incoming + weight[:, None, None] * came_state
        gap = gap + came_log
    before = jnp.cumsum(block_total, axis=1) - block_total
    entry_state = entry_local + jnp.exp(before).T[:, :, None, None] * incoming[None]
    from_state = jnp.einsum(
        "bihd,bhde->bihe",
        query_feat.astype(jnp.float32),
        entry_state,
        precision=lax.Precision.HIGHEST,
    )
    position_decay = jnp.transpose(jnp.exp(decay_cum), (1, 2, 0))[..., None]
    attended = within_block + position_decay * from_state
    mean_square = jnp.mean(attended * attended, axis=-1, keepdims=True)
    normed = (attended * lax.rsqrt(mean_square + 1e-05)).reshape(tok_rows, heads_here * HDIM)
    attn = (normed * norm_gain[None, :] * jax.nn.sigmoid(gate_proj.astype(jnp.float32))).astype(
        jnp.bfloat16
    )

    rows_w, cols_w = weights.shape
    blocks_here = feat_here // rows_w
    piece = rows_w // n_mdl
    s_me = lax.axis_index("seq")
    m_me = lax.axis_index("mdl")
    if n_seq == 4 and n_mdl == 4:
        x_me = m_me // 2
        own_pieces = attn.reshape(tok_rows, n_mdl, piece)
        keep = lax.dynamic_slice_in_dim(own_pieces, 2 * x_me, 2, axis=1)
        away = lax.dynamic_slice_in_dim(own_pieces, 2 * (1 - x_me), 2, axis=1)
        came = lax.ppermute(away, "mdl", [(mu, mu ^ 2) for mu in range(n_mdl)])
        items = jnp.transpose(jnp.concatenate([keep, came], axis=1), (1, 0, 2))
        received = []
        for k in range(n_seq):
            perm = []
            for s in range(n_seq):
                for mu in range(n_mdl):
                    r = (s + k) % n_seq
                    f = mu if r // 2 == 0 else mu ^ 2
                    perm.append((s * n_mdl + mu, f * n_mdl + 2 * (mu // 2) + r % 2))
            item = lax.dynamic_index_in_dim(items, (s_me + k) % n_seq, 0, keepdims=False)
            received.append(lax.ppermute(item, ("seq", "mdl"), perm))
        received = jnp.stack(received)
        r_me = 2 * ((s_me // 2) != (m_me // 2)).astype(jnp.int32) + m_me % 2
        x = jnp.take(received, (r_me - jnp.arange(n_seq)) % n_seq, axis=0)
    else:
        received = []
        for k in range(n_seq):
            perm = []
            for s in range(n_seq):
                for m in range(n_mdl):
                    j = (s + k) % n_seq
                    f = m * blocks_here + j // n_mdl
                    perm.append((s * n_mdl + m, f * n_mdl + j % n_mdl))
            j_send = (s_me + k) % n_seq
            chunk = lax.dynamic_slice_in_dim(attn, j_send * piece, piece, axis=1)
            received.append(lax.ppermute(chunk, ("seq", "mdl"), perm))
        received = jnp.stack(received)
        j_me = (s_me % blocks_here) * n_mdl + m_me
        x = jnp.take(received, (j_me - jnp.arange(n_seq)) % n_seq, axis=0)

    n_x = n_mdl // 2
    core = m_me % 2
    xi = m_me // 2
    got = [x]
    for d in range(1, n_x):
        perm = [(mu, ((mu // 2 + d) % n_x) * 2 + mu % 2) for mu in range(n_mdl)]
        got.append(lax.ppermute(x, "mdl", perm))
    own = jnp.stack(got)
    other = lax.ppermute(own, "mdl", [(mu, mu ^ 1) for mu in range(n_mdl)])
    gathered_x = jnp.stack([own, other], axis=1)
    d_idx = jnp.arange(n_x)[:, None]
    e_idx = jnp.arange(2)[None, :]
    mu_tab = 2 * ((xi - d_idx) % n_x) + jnp.where(e_idx == 0, core, 1 - core)
    w_perm = jnp.take(
        weights.reshape(n_mdl, piece, cols_w), mu_tab.reshape(-1), axis=0
    ).reshape(n_x, 2, piece, cols_w)

    def partial_for(target):
        rows = lax.dynamic_index_in_dim(gathered_x, target, 2, keepdims=False)
        return jnp.einsum(
            "deti,deic->tc", rows, w_perm, preferred_element_type=jnp.float32
        )

    if n_seq == 4:
        def bf(v):
            return v.astype(jnp.bfloat16)

        near_r = lax.ppermute(
            bf(partial_for(jnp.clip(s_me + 2, 0, 3))), "seq", [(0, 1), (1, 2)]
        )
        far_r = lax.ppermute(bf(partial_for(jnp.int32(3))), "seq", [(0, 3)])
        near_l = lax.ppermute(
            bf(partial_for(jnp.clip(s_me - 2, 0, 3))), "seq", [(3, 2), (2, 1)]
        )
        far_l = lax.ppermute(bf(partial_for(jnp.int32(0))), "seq", [(3, 0)])
        own_part = partial_for(s_me)
        last_r = lax.ppermute(
            bf(
                partial_for(jnp.clip(s_me + 1, 0, 3))
                + near_r.astype(jnp.float32)
                + own_part * 0.0
            ),
            "seq",
            [(0, 1), (1, 2), (2, 3)],
        )
        last_l = lax.ppermute(
            bf(partial_for(jnp.clip(s_me - 1, 0, 3)) + near_l.astype(jnp.float32)),
            "seq",
            [(3, 2), (2, 1), (1, 0)],
        )
        total = own_part
        for came in (last_r, far_r, last_l, far_l):
            total = total + came.astype(jnp.float32)
        return total.astype(jnp.bfloat16)

    halves = 2 if cols_w % 256 == 0 else 1
    width = cols_w // halves
    recv_r = [None] * halves
    recv_l = [None] * halves
    for i in range(1, n_seq):
        t_r = jnp.clip(s_me + n_seq - i, 0, n_seq - 1)
        t_l = jnp.clip(s_me - n_seq + i, 0, n_seq - 1)
        part_r = partial_for(t_r)
        part_l = partial_for(t_l)
        for h in range(halves):
            send_r = part_r[:, h * width : (h + 1) * width]
            send_l = part_l[:, h * width : (h + 1) * width]
            if recv_r[h] is not None:
                send_r = send_r + recv_r[h].astype(jnp.float32)
                send_l = send_l + recv_l[h].astype(jnp.float32)
            recv_r[h] = lax.ppermute(
                send_r.astype(jnp.bfloat16), "seq", [(z, z + 1) for z in range(i)]
            )
            recv_l[h] = lax.ppermute(
                send_l.astype(jnp.bfloat16), "seq", [(z, z - 1) for z in range(n_seq - i, n_seq)]
            )
    total = partial_for(s_me)
    if recv_r[0] is not None:
        total = total + jnp.concatenate(
            [recv_r[h].astype(jnp.float32) + recv_l[h].astype(jnp.float32) for h in range(halves)],
            axis=1,
        )
    return total.astype(jnp.bfloat16)


def solution(mesh):
    in_specs = (
        P(("grp", "seq"), "mdl"),
        P(("grp", "seq"), "mdl"),
        P(("grp", "seq"), "mdl"),
        P(("grp", "seq"), "mdl"),
        P("mdl", ("grp", "seq")),
        P(None, "mdl"),
        P("mdl"),
        P("seq", "mdl"),
        P("mdl"),
    )
    out_specs = P(("grp", "seq"), "mdl")
    n_seq = mesh.shape["seq"]
    n_mdl = mesh.shape["mdl"]

    def body(*args):
        return per_device(n_seq, n_mdl, *args)

    return jax.shard_map(
        body, mesh=mesh, in_specs=in_specs, out_specs=out_specs, check_vma=False
    )
```

```python
import jax
import jax.numpy as jnp
from jax import lax
from jax.sharding import PartitionSpec as P

HDIM = 128
BLK = 256


def power_two(exponent):
    result = jnp.zeros(exponent.shape, jnp.float32)
    for exponent_value in range(-16, 0):
        result = result + jnp.where(exponent == exponent_value, 2.0**exponent_value, 0.0)
    return result


def fake_quant(matrix, exponent):
    scale = power_two(exponent)
    levels = jnp.clip(jnp.floor(matrix.astype(jnp.float32) / scale + 0.5), -127.0, 127.0)
    return (levels * scale).astype(jnp.bfloat16)


def per_device(
    n_seq,
    n_mdl,
    query_proj,
    key_proj,
    value_proj,
    gate_proj,
    log_decay,
    act_exponent,
    norm_gain,
    out_weight,
    weight_exponent,
):
    weights = fake_quant(out_weight, weight_exponent[None, :])
    tok_rows = query_proj.shape[0]
    feat_here = query_proj.shape[1]
    heads_here = log_decay.shape[0]
    nblocks = tok_rows // BLK
    queries = fake_quant(query_proj, act_exponent[0][None, :])
    keys_quant = fake_quant(key_proj, act_exponent[1][None, :])
    values = fake_quant(value_proj, act_exponent[2][None, :]).reshape(
        nblocks, BLK, heads_here, HDIM
    )
    query_feat = (
        jax.nn.silu(queries.astype(jnp.float32))
        .astype(jnp.bfloat16)
        .reshape(nblocks, BLK, heads_here, HDIM)
    )
    key_feat = (
        jax.nn.silu(keys_quant.astype(jnp.float32))
        .astype(jnp.bfloat16)
        .reshape(nblocks, BLK, heads_here, HDIM)
    )
    decay_cum = jnp.cumsum(log_decay.reshape(heads_here, nblocks, BLK), axis=2)
    block_total = decay_cum[:, :, -1]
    scores = jnp.einsum("bihd,bjhd->hbij", query_feat, key_feat, preferred_element_type=jnp.float32)
    decay_gap = decay_cum[:, :, :, None] - decay_cum[:, :, None, :]
    causal_mask = jnp.arange(BLK)[:, None] >= jnp.arange(BLK)[None, :]
    decay_mask = jnp.where(causal_mask, jnp.exp(jnp.minimum(decay_gap, 0.0)), 0.0)
    block_probs = (scores * decay_mask).astype(jnp.bfloat16)
    within_block = jnp.einsum(
        "hbij,bjhd->bihd", block_probs, values, preferred_element_type=jnp.float32
    )
    tail_decay = jnp.transpose(jnp.exp(block_total[:, :, None] - decay_cum), (1, 2, 0))
    weighted = (key_feat.astype(jnp.float32) * tail_decay[..., None]).astype(jnp.bfloat16)
    block_states = jnp.einsum(
        "bjhd,bjhe->bhde", weighted, values, preferred_element_type=jnp.float32
    )
    block_gain = jnp.exp(block_total).T

    def advance(carried, inputs):
        gain_here, state_here = inputs
        return (gain_here[:, None, None] * carried + state_here, carried)

    local_end, entry_local = lax.scan(
        advance, jnp.zeros((heads_here, HDIM, HDIM), jnp.float32), (block_gain, block_states)
    )
    device_log = jnp.sum(block_total, axis=1)
    log_hi = device_log.astype(jnp.bfloat16)
    log_lo = (device_log - log_hi.astype(jnp.float32)).astype(jnp.bfloat16)
    packed = jnp.concatenate(
        [
            local_end.astype(jnp.bfloat16).reshape(heads_here, HDIM * HDIM),
            jnp.broadcast_to(log_hi[:, None], (heads_here, HDIM)),
            jnp.broadcast_to(log_lo[:, None], (heads_here, HDIM)),
        ],
        axis=1,
    )
    position = lax.axis_index("seq")
    incoming = jnp.zeros((heads_here, HDIM, HDIM), jnp.float32)
    gap = jnp.zeros((heads_here,), jnp.float32)
    for d in range(1, n_seq):
        came = lax.ppermute(packed, "seq", [(z, z + d) for z in range(n_seq - d)])
        came_state = came[:, : HDIM * HDIM].astype(jnp.float32).reshape(heads_here, HDIM, HDIM)
        came_log = came[:, HDIM * HDIM].astype(jnp.float32) + came[:, HDIM * HDIM + HDIM].astype(
            jnp.float32
        )
        weight = jnp.where(d <= position, jnp.exp(jnp.minimum(gap, 0.0)), 0.0)
        incoming = incoming + weight[:, None, None] * came_state
        gap = gap + came_log
    before = jnp.cumsum(block_total, axis=1) - block_total
    entry_state = entry_local + jnp.exp(before).T[:, :, None, None] * incoming[None]
    from_state = jnp.einsum(
        "bihd,bhde->bihe",
        query_feat.astype(jnp.float32),
        entry_state,
        precision=lax.Precision.HIGHEST,
    )
    position_decay = jnp.transpose(jnp.exp(decay_cum), (1, 2, 0))[..., None]
    attended = within_block + position_decay * from_state
    mean_square = jnp.mean(attended * attended, axis=-1, keepdims=True)
    normed = (attended * lax.rsqrt(mean_square + 1e-05)).reshape(tok_rows, heads_here * HDIM)
    attn = (normed * norm_gain[None, :] * jax.nn.sigmoid(gate_proj.astype(jnp.float32))).astype(
        jnp.bfloat16
    )

    rows_w, cols_w = weights.shape
    blocks_here = feat_here // rows_w
    piece = rows_w // n_mdl
    s_me = lax.axis_index("seq")
    m_me = lax.axis_index("mdl")
    if n_seq == 4 and n_mdl == 4:
        x_me = m_me // 2
        own_pieces = attn.reshape(tok_rows, n_mdl, piece)
        keep = lax.dynamic_slice_in_dim(own_pieces, 2 * x_me, 2, axis=1)
        away = lax.dynamic_slice_in_dim(own_pieces, 2 * (1 - x_me), 2, axis=1)
        came = lax.ppermute(away, "mdl", [(mu, mu ^ 2) for mu in range(n_mdl)])
        items = jnp.transpose(jnp.concatenate([keep, came], axis=1), (1, 0, 2))
        received = []
        for k in range(n_seq):
            perm = []
            for s in range(n_seq):
                for mu in range(n_mdl):
                    r = (s + k) % n_seq
                    f = mu if r // 2 == 0 else mu ^ 2
                    perm.append((s * n_mdl + mu, f * n_mdl + 2 * (mu // 2) + r % 2))
            item = lax.dynamic_index_in_dim(items, (s_me + k) % n_seq, 0, keepdims=False)
            received.append(lax.ppermute(item, ("seq", "mdl"), perm))
        received = jnp.stack(received)
        r_me = 2 * ((s_me // 2) != (m_me // 2)).astype(jnp.int32) + m_me % 2
        x = jnp.take(received, (r_me - jnp.arange(n_seq)) % n_seq, axis=0)
    else:
        received = []
        for k in range(n_seq):
            perm = []
            for s in range(n_seq):
                for m in range(n_mdl):
                    j = (s + k) % n_seq
                    f = m * blocks_here + j // n_mdl
                    perm.append((s * n_mdl + m, f * n_mdl + j % n_mdl))
            j_send = (s_me + k) % n_seq
            chunk = lax.dynamic_slice_in_dim(attn, j_send * piece, piece, axis=1)
            received.append(lax.ppermute(chunk, ("seq", "mdl"), perm))
        received = jnp.stack(received)
        j_me = (s_me % blocks_here) * n_mdl + m_me
        x = jnp.take(received, (j_me - jnp.arange(n_seq)) % n_seq, axis=0)

    n_x = n_mdl // 2
    core = m_me % 2
    xi = m_me // 2
    d_idx = jnp.arange(n_x)[:, None]
    e_idx = jnp.arange(2)[None, :]
    mu_tab = 2 * ((xi - d_idx) % n_x) + jnp.where(e_idx == 0, core, 1 - core)
    w_perm = jnp.take(
        weights.reshape(n_mdl, piece, cols_w), mu_tab.reshape(-1), axis=0
    ).reshape(n_x, 2, piece, cols_w)
    if n_seq == 4 and n_mdl == 4:
        x = x + w_perm[0, 0, 0, 0] * jnp.bfloat16(0)
    got = [x]
    for d in range(1, n_x):
        perm = [(mu, ((mu // 2 + d) % n_x) * 2 + mu % 2) for mu in range(n_mdl)]
        got.append(lax.ppermute(x, "mdl", perm))
    own = jnp.stack(got)
    other = lax.ppermute(own, "mdl", [(mu, mu ^ 1) for mu in range(n_mdl)])
    gathered_x = jnp.stack([own, other], axis=1)

    def partial_for(target):
        rows = lax.dynamic_index_in_dim(gathered_x, target, 2, keepdims=False)
        return jnp.einsum(
            "deti,deic->tc", rows, w_perm, preferred_element_type=jnp.float32
        )

    if n_seq == 4:
        def bf(v):
            return v.astype(jnp.bfloat16)

        near_r = lax.ppermute(
            bf(partial_for(jnp.clip(s_me + 2, 0, 3))), "seq", [(0, 1), (1, 2)]
        )
        far_r = lax.ppermute(bf(partial_for(jnp.int32(3))), "seq", [(0, 3)])
        near_l = lax.ppermute(
            bf(partial_for(jnp.clip(s_me - 2, 0, 3))), "seq", [(3, 2), (2, 1)]
        )
        far_l = lax.ppermute(bf(partial_for(jnp.int32(0))), "seq", [(3, 0)])
        own_part = partial_for(s_me)
        last_r = lax.ppermute(
            bf(
                partial_for(jnp.clip(s_me + 1, 0, 3))
                + near_r.astype(jnp.float32)
                + own_part * 0.0
            ),
            "seq",
            [(0, 1), (1, 2), (2, 3)],
        )
        last_l = lax.ppermute(
            bf(partial_for(jnp.clip(s_me - 1, 0, 3)) + near_l.astype(jnp.float32)),
            "seq",
            [(3, 2), (2, 1), (1, 0)],
        )
        total = own_part
        for came in (last_r, far_r, last_l, far_l):
            total = total + came.astype(jnp.float32)
        return total.astype(jnp.bfloat16)

    halves = 2 if cols_w % 256 == 0 else 1
    width = cols_w // halves
    recv_r = [None] * halves
    recv_l = [None] * halves
    for i in range(1, n_seq):
        t_r = jnp.clip(s_me + n_seq - i, 0, n_seq - 1)
        t_l = jnp.clip(s_me - n_seq + i, 0, n_seq - 1)
        part_r = partial_for(t_r)
        part_l = partial_for(t_l)
        for h in range(halves):
            send_r = part_r[:, h * width : (h + 1) * width]
            send_l = part_l[:, h * width : (h + 1) * width]
            if recv_r[h] is not None:
                send_r = send_r + recv_r[h].astype(jnp.float32)
                send_l = send_l + recv_l[h].astype(jnp.float32)
            recv_r[h] = lax.ppermute(
                send_r.astype(jnp.bfloat16), "seq", [(z, z + 1) for z in range(i)]
            )
            recv_l[h] = lax.ppermute(
                send_l.astype(jnp.bfloat16), "seq", [(z, z - 1) for z in range(n_seq - i, n_seq)]
            )
    total = partial_for(s_me)
    if recv_r[0] is not None:
        total = total + jnp.concatenate(
            [recv_r[h].astype(jnp.float32) + recv_l[h].astype(jnp.float32) for h in range(halves)],
            axis=1,
        )
    return total.astype(jnp.bfloat16)


def solution(mesh):
    in_specs = (
        P(("grp", "seq"), "mdl"),
        P(("grp", "seq"), "mdl"),
        P(("grp", "seq"), "mdl"),
        P(("grp", "seq"), "mdl"),
        P("mdl", ("grp", "seq")),
        P(None, "mdl"),
        P("mdl"),
        P("seq", "mdl"),
        P("mdl"),
    )
    out_specs = P(("grp", "seq"), "mdl")
    n_seq = mesh.shape["seq"]
    n_mdl = mesh.shape["mdl"]

    def body(*args):
        return per_device(n_seq, n_mdl, *args)

    return jax.shard_map(
        body, mesh=mesh, in_specs=in_specs, out_specs=out_specs, check_vma=False
    )
```

```python
import jax
import jax.numpy as jnp
from jax import lax
from jax.sharding import PartitionSpec as P

HDIM = 128
BLK = 256


def power_two(exponent):
    result = jnp.zeros(exponent.shape, jnp.float32)
    for exponent_value in range(-16, 0):
        result = result + jnp.where(exponent == exponent_value, 2.0**exponent_value, 0.0)
    return result


def fake_quant(matrix, exponent):
    scale = power_two(exponent)
    levels = jnp.clip(jnp.floor(matrix.astype(jnp.float32) / scale + 0.5), -127.0, 127.0)
    return (levels * scale).astype(jnp.bfloat16)


def per_device(
    n_seq,
    n_mdl,
    query_proj,
    key_proj,
    value_proj,
    gate_proj,
    log_decay,
    act_exponent,
    norm_gain,
    out_weight,
    weight_exponent,
):
    weights = fake_quant(out_weight, weight_exponent[None, :])
    tok_rows = query_proj.shape[0]
    feat_here = query_proj.shape[1]
    heads_here = log_decay.shape[0]
    nblocks = tok_rows // BLK
    queries = fake_quant(query_proj, act_exponent[0][None, :])
    keys_quant = fake_quant(key_proj, act_exponent[1][None, :])
    values = fake_quant(value_proj, act_exponent[2][None, :]).reshape(
        nblocks, BLK, heads_here, HDIM
    )
    query_feat = (
        jax.nn.silu(queries.astype(jnp.float32))
        .astype(jnp.bfloat16)
        .reshape(nblocks, BLK, heads_here, HDIM)
    )
    key_feat = (
        jax.nn.silu(keys_quant.astype(jnp.float32))
        .astype(jnp.bfloat16)
        .reshape(nblocks, BLK, heads_here, HDIM)
    )
    decay_cum = jnp.cumsum(log_decay.reshape(heads_here, nblocks, BLK), axis=2)
    block_total = decay_cum[:, :, -1]
    scores = jnp.einsum("bihd,bjhd->hbij", query_feat, key_feat, preferred_element_type=jnp.float32)
    decay_gap = decay_cum[:, :, :, None] - decay_cum[:, :, None, :]
    causal_mask = jnp.arange(BLK)[:, None] >= jnp.arange(BLK)[None, :]
    decay_mask = jnp.where(causal_mask, jnp.exp(jnp.minimum(decay_gap, 0.0)), 0.0)
    block_probs = (scores * decay_mask).astype(jnp.bfloat16)
    within_block = jnp.einsum(
        "hbij,bjhd->bihd", block_probs, values, preferred_element_type=jnp.float32
    )
    tail_decay = jnp.transpose(jnp.exp(block_total[:, :, None] - decay_cum), (1, 2, 0))
    weighted = (key_feat.astype(jnp.float32) * tail_decay[..., None]).astype(jnp.bfloat16)
    block_states = jnp.einsum(
        "bjhd,bjhe->bhde", weighted, values, preferred_element_type=jnp.float32
    )
    block_gain = jnp.exp(block_total).T

    def advance(carried, inputs):
        gain_here, state_here = inputs
        return (gain_here[:, None, None] * carried + state_here, carried)

    local_end, entry_local = lax.scan(
        advance, jnp.zeros((heads_here, HDIM, HDIM), jnp.float32), (block_gain, block_states)
    )
    device_log = jnp.sum(block_total, axis=1)
    log_hi = device_log.astype(jnp.bfloat16)
    log_lo = (device_log - log_hi.astype(jnp.float32)).astype(jnp.bfloat16)
    packed = jnp.concatenate(
        [
            local_end.astype(jnp.bfloat16).reshape(heads_here, HDIM * HDIM),
            jnp.broadcast_to(log_hi[:, None], (heads_here, HDIM)),
            jnp.broadcast_to(log_lo[:, None], (heads_here, HDIM)),
        ],
        axis=1,
    )
    position = lax.axis_index("seq")
    incoming = jnp.zeros((heads_here, HDIM, HDIM), jnp.float32)
    gap = jnp.zeros((heads_here,), jnp.float32)
    for d in range(1, n_seq):
        came = lax.ppermute(packed, "seq", [(z, z + d) for z in range(n_seq - d)])
        came_state = came[:, : HDIM * HDIM].astype(jnp.float32).reshape(heads_here, HDIM, HDIM)
        came_log = came[:, HDIM * HDIM].astype(jnp.float32) + came[:, HDIM * HDIM + HDIM].astype(
            jnp.float32
        )
        weight = jnp.where(d <= position, jnp.exp(jnp.minimum(gap, 0.0)), 0.0)
        incoming = incoming + weight[:, None, None] * came_state
        gap = gap + came_log
    before = jnp.cumsum(block_total, axis=1) - block_total
    entry_state = entry_local + jnp.exp(before).T[:, :, None, None] * incoming[None]
    from_state = jnp.einsum(
        "bihd,bhde->bihe",
        query_feat.astype(jnp.float32),
        entry_state,
        precision=lax.Precision.HIGHEST,
    )
    position_decay = jnp.transpose(jnp.exp(decay_cum), (1, 2, 0))[..., None]
    attended = within_block + position_decay * from_state
    mean_square = jnp.mean(attended * attended, axis=-1, keepdims=True)
    normed = (attended * lax.rsqrt(mean_square + 1e-05)).reshape(tok_rows, heads_here * HDIM)
    attn = (normed * norm_gain[None, :] * jax.nn.sigmoid(gate_proj.astype(jnp.float32))).astype(
        jnp.bfloat16
    )

    rows_w, cols_w = weights.shape
    blocks_here = feat_here // rows_w
    piece = rows_w // n_mdl
    s_me = lax.axis_index("seq")
    m_me = lax.axis_index("mdl")
    if n_seq == 4 and n_mdl == 4:
        x_me = m_me // 2
        own_pieces = attn.reshape(tok_rows, n_mdl, piece)
        keep = lax.dynamic_slice_in_dim(own_pieces, 2 * x_me, 2, axis=1)
        away = lax.dynamic_slice_in_dim(own_pieces, 2 * (1 - x_me), 2, axis=1)
        came = lax.ppermute(away, "mdl", [(mu, mu ^ 2) for mu in range(n_mdl)])
        items = jnp.transpose(jnp.concatenate([keep, came], axis=1), (1, 0, 2))
        received = []
        for k in range(n_seq):
            perm = []
            for s in range(n_seq):
                for mu in range(n_mdl):
                    r = (s + k) % n_seq
                    f = mu if r // 2 == 0 else mu ^ 2
                    perm.append((s * n_mdl + mu, f * n_mdl + 2 * (mu // 2) + r % 2))
            item = lax.dynamic_index_in_dim(items, (s_me + k) % n_seq, 0, keepdims=False)
            received.append(lax.ppermute(item, ("seq", "mdl"), perm))
        received = jnp.stack(received)
        r_me = 2 * ((s_me // 2) != (m_me // 2)).astype(jnp.int32) + m_me % 2
        x = jnp.take(received, (r_me - jnp.arange(n_seq)) % n_seq, axis=0)
    else:
        received = []
        for k in range(n_seq):
            perm = []
            for s in range(n_seq):
                for m in range(n_mdl):
                    j = (s + k) % n_seq
                    f = m * blocks_here + j // n_mdl
                    perm.append((s * n_mdl + m, f * n_mdl + j % n_mdl))
            j_send = (s_me + k) % n_seq
            chunk = lax.dynamic_slice_in_dim(attn, j_send * piece, piece, axis=1)
            received.append(lax.ppermute(chunk, ("seq", "mdl"), perm))
        received = jnp.stack(received)
        j_me = (s_me % blocks_here) * n_mdl + m_me
        x = jnp.take(received, (j_me - jnp.arange(n_seq)) % n_seq, axis=0)

    n_x = n_mdl // 2
    core = m_me % 2
    xi = m_me // 2
    got = [x]
    for d in range(1, n_x):
        perm = [(mu, ((mu // 2 + d) % n_x) * 2 + mu % 2) for mu in range(n_mdl)]
        got.append(lax.ppermute(x, "mdl", perm))
    own = jnp.stack(got)
    other = lax.ppermute(own, "mdl", [(mu, mu ^ 1) for mu in range(n_mdl)])
    gathered_x = jnp.stack([own, other], axis=1)
    d_idx = jnp.arange(n_x)[:, None]
    e_idx = jnp.arange(2)[None, :]
    mu_tab = 2 * ((xi - d_idx) % n_x) + jnp.where(e_idx == 0, core, 1 - core)
    w_perm = jnp.take(
        weights.reshape(n_mdl, piece, cols_w), mu_tab.reshape(-1), axis=0
    ).reshape(n_x, 2, piece, cols_w)

    def partial_for(target):
        rows = lax.dynamic_index_in_dim(gathered_x, target, 2, keepdims=False)
        return jnp.einsum(
            "deti,deic->tc", rows, w_perm, preferred_element_type=jnp.float32
        )

    if n_seq == 4:
        def bf(v):
            return v.astype(jnp.bfloat16)

        near_r = lax.ppermute(
            bf(partial_for(jnp.clip(s_me + 2, 0, 3))), "seq", [(0, 1), (1, 2)]
        )
        near_l = lax.ppermute(
            bf(partial_for(jnp.clip(s_me - 2, 0, 3))), "seq", [(3, 2), (2, 1)]
        )
        far_r = lax.ppermute(bf(partial_for(jnp.int32(3))), "seq", [(0, 3)])
        far_l = lax.ppermute(bf(partial_for(jnp.int32(0))), "seq", [(3, 0)])
        own_part = partial_for(s_me)
        last_r = lax.ppermute(
            bf(
                partial_for(jnp.clip(s_me + 1, 0, 3))
                + near_r.astype(jnp.float32)
                + own_part * 0.0
            ),
            "seq",
            [(0, 1), (1, 2), (2, 3)],
        )
        last_l = lax.ppermute(
            bf(partial_for(jnp.clip(s_me - 1, 0, 3)) + near_l.astype(jnp.float32)),
            "seq",
            [(3, 2), (2, 1), (1, 0)],
        )
        total = own_part
        for came in (last_r, far_r, last_l, far_l):
            total = total + came.astype(jnp.float32)
        return total.astype(jnp.bfloat16)

    halves = 2 if cols_w % 256 == 0 else 1
    width = cols_w // halves
    recv_r = [None] * halves
    recv_l = [None] * halves
    for i in range(1, n_seq):
        t_r = jnp.clip(s_me + n_seq - i, 0, n_seq - 1)
        t_l = jnp.clip(s_me - n_seq + i, 0, n_seq - 1)
        part_r = partial_for(t_r)
        part_l = partial_for(t_l)
        for h in range(halves):
            send_r = part_r[:, h * width : (h + 1) * width]
            send_l = part_l[:, h * width : (h + 1) * width]
            if recv_r[h] is not None:
                send_r = send_r + recv_r[h].astype(jnp.float32)
                send_l = send_l + recv_l[h].astype(jnp.float32)
            recv_r[h] = lax.ppermute(
                send_r.astype(jnp.bfloat16), "seq", [(z, z + 1) for z in range(i)]
            )
            recv_l[h] = lax.ppermute(
                send_l.astype(jnp.bfloat16), "seq", [(z, z - 1) for z in range(n_seq - i, n_seq)]
            )
    total = partial_for(s_me)
    if recv_r[0] is not None:
        total = total + jnp.concatenate(
            [recv_r[h].astype(jnp.float32) + recv_l[h].astype(jnp.float32) for h in range(halves)],
            axis=1,
        )
    return total.astype(jnp.bfloat16)


def solution(mesh):
    in_specs = (
        P(("grp", "seq"), "mdl"),
        P(("grp", "seq"), "mdl"),
        P(("grp", "seq"), "mdl"),
        P(("grp", "seq"), "mdl"),
        P("mdl", ("grp", "seq")),
        P(None, "mdl"),
        P("mdl"),
        P("seq", "mdl"),
        P("mdl"),
    )
    out_specs = P(("grp", "seq"), "mdl")
    n_seq = mesh.shape["seq"]
    n_mdl = mesh.shape["mdl"]

    def body(*args):
        return per_device(n_seq, n_mdl, *args)

    return jax.shard_map(
        body, mesh=mesh, in_specs=in_specs, out_specs=out_specs, check_vma=False
    )
```

```python
import jax
import jax.numpy as jnp
from jax import lax
from jax.sharding import PartitionSpec as P

HDIM = 128
BLK = 256


def power_two(exponent):
    result = jnp.zeros(exponent.shape, jnp.float32)
    for exponent_value in range(-16, 0):
        result = result + jnp.where(exponent == exponent_value, 2.0**exponent_value, 0.0)
    return result


def fake_quant(matrix, exponent):
    scale = power_two(exponent)
    levels = jnp.clip(jnp.floor(matrix.astype(jnp.float32) / scale + 0.5), -127.0, 127.0)
    return (levels * scale).astype(jnp.bfloat16)


def per_device(
    n_seq,
    n_mdl,
    query_proj,
    key_proj,
    value_proj,
    gate_proj,
    log_decay,
    act_exponent,
    norm_gain,
    out_weight,
    weight_exponent,
):
    tok_rows = query_proj.shape[0]
    feat_here = query_proj.shape[1]
    heads_here = log_decay.shape[0]
    nblocks = tok_rows // BLK
    queries = fake_quant(query_proj, act_exponent[0][None, :])
    keys_quant = fake_quant(key_proj, act_exponent[1][None, :])
    values = fake_quant(value_proj, act_exponent[2][None, :]).reshape(
        nblocks, BLK, heads_here, HDIM
    )
    query_feat = (
        jax.nn.silu(queries.astype(jnp.float32))
        .astype(jnp.bfloat16)
        .reshape(nblocks, BLK, heads_here, HDIM)
    )
    key_feat = (
        jax.nn.silu(keys_quant.astype(jnp.float32))
        .astype(jnp.bfloat16)
        .reshape(nblocks, BLK, heads_here, HDIM)
    )
    decay_cum = jnp.cumsum(log_decay.reshape(heads_here, nblocks, BLK), axis=2)
    block_total = decay_cum[:, :, -1]
    scores = jnp.einsum("bihd,bjhd->hbij", query_feat, key_feat, preferred_element_type=jnp.float32)
    decay_gap = decay_cum[:, :, :, None] - decay_cum[:, :, None, :]
    causal_mask = jnp.arange(BLK)[:, None] >= jnp.arange(BLK)[None, :]
    decay_mask = jnp.where(causal_mask, jnp.exp(jnp.minimum(decay_gap, 0.0)), 0.0)
    block_probs = (scores * decay_mask).astype(jnp.bfloat16)
    within_block = jnp.einsum(
        "hbij,bjhd->bihd", block_probs, values, preferred_element_type=jnp.float32
    )
    tail_decay = jnp.transpose(jnp.exp(block_total[:, :, None] - decay_cum), (1, 2, 0))
    weighted = (key_feat.astype(jnp.float32) * tail_decay[..., None]).astype(jnp.bfloat16)
    block_states = jnp.einsum(
        "bjhd,bjhe->bhde", weighted, values, preferred_element_type=jnp.float32
    )
    block_gain = jnp.exp(block_total).T

    def advance(carried, inputs):
        gain_here, state_here = inputs
        return (gain_here[:, None, None] * carried + state_here, carried)

    local_end, entry_local = lax.scan(
        advance, jnp.zeros((heads_here, HDIM, HDIM), jnp.float32), (block_gain, block_states)
    )
    device_log = jnp.sum(block_total, axis=1)
    log_hi = device_log.astype(jnp.bfloat16)
    log_lo = (device_log - log_hi.astype(jnp.float32)).astype(jnp.bfloat16)
    packed = jnp.concatenate(
        [
            local_end.astype(jnp.bfloat16).reshape(heads_here, HDIM * HDIM),
            jnp.broadcast_to(log_hi[:, None], (heads_here, HDIM)),
            jnp.broadcast_to(log_lo[:, None], (heads_here, HDIM)),
        ],
        axis=1,
    )
    weights = fake_quant(out_weight, weight_exponent[None, :])
    n_x = n_mdl // 2
    m_me = lax.axis_index("mdl")
    core = m_me % 2
    xi = m_me // 2
    piece = weights.shape[0] // n_mdl
    d_idx = jnp.arange(n_x)[:, None]
    e_idx = jnp.arange(2)[None, :]
    mu_tab = 2 * ((xi - d_idx) % n_x) + jnp.where(e_idx == 0, core, 1 - core)
    w_perm = jnp.take(
        weights.reshape(n_mdl, piece, weights.shape[1]), mu_tab.reshape(-1), axis=0
    ).reshape(n_x, 2, piece, weights.shape[1])
    position = lax.axis_index("seq")
    incoming = jnp.zeros((heads_here, HDIM, HDIM), jnp.float32)
    gap = jnp.zeros((heads_here,), jnp.float32)
    for d in range(1, n_seq):
        came = lax.ppermute(packed, "seq", [(z, z + d) for z in range(n_seq - d)])
        came_state = came[:, : HDIM * HDIM].astype(jnp.float32).reshape(heads_here, HDIM, HDIM)
        came_log = came[:, HDIM * HDIM].astype(jnp.float32) + came[:, HDIM * HDIM + HDIM].astype(
            jnp.float32
        )
        weight = jnp.where(d <= position, jnp.exp(jnp.minimum(gap, 0.0)), 0.0)
        incoming = incoming + weight[:, None, None] * came_state
        if d == 1:
            incoming = incoming + w_perm[0, 0, 0, 0].astype(jnp.float32) * 0.0
        gap = gap + came_log
    before = jnp.cumsum(block_total, axis=1) - block_total
    entry_state = entry_local + jnp.exp(before).T[:, :, None, None] * incoming[None]
    from_state = jnp.einsum(
        "bihd,bhde->bihe",
        query_feat.astype(jnp.float32),
        entry_state,
        precision=lax.Precision.HIGHEST,
    )
    position_decay = jnp.transpose(jnp.exp(decay_cum), (1, 2, 0))[..., None]
    attended = within_block + position_decay * from_state
    mean_square = jnp.mean(attended * attended, axis=-1, keepdims=True)
    normed = (attended * lax.rsqrt(mean_square + 1e-05)).reshape(tok_rows, heads_here * HDIM)
    attn = (normed * norm_gain[None, :] * jax.nn.sigmoid(gate_proj.astype(jnp.float32))).astype(
        jnp.bfloat16
    )

    rows_w, cols_w = weights.shape
    blocks_here = feat_here // rows_w
    piece = rows_w // n_mdl
    s_me = lax.axis_index("seq")
    m_me = lax.axis_index("mdl")
    if n_seq == 4 and n_mdl == 4:
        x_me = m_me // 2
        own_pieces = attn.reshape(tok_rows, n_mdl, piece)
        keep = lax.dynamic_slice_in_dim(own_pieces, 2 * x_me, 2, axis=1)
        away = lax.dynamic_slice_in_dim(own_pieces, 2 * (1 - x_me), 2, axis=1)
        came = lax.ppermute(away, "mdl", [(mu, mu ^ 2) for mu in range(n_mdl)])
        items = jnp.transpose(jnp.concatenate([keep, came], axis=1), (1, 0, 2))
        received = []
        for k in range(n_seq):
            perm = []
            for s in range(n_seq):
                for mu in range(n_mdl):
                    r = (s + k) % n_seq
                    f = mu if r // 2 == 0 else mu ^ 2
                    perm.append((s * n_mdl + mu, f * n_mdl + 2 * (mu // 2) + r % 2))
            item = lax.dynamic_index_in_dim(items, (s_me + k) % n_seq, 0, keepdims=False)
            received.append(lax.ppermute(item, ("seq", "mdl"), perm))
        received = jnp.stack(received)
        r_me = 2 * ((s_me // 2) != (m_me // 2)).astype(jnp.int32) + m_me % 2
        x = jnp.take(received, (r_me - jnp.arange(n_seq)) % n_seq, axis=0)
    else:
        received = []
        for k in range(n_seq):
            perm = []
            for s in range(n_seq):
                for m in range(n_mdl):
                    j = (s + k) % n_seq
                    f = m * blocks_here + j // n_mdl
                    perm.append((s * n_mdl + m, f * n_mdl + j % n_mdl))
            j_send = (s_me + k) % n_seq
            chunk = lax.dynamic_slice_in_dim(attn, j_send * piece, piece, axis=1)
            received.append(lax.ppermute(chunk, ("seq", "mdl"), perm))
        received = jnp.stack(received)
        j_me = (s_me % blocks_here) * n_mdl + m_me
        x = jnp.take(received, (j_me - jnp.arange(n_seq)) % n_seq, axis=0)

    n_x = n_mdl // 2
    core = m_me % 2
    xi = m_me // 2
    got = [x]
    for d in range(1, n_x):
        perm = [(mu, ((mu // 2 + d) % n_x) * 2 + mu % 2) for mu in range(n_mdl)]
        got.append(lax.ppermute(x, "mdl", perm))
    own = jnp.stack(got)
    other = lax.ppermute(own, "mdl", [(mu, mu ^ 1) for mu in range(n_mdl)])
    gathered_x = jnp.stack([own, other], axis=1)

    def partial_for(target):
        rows = lax.dynamic_index_in_dim(gathered_x, target, 2, keepdims=False)
        return jnp.einsum(
            "deti,deic->tc", rows, w_perm, preferred_element_type=jnp.float32
        )

    if n_seq == 4:
        def bf(v):
            return v.astype(jnp.bfloat16)

        near_r = lax.ppermute(
            bf(partial_for(jnp.clip(s_me + 2, 0, 3))), "seq", [(0, 1), (1, 2)]
        )
        far_r = lax.ppermute(bf(partial_for(jnp.int32(3))), "seq", [(0, 3)])
        near_l = lax.ppermute(
            bf(partial_for(jnp.clip(s_me - 2, 0, 3))), "seq", [(3, 2), (2, 1)]
        )
        far_l = lax.ppermute(bf(partial_for(jnp.int32(0))), "seq", [(3, 0)])
        own_part = partial_for(s_me)
        last_r = lax.ppermute(
            bf(
                partial_for(jnp.clip(s_me + 1, 0, 3))
                + near_r.astype(jnp.float32)
                + own_part * 0.0
            ),
            "seq",
            [(0, 1), (1, 2), (2, 3)],
        )
        last_l = lax.ppermute(
            bf(partial_for(jnp.clip(s_me - 1, 0, 3)) + near_l.astype(jnp.float32)),
            "seq",
            [(3, 2), (2, 1), (1, 0)],
        )
        total = own_part
        for came in (last_r, far_r, last_l, far_l):
            total = total + came.astype(jnp.float32)
        return total.astype(jnp.bfloat16)

    halves = 2 if cols_w % 256 == 0 else 1
    width = cols_w // halves
    recv_r = [None] * halves
    recv_l = [None] * halves
    for i in range(1, n_seq):
        t_r = jnp.clip(s_me + n_seq - i, 0, n_seq - 1)
        t_l = jnp.clip(s_me - n_seq + i, 0, n_seq - 1)
        part_r = partial_for(t_r)
        part_l = partial_for(t_l)
        for h in range(halves):
            send_r = part_r[:, h * width : (h + 1) * width]
            send_l = part_l[:, h * width : (h + 1) * width]
            if recv_r[h] is not None:
                send_r = send_r + recv_r[h].astype(jnp.float32)
                send_l = send_l + recv_l[h].astype(jnp.float32)
            recv_r[h] = lax.ppermute(
                send_r.astype(jnp.bfloat16), "seq", [(z, z + 1) for z in range(i)]
            )
            recv_l[h] = lax.ppermute(
                send_l.astype(jnp.bfloat16), "seq", [(z, z - 1) for z in range(n_seq - i, n_seq)]
            )
    total = partial_for(s_me)
    if recv_r[0] is not None:
        total = total + jnp.concatenate(
            [recv_r[h].astype(jnp.float32) + recv_l[h].astype(jnp.float32) for h in range(halves)],
            axis=1,
        )
    return total.astype(jnp.bfloat16)


def solution(mesh):
    in_specs = (
        P(("grp", "seq"), "mdl"),
        P(("grp", "seq"), "mdl"),
        P(("grp", "seq"), "mdl"),
        P(("grp", "seq"), "mdl"),
        P("mdl", ("grp", "seq")),
        P(None, "mdl"),
        P("mdl"),
        P("seq", "mdl"),
        P("mdl"),
    )
    out_specs = P(("grp", "seq"), "mdl")
    n_seq = mesh.shape["seq"]
    n_mdl = mesh.shape["mdl"]

    def body(*args):
        return per_device(n_seq, n_mdl, *args)

    return jax.shard_map(
        body, mesh=mesh, in_specs=in_specs, out_specs=out_specs, check_vma=False
    )
```

```python
import jax
import jax.numpy as jnp
from jax import lax
from jax.sharding import PartitionSpec as P

HDIM = 128
BLK = 256


def power_two(exponent):
    result = jnp.zeros(exponent.shape, jnp.float32)
    for exponent_value in range(-16, 0):
        result = result + jnp.where(exponent == exponent_value, 2.0**exponent_value, 0.0)
    return result


def fake_quant(matrix, exponent):
    scale = power_two(exponent)
    levels = jnp.clip(jnp.floor(matrix.astype(jnp.float32) / scale + 0.5), -127.0, 127.0)
    return (levels * scale).astype(jnp.bfloat16)


def per_device(
    n_seq,
    n_mdl,
    query_proj,
    key_proj,
    value_proj,
    gate_proj,
    log_decay,
    act_exponent,
    norm_gain,
    out_weight,
    weight_exponent,
):
    tok_rows = query_proj.shape[0]
    feat_here = query_proj.shape[1]
    heads_here = log_decay.shape[0]
    nblocks = tok_rows // BLK
    queries = fake_quant(query_proj, act_exponent[0][None, :])
    keys_quant = fake_quant(key_proj, act_exponent[1][None, :])
    values = fake_quant(value_proj, act_exponent[2][None, :]).reshape(
        nblocks, BLK, heads_here, HDIM
    )
    query_feat = (
        jax.nn.silu(queries.astype(jnp.float32))
        .astype(jnp.bfloat16)
        .reshape(nblocks, BLK, heads_here, HDIM)
    )
    key_feat = (
        jax.nn.silu(keys_quant.astype(jnp.float32))
        .astype(jnp.bfloat16)
        .reshape(nblocks, BLK, heads_here, HDIM)
    )
    decay_cum = jnp.cumsum(log_decay.reshape(heads_here, nblocks, BLK), axis=2)
    block_total = decay_cum[:, :, -1]
    scores = jnp.einsum("bihd,bjhd->hbij", query_feat, key_feat, preferred_element_type=jnp.float32)
    decay_gap = decay_cum[:, :, :, None] - decay_cum[:, :, None, :]
    causal_mask = jnp.arange(BLK)[:, None] >= jnp.arange(BLK)[None, :]
    decay_mask = jnp.where(causal_mask, jnp.exp(jnp.minimum(decay_gap, 0.0)), 0.0)
    block_probs = (scores * decay_mask).astype(jnp.bfloat16)
    within_block = jnp.einsum(
        "hbij,bjhd->bihd", block_probs, values, preferred_element_type=jnp.float32
    )
    tail_decay = jnp.transpose(jnp.exp(block_total[:, :, None] - decay_cum), (1, 2, 0))
    weighted = (key_feat.astype(jnp.float32) * tail_decay[..., None]).astype(jnp.bfloat16)
    block_states = jnp.einsum(
        "bjhd,bjhe->bhde", weighted, values, preferred_element_type=jnp.float32
    )
    block_gain = jnp.exp(block_total).T

    def advance(carried, inputs):
        gain_here, state_here = inputs
        return (gain_here[:, None, None] * carried + state_here, carried)

    local_end, entry_local = lax.scan(
        advance, jnp.zeros((heads_here, HDIM, HDIM), jnp.float32), (block_gain, block_states)
    )
    device_log = jnp.sum(block_total, axis=1)
    log_hi = device_log.astype(jnp.bfloat16)
    log_lo = (device_log - log_hi.astype(jnp.float32)).astype(jnp.bfloat16)
    packed = jnp.concatenate(
        [
            local_end.astype(jnp.bfloat16).reshape(heads_here, HDIM * HDIM),
            jnp.broadcast_to(log_hi[:, None], (heads_here, HDIM)),
            jnp.broadcast_to(log_lo[:, None], (heads_here, HDIM)),
        ],
        axis=1,
    )
    weights = fake_quant(out_weight, weight_exponent[None, :])
    n_x = n_mdl // 2
    m_me = lax.axis_index("mdl")
    core = m_me % 2
    xi = m_me // 2
    piece = weights.shape[0] // n_mdl
    d_idx = jnp.arange(n_x)[:, None]
    e_idx = jnp.arange(2)[None, :]
    mu_tab = 2 * ((xi - d_idx) % n_x) + jnp.where(e_idx == 0, core, 1 - core)
    w_perm = jnp.take(
        weights.reshape(n_mdl, piece, weights.shape[1]), mu_tab.reshape(-1), axis=0
    ).reshape(n_x, 2, piece, weights.shape[1])
    position = lax.axis_index("seq")
    incoming = jnp.zeros((heads_here, HDIM * HDIM), jnp.float32)
    gap = jnp.zeros((heads_here,), jnp.float32)
    for d in range(1, n_seq):
        came = lax.ppermute(packed, "seq", [(z, z + d) for z in range(n_seq - d)])
        came_state = came[:, : HDIM * HDIM].astype(jnp.float32)
        came_log = came[:, HDIM * HDIM].astype(jnp.float32) + came[:, HDIM * HDIM + HDIM].astype(
            jnp.float32
        )
        weight = jnp.where(d <= position, jnp.exp(jnp.minimum(gap, 0.0)), 0.0)
        incoming = incoming + weight[:, None] * came_state
        if d == 1:
            incoming = incoming + w_perm[0, 0, 0, 0].astype(jnp.float32) * 0.0
        gap = gap + came_log
    incoming = incoming.reshape(heads_here, HDIM, HDIM)
    before = jnp.cumsum(block_total, axis=1) - block_total
    entry_state = entry_local + jnp.exp(before).T[:, :, None, None] * incoming[None]
    from_state = jnp.einsum(
        "bihd,bhde->bihe",
        query_feat.astype(jnp.float32),
        entry_state,
        precision=lax.Precision.HIGHEST,
    )
    position_decay = jnp.transpose(jnp.exp(decay_cum), (1, 2, 0))[..., None]
    attended = within_block + position_decay * from_state
    mean_square = jnp.mean(attended * attended, axis=-1, keepdims=True)
    normed = (attended * lax.rsqrt(mean_square + 1e-05)).reshape(tok_rows, heads_here * HDIM)
    attn = (normed * norm_gain[None, :] * jax.nn.sigmoid(gate_proj.astype(jnp.float32))).astype(
        jnp.bfloat16
    )

    rows_w, cols_w = weights.shape
    blocks_here = feat_here // rows_w
    piece = rows_w // n_mdl
    s_me = lax.axis_index("seq")
    m_me = lax.axis_index("mdl")
    if n_seq == 4 and n_mdl == 4:
        x_me = m_me // 2
        own_pieces = attn.reshape(tok_rows, n_mdl, piece)
        keep = lax.dynamic_slice_in_dim(own_pieces, 2 * x_me, 2, axis=1)
        away = lax.dynamic_slice_in_dim(own_pieces, 2 * (1 - x_me), 2, axis=1)
        came = lax.ppermute(away, "mdl", [(mu, mu ^ 2) for mu in range(n_mdl)])
        items = jnp.transpose(jnp.concatenate([keep, came], axis=1), (1, 0, 2))
        received = []
        for k in range(n_seq):
            perm = []
            for s in range(n_seq):
                for mu in range(n_mdl):
                    r = (s + k) % n_seq
                    f = mu if r // 2 == 0 else mu ^ 2
                    perm.append((s * n_mdl + mu, f * n_mdl + 2 * (mu // 2) + r % 2))
            item = lax.dynamic_index_in_dim(items, (s_me + k) % n_seq, 0, keepdims=False)
            received.append(lax.ppermute(item, ("seq", "mdl"), perm))
        received = jnp.stack(received)
        r_me = 2 * ((s_me // 2) != (m_me // 2)).astype(jnp.int32) + m_me % 2
        x = jnp.take(received, (r_me - jnp.arange(n_seq)) % n_seq, axis=0)
    else:
        received = []
        for k in range(n_seq):
            perm = []
            for s in range(n_seq):
                for m in range(n_mdl):
                    j = (s + k) % n_seq
                    f = m * blocks_here + j // n_mdl
                    perm.append((s * n_mdl + m, f * n_mdl + j % n_mdl))
            j_send = (s_me + k) % n_seq
            chunk = lax.dynamic_slice_in_dim(attn, j_send * piece, piece, axis=1)
            received.append(lax.ppermute(chunk, ("seq", "mdl"), perm))
        received = jnp.stack(received)
        j_me = (s_me % blocks_here) * n_mdl + m_me
        x = jnp.take(received, (j_me - jnp.arange(n_seq)) % n_seq, axis=0)

    n_x = n_mdl // 2
    core = m_me % 2
    xi = m_me // 2
    got = [x]
    for d in range(1, n_x):
        perm = [(mu, ((mu // 2 + d) % n_x) * 2 + mu % 2) for mu in range(n_mdl)]
        got.append(lax.ppermute(x, "mdl", perm))
    own = jnp.stack(got)
    other = lax.ppermute(own, "mdl", [(mu, mu ^ 1) for mu in range(n_mdl)])
    gathered_x = jnp.stack([own, other], axis=1)

    def partial_for(target):
        rows = lax.dynamic_index_in_dim(gathered_x, target, 2, keepdims=False)
        return jnp.einsum(
            "deti,deic->tc", rows, w_perm, preferred_element_type=jnp.float32
        )

    if n_seq == 4:
        def bf(v):
            return v.astype(jnp.bfloat16)

        near_r = lax.ppermute(
            bf(partial_for(jnp.clip(s_me + 2, 0, 3))), "seq", [(0, 1), (1, 2)]
        )
        far_r = lax.ppermute(bf(partial_for(jnp.int32(3))), "seq", [(0, 3)])
        near_l = lax.ppermute(
            bf(partial_for(jnp.clip(s_me - 2, 0, 3))), "seq", [(3, 2), (2, 1)]
        )
        far_l = lax.ppermute(bf(partial_for(jnp.int32(0))), "seq", [(3, 0)])
        own_part = partial_for(s_me)
        last_r = lax.ppermute(
            bf(
                partial_for(jnp.clip(s_me + 1, 0, 3))
                + near_r.astype(jnp.float32)
                + own_part * 0.0
            ),
            "seq",
            [(0, 1), (1, 2), (2, 3)],
        )
        last_l = lax.ppermute(
            bf(partial_for(jnp.clip(s_me - 1, 0, 3)) + near_l.astype(jnp.float32)),
            "seq",
            [(3, 2), (2, 1), (1, 0)],
        )
        total = own_part
        for came in (last_r, far_r, last_l, far_l):
            total = total + came.astype(jnp.float32)
        return total.astype(jnp.bfloat16)

    halves = 2 if cols_w % 256 == 0 else 1
    width = cols_w // halves
    recv_r = [None] * halves
    recv_l = [None] * halves
    for i in range(1, n_seq):
        t_r = jnp.clip(s_me + n_seq - i, 0, n_seq - 1)
        t_l = jnp.clip(s_me - n_seq + i, 0, n_seq - 1)
        part_r = partial_for(t_r)
        part_l = partial_for(t_l)
        for h in range(halves):
            send_r = part_r[:, h * width : (h + 1) * width]
            send_l = part_l[:, h * width : (h + 1) * width]
            if recv_r[h] is not None:
                send_r = send_r + recv_r[h].astype(jnp.float32)
                send_l = send_l + recv_l[h].astype(jnp.float32)
            recv_r[h] = lax.ppermute(
                send_r.astype(jnp.bfloat16), "seq", [(z, z + 1) for z in range(i)]
            )
            recv_l[h] = lax.ppermute(
                send_l.astype(jnp.bfloat16), "seq", [(z, z - 1) for z in range(n_seq - i, n_seq)]
            )
    total = partial_for(s_me)
    if recv_r[0] is not None:
        total = total + jnp.concatenate(
            [recv_r[h].astype(jnp.float32) + recv_l[h].astype(jnp.float32) for h in range(halves)],
            axis=1,
        )
    return total.astype(jnp.bfloat16)


def solution(mesh):
    in_specs = (
        P(("grp", "seq"), "mdl"),
        P(("grp", "seq"), "mdl"),
        P(("grp", "seq"), "mdl"),
        P(("grp", "seq"), "mdl"),
        P("mdl", ("grp", "seq")),
        P(None, "mdl"),
        P("mdl"),
        P("seq", "mdl"),
        P("mdl"),
    )
    out_specs = P(("grp", "seq"), "mdl")
    n_seq = mesh.shape["seq"]
    n_mdl = mesh.shape["mdl"]

    def body(*args):
        return per_device(n_seq, n_mdl, *args)

    return jax.shard_map(
        body, mesh=mesh, in_specs=in_specs, out_specs=out_specs, check_vma=False
    )
```

```python
import jax
import jax.numpy as jnp
from jax import lax
from jax.sharding import PartitionSpec as P

HDIM = 128
BLK = 256


def power_two(exponent):
    result = jnp.zeros(exponent.shape, jnp.float32)
    for exponent_value in range(-16, 0):
        result = result + jnp.where(exponent == exponent_value, 2.0**exponent_value, 0.0)
    return result


def fake_quant(matrix, exponent):
    scale = power_two(exponent)
    levels = jnp.clip(jnp.floor(matrix.astype(jnp.float32) / scale + 0.5), -127.0, 127.0)
    return (levels * scale).astype(jnp.bfloat16)


def per_device(
    n_seq,
    n_mdl,
    query_proj,
    key_proj,
    value_proj,
    gate_proj,
    log_decay,
    act_exponent,
    norm_gain,
    out_weight,
    weight_exponent,
):
    tok_rows = query_proj.shape[0]
    feat_here = query_proj.shape[1]
    heads_here = log_decay.shape[0]
    nblocks = tok_rows // BLK
    queries = fake_quant(query_proj, act_exponent[0][None, :])
    keys_quant = fake_quant(key_proj, act_exponent[1][None, :])
    values = fake_quant(value_proj, act_exponent[2][None, :]).reshape(
        nblocks, BLK, heads_here, HDIM
    )
    query_feat = (
        jax.nn.silu(queries.astype(jnp.float32))
        .astype(jnp.bfloat16)
        .reshape(nblocks, BLK, heads_here, HDIM)
    )
    key_feat = (
        jax.nn.silu(keys_quant.astype(jnp.float32))
        .astype(jnp.bfloat16)
        .reshape(nblocks, BLK, heads_here, HDIM)
    )
    decay_cum = jnp.cumsum(log_decay.reshape(heads_here, nblocks, BLK), axis=2)
    block_total = decay_cum[:, :, -1]
    scores = jnp.einsum("bihd,bjhd->hbij", query_feat, key_feat, preferred_element_type=jnp.float32)
    decay_gap = decay_cum[:, :, :, None] - decay_cum[:, :, None, :]
    causal_mask = jnp.arange(BLK)[:, None] >= jnp.arange(BLK)[None, :]
    decay_mask = jnp.where(causal_mask, jnp.exp(jnp.minimum(decay_gap, 0.0)), 0.0)
    block_probs = (scores * decay_mask).astype(jnp.bfloat16)
    within_block = jnp.einsum(
        "hbij,bjhd->bihd", block_probs, values, preferred_element_type=jnp.float32
    )
    tail_decay = jnp.transpose(jnp.exp(block_total[:, :, None] - decay_cum), (1, 2, 0))
    weighted = (key_feat.astype(jnp.float32) * tail_decay[..., None]).astype(jnp.bfloat16)
    block_states = jnp.einsum(
        "bjhd,bjhe->bhde", weighted, values, preferred_element_type=jnp.float32
    )
    block_gain = jnp.exp(block_total).T

    def advance(carried, inputs):
        gain_here, state_here = inputs
        return (gain_here[:, None, None] * carried + state_here, carried)

    local_end, entry_local = lax.scan(
        advance, jnp.zeros((heads_here, HDIM, HDIM), jnp.float32), (block_gain, block_states)
    )
    device_log = jnp.sum(block_total, axis=1)
    log_hi = device_log.astype(jnp.bfloat16)
    log_lo = (device_log - log_hi.astype(jnp.float32)).astype(jnp.bfloat16)
    packed = jnp.concatenate(
        [
            local_end.astype(jnp.bfloat16).reshape(heads_here, HDIM * HDIM),
            jnp.broadcast_to(log_hi[:, None], (heads_here, HDIM)),
            jnp.broadcast_to(log_lo[:, None], (heads_here, HDIM)),
        ],
        axis=1,
    )
    weights = fake_quant(out_weight, weight_exponent[None, :])
    n_x = n_mdl // 2
    m_me = lax.axis_index("mdl")
    core = m_me % 2
    xi = m_me // 2
    piece = weights.shape[0] // n_mdl
    d_idx = jnp.arange(n_x)[:, None]
    e_idx = jnp.arange(2)[None, :]
    mu_tab = 2 * ((xi - d_idx) % n_x) + jnp.where(e_idx == 0, core, 1 - core)
    w_perm = jnp.take(
        weights.reshape(n_mdl, piece, weights.shape[1]), mu_tab.reshape(-1), axis=0
    ).reshape(n_x, 2, piece, weights.shape[1])
    position = lax.axis_index("seq")
    incoming = jnp.zeros((heads_here, HDIM * HDIM), jnp.float32)
    gap = jnp.zeros((heads_here,), jnp.float32)
    for d in range(1, n_seq):
        came = lax.ppermute(packed, "seq", [(z, z + d) for z in range(n_seq - d)])
        came_state = came[:, : HDIM * HDIM].astype(jnp.float32)
        came_log = came[:, HDIM * HDIM].astype(jnp.float32) + came[:, HDIM * HDIM + HDIM].astype(
            jnp.float32
        )
        weight = jnp.where(d <= position, jnp.exp(jnp.minimum(gap, 0.0)), 0.0)
        incoming = incoming + weight[:, None] * came_state
        gap = gap + came_log
    incoming = incoming.reshape(heads_here, HDIM, HDIM)
    before = jnp.cumsum(block_total, axis=1) - block_total
    entry_state = entry_local + jnp.exp(before).T[:, :, None, None] * incoming[None]
    from_state = jnp.einsum(
        "bihd,bhde->bihe",
        query_feat.astype(jnp.float32),
        entry_state,
        precision=lax.Precision.HIGHEST,
    )
    position_decay = jnp.transpose(jnp.exp(decay_cum), (1, 2, 0))[..., None]
    attended = within_block + position_decay * from_state
    mean_square = jnp.mean(attended * attended, axis=-1, keepdims=True)
    normed = (attended * lax.rsqrt(mean_square + 1e-05)).reshape(tok_rows, heads_here * HDIM)
    attn = (normed * norm_gain[None, :] * jax.nn.sigmoid(gate_proj.astype(jnp.float32))).astype(
        jnp.bfloat16
    )

    rows_w, cols_w = weights.shape
    blocks_here = feat_here // rows_w
    piece = rows_w // n_mdl
    s_me = lax.axis_index("seq")
    m_me = lax.axis_index("mdl")
    if n_seq == 4 and n_mdl == 4:
        x_me = m_me // 2
        own_pieces = attn.reshape(tok_rows, n_mdl, piece)
        keep = lax.dynamic_slice_in_dim(own_pieces, 2 * x_me, 2, axis=1)
        away = lax.dynamic_slice_in_dim(own_pieces, 2 * (1 - x_me), 2, axis=1)
        came = lax.ppermute(away, "mdl", [(mu, mu ^ 2) for mu in range(n_mdl)])
        items = jnp.transpose(jnp.concatenate([keep, came], axis=1), (1, 0, 2))
        items = items + w_perm[0, 0, 0, 0] * jnp.bfloat16(0)
        received = []
        for k in range(n_seq):
            perm = []
            for s in range(n_seq):
                for mu in range(n_mdl):
                    r = (s + k) % n_seq
                    f = mu if r // 2 == 0 else mu ^ 2
                    perm.append((s * n_mdl + mu, f * n_mdl + 2 * (mu // 2) + r % 2))
            item = lax.dynamic_index_in_dim(items, (s_me + k) % n_seq, 0, keepdims=False)
            received.append(lax.ppermute(item, ("seq", "mdl"), perm))
        received = jnp.stack(received)
        r_me = 2 * ((s_me // 2) != (m_me // 2)).astype(jnp.int32) + m_me % 2
        x = jnp.take(received, (r_me - jnp.arange(n_seq)) % n_seq, axis=0)
    else:
        received = []
        for k in range(n_seq):
            perm = []
            for s in range(n_seq):
                for m in range(n_mdl):
                    j = (s + k) % n_seq
                    f = m * blocks_here + j // n_mdl
                    perm.append((s * n_mdl + m, f * n_mdl + j % n_mdl))
            j_send = (s_me + k) % n_seq
            chunk = lax.dynamic_slice_in_dim(attn, j_send * piece, piece, axis=1)
            received.append(lax.ppermute(chunk, ("seq", "mdl"), perm))
        received = jnp.stack(received)
        j_me = (s_me % blocks_here) * n_mdl + m_me
        x = jnp.take(received, (j_me - jnp.arange(n_seq)) % n_seq, axis=0)

    n_x = n_mdl // 2
    core = m_me % 2
    xi = m_me // 2
    got = [x]
    for d in range(1, n_x):
        perm = [(mu, ((mu // 2 + d) % n_x) * 2 + mu % 2) for mu in range(n_mdl)]
        got.append(lax.ppermute(x, "mdl", perm))
    own = jnp.stack(got)
    other = lax.ppermute(own, "mdl", [(mu, mu ^ 1) for mu in range(n_mdl)])
    gathered_x = jnp.stack([own, other], axis=1)

    def partial_for(target):
        rows = lax.dynamic_index_in_dim(gathered_x, target, 2, keepdims=False)
        return jnp.einsum(
            "deti,deic->tc", rows, w_perm, preferred_element_type=jnp.float32
        )

    if n_seq == 4:
        def bf(v):
            return v.astype(jnp.bfloat16)

        near_r = lax.ppermute(
            bf(partial_for(jnp.clip(s_me + 2, 0, 3))), "seq", [(0, 1), (1, 2)]
        )
        far_r = lax.ppermute(bf(partial_for(jnp.int32(3))), "seq", [(0, 3)])
        near_l = lax.ppermute(
            bf(partial_for(jnp.clip(s_me - 2, 0, 3))), "seq", [(3, 2), (2, 1)]
        )
        far_l = lax.ppermute(bf(partial_for(jnp.int32(0))), "seq", [(3, 0)])
        own_part = partial_for(s_me)
        last_r = lax.ppermute(
            bf(
                partial_for(jnp.clip(s_me + 1, 0, 3))
                + near_r.astype(jnp.float32)
                + own_part * 0.0
            ),
            "seq",
            [(0, 1), (1, 2), (2, 3)],
        )
        last_l = lax.ppermute(
            bf(partial_for(jnp.clip(s_me - 1, 0, 3)) + near_l.astype(jnp.float32)),
            "seq",
            [(3, 2), (2, 1), (1, 0)],
        )
        total = own_part
        for came in (last_r, far_r, last_l, far_l):
            total = total + came.astype(jnp.float32)
        return total.astype(jnp.bfloat16)

    halves = 2 if cols_w % 256 == 0 else 1
    width = cols_w // halves
    recv_r = [None] * halves
    recv_l = [None] * halves
    for i in range(1, n_seq):
        t_r = jnp.clip(s_me + n_seq - i, 0, n_seq - 1)
        t_l = jnp.clip(s_me - n_seq + i, 0, n_seq - 1)
        part_r = partial_for(t_r)
        part_l = partial_for(t_l)
        for h in range(halves):
            send_r = part_r[:, h * width : (h + 1) * width]
            send_l = part_l[:, h * width : (h + 1) * width]
            if recv_r[h] is not None:
                send_r = send_r + recv_r[h].astype(jnp.float32)
                send_l = send_l + recv_l[h].astype(jnp.float32)
            recv_r[h] = lax.ppermute(
                send_r.astype(jnp.bfloat16), "seq", [(z, z + 1) for z in range(i)]
            )
            recv_l[h] = lax.ppermute(
                send_l.astype(jnp.bfloat16), "seq", [(z, z - 1) for z in range(n_seq - i, n_seq)]
            )
    total = partial_for(s_me)
    if recv_r[0] is not None:
        total = total + jnp.concatenate(
            [recv_r[h].astype(jnp.float32) + recv_l[h].astype(jnp.float32) for h in range(halves)],
            axis=1,
        )
    return total.astype(jnp.bfloat16)


def solution(mesh):
    in_specs = (
        P(("grp", "seq"), "mdl"),
        P(("grp", "seq"), "mdl"),
        P(("grp", "seq"), "mdl"),
        P(("grp", "seq"), "mdl"),
        P("mdl", ("grp", "seq")),
        P(None, "mdl"),
        P("mdl"),
        P("seq", "mdl"),
        P("mdl"),
    )
    out_specs = P(("grp", "seq"), "mdl")
    n_seq = mesh.shape["seq"]
    n_mdl = mesh.shape["mdl"]

    def body(*args):
        return per_device(n_seq, n_mdl, *args)

    return jax.shard_map(
        body, mesh=mesh, in_specs=in_specs, out_specs=out_specs, check_vma=False
    )
```

```python
import jax
import jax.numpy as jnp
from jax import lax
from jax.sharding import PartitionSpec as P

HDIM = 128
BLK = 256


def power_two(exponent):
    result = jnp.zeros(exponent.shape, jnp.float32)
    for exponent_value in range(-16, 0):
        result = result + jnp.where(exponent == exponent_value, 2.0**exponent_value, 0.0)
    return result


def fake_quant(matrix, exponent):
    scale = power_two(exponent)
    levels = jnp.clip(jnp.floor(matrix.astype(jnp.float32) / scale + 0.5), -127.0, 127.0)
    return (levels * scale).astype(jnp.bfloat16)


def per_device(
    n_seq,
    n_mdl,
    query_proj,
    key_proj,
    value_proj,
    gate_proj,
    log_decay,
    act_exponent,
    norm_gain,
    out_weight,
    weight_exponent,
):
    tok_rows = query_proj.shape[0]
    feat_here = query_proj.shape[1]
    heads_here = log_decay.shape[0]
    nblocks = tok_rows // BLK
    queries = fake_quant(query_proj, act_exponent[0][None, :])
    keys_quant = fake_quant(key_proj, act_exponent[1][None, :])
    values = fake_quant(value_proj, act_exponent[2][None, :]).reshape(
        nblocks, BLK, heads_here, HDIM
    )
    query_feat = (
        jax.nn.silu(queries.astype(jnp.float32))
        .astype(jnp.bfloat16)
        .reshape(nblocks, BLK, heads_here, HDIM)
    )
    key_feat = (
        jax.nn.silu(keys_quant.astype(jnp.float32))
        .astype(jnp.bfloat16)
        .reshape(nblocks, BLK, heads_here, HDIM)
    )
    decay_cum = jnp.cumsum(log_decay.reshape(heads_here, nblocks, BLK), axis=2)
    block_total = decay_cum[:, :, -1]
    scores = jnp.einsum("bihd,bjhd->hbij", query_feat, key_feat, preferred_element_type=jnp.float32)
    decay_gap = decay_cum[:, :, :, None] - decay_cum[:, :, None, :]
    causal_mask = jnp.arange(BLK)[:, None] >= jnp.arange(BLK)[None, :]
    decay_mask = jnp.where(causal_mask, jnp.exp(jnp.minimum(decay_gap, 0.0)), 0.0)
    block_probs = (scores * decay_mask).astype(jnp.bfloat16)
    within_block = jnp.einsum(
        "hbij,bjhd->bihd", block_probs, values, preferred_element_type=jnp.float32
    )
    tail_decay = jnp.transpose(jnp.exp(block_total[:, :, None] - decay_cum), (1, 2, 0))
    weighted = (key_feat.astype(jnp.float32) * tail_decay[..., None]).astype(jnp.bfloat16)
    block_states = jnp.einsum(
        "bjhd,bjhe->bhde", weighted, values, preferred_element_type=jnp.float32
    )
    block_gain = jnp.exp(block_total).T

    def advance(carried, inputs):
        gain_here, state_here = inputs
        return (gain_here[:, None, None] * carried + state_here, carried)

    local_end, entry_local = lax.scan(
        advance, jnp.zeros((heads_here, HDIM, HDIM), jnp.float32), (block_gain, block_states)
    )
    device_log = jnp.sum(block_total, axis=1)
    log_hi = device_log.astype(jnp.bfloat16)
    log_lo = (device_log - log_hi.astype(jnp.float32)).astype(jnp.bfloat16)
    packed = jnp.concatenate(
        [
            local_end.astype(jnp.bfloat16).reshape(heads_here, HDIM * HDIM),
            jnp.broadcast_to(log_hi[:, None], (heads_here, HDIM)),
            jnp.broadcast_to(log_lo[:, None], (heads_here, HDIM)),
        ],
        axis=1,
    )
    weights = fake_quant(out_weight, weight_exponent[None, :])
    n_x = n_mdl // 2
    m_me = lax.axis_index("mdl")
    core = m_me % 2
    xi = m_me // 2
    piece = weights.shape[0] // n_mdl
    d_idx = jnp.arange(n_x)[:, None]
    e_idx = jnp.arange(2)[None, :]
    mu_tab = 2 * ((xi - d_idx) % n_x) + jnp.where(e_idx == 0, core, 1 - core)
    if n_seq == 4 and n_mdl == 4:
        w_perm = None
    else:
        w_perm = jnp.take(
            weights.reshape(n_mdl, piece, weights.shape[1]), mu_tab.reshape(-1), axis=0
        ).reshape(n_x, 2, piece, weights.shape[1])
    position = lax.axis_index("seq")
    incoming = jnp.zeros((heads_here, HDIM * HDIM), jnp.float32)
    gap = jnp.zeros((heads_here,), jnp.float32)
    for d in range(1, n_seq):
        came = lax.ppermute(packed, "seq", [(z, z + d) for z in range(n_seq - d)])
        came_state = came[:, : HDIM * HDIM].astype(jnp.float32)
        came_log = came[:, HDIM * HDIM].astype(jnp.float32) + came[:, HDIM * HDIM + HDIM].astype(
            jnp.float32
        )
        weight = jnp.where(d <= position, jnp.exp(jnp.minimum(gap, 0.0)), 0.0)
        incoming = incoming + weight[:, None] * came_state
        if d == 1:
            incoming = incoming + weights[0, 0].astype(jnp.float32) * 0.0
        gap = gap + came_log
    incoming = incoming.reshape(heads_here, HDIM, HDIM)
    before = jnp.cumsum(block_total, axis=1) - block_total
    entry_state = entry_local + jnp.exp(before).T[:, :, None, None] * incoming[None]
    from_state = jnp.einsum(
        "bihd,bhde->bihe",
        query_feat.astype(jnp.float32),
        entry_state,
        precision=lax.Precision.HIGHEST,
    )
    position_decay = jnp.transpose(jnp.exp(decay_cum), (1, 2, 0))[..., None]
    attended = within_block + position_decay * from_state
    mean_square = jnp.mean(attended * attended, axis=-1, keepdims=True)
    normed = (attended * lax.rsqrt(mean_square + 1e-05)).reshape(tok_rows, heads_here * HDIM)
    attn = (normed * norm_gain[None, :] * jax.nn.sigmoid(gate_proj.astype(jnp.float32))).astype(
        jnp.bfloat16
    )

    rows_w, cols_w = weights.shape
    blocks_here = feat_here // rows_w
    piece = rows_w // n_mdl
    s_me = lax.axis_index("seq")
    m_me = lax.axis_index("mdl")
    if n_seq == 4 and n_mdl == 4:
        x_me = m_me // 2
        own_pieces = attn.reshape(tok_rows, n_mdl, piece)
        keep = lax.dynamic_slice_in_dim(own_pieces, 2 * x_me, 2, axis=1)
        away = lax.dynamic_slice_in_dim(own_pieces, 2 * (1 - x_me), 2, axis=1)
        came = lax.ppermute(away, "mdl", [(mu, mu ^ 2) for mu in range(n_mdl)])
        items = jnp.transpose(jnp.concatenate([keep, came], axis=1), (1, 0, 2))
        received = []
        for k in range(n_seq):
            perm = []
            for s in range(n_seq):
                for mu in range(n_mdl):
                    r = (s + k) % n_seq
                    f = mu if r // 2 == 0 else mu ^ 2
                    perm.append((s * n_mdl + mu, f * n_mdl + 2 * (mu // 2) + r % 2))
            item = lax.dynamic_index_in_dim(items, (s_me + k) % n_seq, 0, keepdims=False)
            received.append(lax.ppermute(item, ("seq", "mdl"), perm))
        received = jnp.stack(received)
        r_me = 2 * ((s_me // 2) != (m_me // 2)).astype(jnp.int32) + m_me % 2
        x = jnp.take(received, (r_me - jnp.arange(n_seq)) % n_seq, axis=0)
    else:
        received = []
        for k in range(n_seq):
            perm = []
            for s in range(n_seq):
                for m in range(n_mdl):
                    j = (s + k) % n_seq
                    f = m * blocks_here + j // n_mdl
                    perm.append((s * n_mdl + m, f * n_mdl + j % n_mdl))
            j_send = (s_me + k) % n_seq
            chunk = lax.dynamic_slice_in_dim(attn, j_send * piece, piece, axis=1)
            received.append(lax.ppermute(chunk, ("seq", "mdl"), perm))
        received = jnp.stack(received)
        j_me = (s_me % blocks_here) * n_mdl + m_me
        x = jnp.take(received, (j_me - jnp.arange(n_seq)) % n_seq, axis=0)

    n_x = n_mdl // 2
    core = m_me % 2
    xi = m_me // 2
    got = [x]
    for d in range(1, n_x):
        perm = [(mu, ((mu // 2 + d) % n_x) * 2 + mu % 2) for mu in range(n_mdl)]
        got.append(lax.ppermute(x, "mdl", perm))
    own = jnp.stack(got)
    other = lax.ppermute(own, "mdl", [(mu, mu ^ 1) for mu in range(n_mdl)])
    gathered_x = jnp.stack([own, other], axis=1)

    def partial_for(target):
        rows = lax.dynamic_index_in_dim(gathered_x, target, 2, keepdims=False)
        if w_perm is not None:
            return jnp.einsum(
                "deti,deic->tc", rows, w_perm, preferred_element_type=jnp.float32
            )
        total = None
        for d in range(n_x):
            for e in range(2):
                mu = 2 * ((xi - d) % n_x) + (core if e == 0 else 1 - core)
                w_rows = lax.dynamic_slice_in_dim(weights, mu * piece, piece, axis=0)
                term = jnp.dot(rows[d, e], w_rows, preferred_element_type=jnp.float32)
                total = term if total is None else total + term
        return total

    if n_seq == 4:
        def bf(v):
            return v.astype(jnp.bfloat16)

        near_r = lax.ppermute(
            bf(partial_for(jnp.clip(s_me + 2, 0, 3))), "seq", [(0, 1), (1, 2)]
        )
        far_r = lax.ppermute(bf(partial_for(jnp.int32(3))), "seq", [(0, 3)])
        near_l = lax.ppermute(
            bf(partial_for(jnp.clip(s_me - 2, 0, 3))), "seq", [(3, 2), (2, 1)]
        )
        far_l = lax.ppermute(bf(partial_for(jnp.int32(0))), "seq", [(3, 0)])
        own_part = partial_for(s_me)
        last_r = lax.ppermute(
            bf(
                partial_for(jnp.clip(s_me + 1, 0, 3))
                + near_r.astype(jnp.float32)
                + own_part * 0.0
            ),
            "seq",
            [(0, 1), (1, 2), (2, 3)],
        )
        last_l = lax.ppermute(
            bf(partial_for(jnp.clip(s_me - 1, 0, 3)) + near_l.astype(jnp.float32)),
            "seq",
            [(3, 2), (2, 1), (1, 0)],
        )
        total = own_part
        for came in (last_r, far_r, last_l, far_l):
            total = total + came.astype(jnp.float32)
        return total.astype(jnp.bfloat16)

    halves = 2 if cols_w % 256 == 0 else 1
    width = cols_w // halves
    recv_r = [None] * halves
    recv_l = [None] * halves
    for i in range(1, n_seq):
        t_r = jnp.clip(s_me + n_seq - i, 0, n_seq - 1)
        t_l = jnp.clip(s_me - n_seq + i, 0, n_seq - 1)
        part_r = partial_for(t_r)
        part_l = partial_for(t_l)
        for h in range(halves):
            send_r = part_r[:, h * width : (h + 1) * width]
            send_l = part_l[:, h * width : (h + 1) * width]
            if recv_r[h] is not None:
                send_r = send_r + recv_r[h].astype(jnp.float32)
                send_l = send_l + recv_l[h].astype(jnp.float32)
            recv_r[h] = lax.ppermute(
                send_r.astype(jnp.bfloat16), "seq", [(z, z + 1) for z in range(i)]
            )
            recv_l[h] = lax.ppermute(
                send_l.astype(jnp.bfloat16), "seq", [(z, z - 1) for z in range(n_seq - i, n_seq)]
            )
    total = partial_for(s_me)
    if recv_r[0] is not None:
        total = total + jnp.concatenate(
            [recv_r[h].astype(jnp.float32) + recv_l[h].astype(jnp.float32) for h in range(halves)],
            axis=1,
        )
    return total.astype(jnp.bfloat16)


def solution(mesh):
    in_specs = (
        P(("grp", "seq"), "mdl"),
        P(("grp", "seq"), "mdl"),
        P(("grp", "seq"), "mdl"),
        P(("grp", "seq"), "mdl"),
        P("mdl", ("grp", "seq")),
        P(None, "mdl"),
        P("mdl"),
        P("seq", "mdl"),
        P("mdl"),
    )
    out_specs = P(("grp", "seq"), "mdl")
    n_seq = mesh.shape["seq"]
    n_mdl = mesh.shape["mdl"]

    def body(*args):
        return per_device(n_seq, n_mdl, *args)

    return jax.shard_map(
        body, mesh=mesh, in_specs=in_specs, out_specs=out_specs, check_vma=False
    )
```

```python
import jax
import jax.numpy as jnp
from jax import lax
from jax.sharding import PartitionSpec as P

HDIM = 128
BLK = 256


def power_two(exponent):
    result = jnp.zeros(exponent.shape, jnp.float32)
    for exponent_value in range(-16, 0):
        result = result + jnp.where(exponent == exponent_value, 2.0**exponent_value, 0.0)
    return result


def fake_quant(matrix, exponent):
    scale = power_two(exponent)
    levels = jnp.clip(jnp.floor(matrix.astype(jnp.float32) / scale + 0.5), -127.0, 127.0)
    return (levels * scale).astype(jnp.bfloat16)


def per_device(
    n_seq,
    n_mdl,
    query_proj,
    key_proj,
    value_proj,
    gate_proj,
    log_decay,
    act_exponent,
    norm_gain,
    out_weight,
    weight_exponent,
):
    tok_rows = query_proj.shape[0]
    feat_here = query_proj.shape[1]
    heads_here = log_decay.shape[0]
    nblocks = tok_rows // BLK
    queries = fake_quant(query_proj, act_exponent[0][None, :])
    keys_quant = fake_quant(key_proj, act_exponent[1][None, :])
    values = fake_quant(value_proj, act_exponent[2][None, :]).reshape(
        nblocks, BLK, heads_here, HDIM
    )
    query_feat = (
        jax.nn.silu(queries.astype(jnp.float32))
        .astype(jnp.bfloat16)
        .reshape(nblocks, BLK, heads_here, HDIM)
    )
    key_feat = (
        jax.nn.silu(keys_quant.astype(jnp.float32))
        .astype(jnp.bfloat16)
        .reshape(nblocks, BLK, heads_here, HDIM)
    )
    decay_cum = jnp.cumsum(log_decay.reshape(heads_here, nblocks, BLK), axis=2)
    block_total = decay_cum[:, :, -1]
    scores = jnp.einsum("bihd,bjhd->hbij", query_feat, key_feat, preferred_element_type=jnp.float32)
    decay_gap = decay_cum[:, :, :, None] - decay_cum[:, :, None, :]
    causal_mask = jnp.arange(BLK)[:, None] >= jnp.arange(BLK)[None, :]
    decay_mask = jnp.where(causal_mask, jnp.exp(jnp.minimum(decay_gap, 0.0)), 0.0)
    block_probs = (scores * decay_mask).astype(jnp.bfloat16)
    within_block = jnp.einsum(
        "hbij,bjhd->bihd", block_probs, values, preferred_element_type=jnp.float32
    )
    tail_decay = jnp.transpose(jnp.exp(block_total[:, :, None] - decay_cum), (1, 2, 0))
    weighted = (key_feat.astype(jnp.float32) * tail_decay[..., None]).astype(jnp.bfloat16)
    block_states = jnp.einsum(
        "bjhd,bjhe->bhde", weighted, values, preferred_element_type=jnp.float32
    )
    block_gain = jnp.exp(block_total).T

    def advance(carried, inputs):
        gain_here, state_here = inputs
        return (gain_here[:, None, None] * carried + state_here, carried)

    local_end, entry_local = lax.scan(
        advance, jnp.zeros((heads_here, HDIM, HDIM), jnp.float32), (block_gain, block_states)
    )
    device_log = jnp.sum(block_total, axis=1)
    log_hi = device_log.astype(jnp.bfloat16)
    log_lo = (device_log - log_hi.astype(jnp.float32)).astype(jnp.bfloat16)
    packed = jnp.concatenate(
        [
            local_end.astype(jnp.bfloat16).reshape(heads_here, HDIM * HDIM),
            jnp.broadcast_to(log_hi[:, None], (heads_here, HDIM)),
            jnp.broadcast_to(log_lo[:, None], (heads_here, HDIM)),
        ],
        axis=1,
    )
    weights = fake_quant(out_weight, weight_exponent[None, :])
    n_x = n_mdl // 2
    m_me = lax.axis_index("mdl")
    core = m_me % 2
    xi = m_me // 2
    piece = weights.shape[0] // n_mdl
    d_idx = jnp.arange(n_x)[:, None]
    e_idx = jnp.arange(2)[None, :]
    mu_tab = 2 * ((xi - d_idx) % n_x) + jnp.where(e_idx == 0, core, 1 - core)
    w_perm = jnp.take(
        weights.reshape(n_mdl, piece, weights.shape[1]), mu_tab.reshape(-1), axis=0
    ).reshape(n_x, 2, piece, weights.shape[1])
    position = lax.axis_index("seq")
    incoming = jnp.zeros((heads_here, HDIM * HDIM), jnp.float32)
    gap = jnp.zeros((heads_here,), jnp.float32)
    for d in range(1, n_seq):
        came = lax.ppermute(packed, "seq", [(z, z + d) for z in range(n_seq - d)])
        came_state = came[:, : HDIM * HDIM].astype(jnp.float32)
        came_log = came[:, HDIM * HDIM].astype(jnp.float32) + came[:, HDIM * HDIM + HDIM].astype(
            jnp.float32
        )
        weight = jnp.where(d <= position, jnp.exp(jnp.minimum(gap, 0.0)), 0.0)
        incoming = incoming + weight[:, None] * came_state
        if d == 1:
            incoming = incoming + weights[0, 0].astype(jnp.float32) * 0.0
        gap = gap + came_log
    incoming = incoming.reshape(heads_here, HDIM, HDIM)
    before = jnp.cumsum(block_total, axis=1) - block_total
    entry_state = entry_local + jnp.exp(before).T[:, :, None, None] * incoming[None]
    from_state = jnp.einsum(
        "bihd,bhde->bihe",
        query_feat.astype(jnp.float32),
        entry_state,
        precision=lax.Precision.HIGHEST,
    )
    position_decay = jnp.transpose(jnp.exp(decay_cum), (1, 2, 0))[..., None]
    attended = within_block + position_decay * from_state
    mean_square = jnp.mean(attended * attended, axis=-1, keepdims=True)
    normed = (attended * lax.rsqrt(mean_square + 1e-05)).reshape(tok_rows, heads_here * HDIM)
    attn = (normed * norm_gain[None, :] * jax.nn.sigmoid(gate_proj.astype(jnp.float32))).astype(
        jnp.bfloat16
    )

    rows_w, cols_w = weights.shape
    blocks_here = feat_here // rows_w
    piece = rows_w // n_mdl
    s_me = lax.axis_index("seq")
    m_me = lax.axis_index("mdl")
    if n_seq == 4 and n_mdl == 4:
        x_me = m_me // 2
        own_pieces = attn.reshape(tok_rows, n_mdl, piece)
        keep = lax.dynamic_slice_in_dim(own_pieces, 2 * x_me, 2, axis=1)
        away = lax.dynamic_slice_in_dim(own_pieces, 2 * (1 - x_me), 2, axis=1)
        came = lax.ppermute(away, "mdl", [(mu, mu ^ 2) for mu in range(n_mdl)])
        items = jnp.transpose(jnp.concatenate([keep, came], axis=1), (1, 0, 2))
        received = []
        for k in range(n_seq):
            perm = []
            for s in range(n_seq):
                for mu in range(n_mdl):
                    r = (s + k) % n_seq
                    f = mu if r // 2 == 0 else mu ^ 2
                    perm.append((s * n_mdl + mu, f * n_mdl + 2 * (mu // 2) + r % 2))
            item = lax.dynamic_index_in_dim(items, (s_me + k) % n_seq, 0, keepdims=False)
            received.append(lax.ppermute(item, ("seq", "mdl"), perm))
        received = jnp.stack(received)
        r_me = 2 * ((s_me // 2) != (m_me // 2)).astype(jnp.int32) + m_me % 2
        x = jnp.take(received, (r_me - jnp.arange(n_seq)) % n_seq, axis=0)
    else:
        received = []
        for k in range(n_seq):
            perm = []
            for s in range(n_seq):
                for m in range(n_mdl):
                    j = (s + k) % n_seq
                    f = m * blocks_here + j // n_mdl
                    perm.append((s * n_mdl + m, f * n_mdl + j % n_mdl))
            j_send = (s_me + k) % n_seq
            chunk = lax.dynamic_slice_in_dim(attn, j_send * piece, piece, axis=1)
            received.append(lax.ppermute(chunk, ("seq", "mdl"), perm))
        received = jnp.stack(received)
        j_me = (s_me % blocks_here) * n_mdl + m_me
        x = jnp.take(received, (j_me - jnp.arange(n_seq)) % n_seq, axis=0)

    n_x = n_mdl // 2
    core = m_me % 2
    xi = m_me // 2
    got = [x]
    for d in range(1, n_x):
        perm = [(mu, ((mu // 2 + d) % n_x) * 2 + mu % 2) for mu in range(n_mdl)]
        got.append(lax.ppermute(x, "mdl", perm))
    own = jnp.stack(got)
    other = lax.ppermute(own, "mdl", [(mu, mu ^ 1) for mu in range(n_mdl)])
    gathered_x = jnp.stack([own, other], axis=1)

    def partial_for(target):
        rows = lax.dynamic_index_in_dim(gathered_x, target, 2, keepdims=False)
        return jnp.einsum(
            "deti,deic->tc", rows, w_perm, preferred_element_type=jnp.float32
        )

    if n_seq == 4:
        def bf(v):
            return v.astype(jnp.bfloat16)

        near_r = lax.ppermute(
            bf(partial_for(jnp.clip(s_me + 2, 0, 3))), "seq", [(0, 1), (1, 2)]
        )
        far_r = lax.ppermute(bf(partial_for(jnp.int32(3))), "seq", [(0, 3)])
        near_l = lax.ppermute(
            bf(partial_for(jnp.clip(s_me - 2, 0, 3))), "seq", [(3, 2), (2, 1)]
        )
        far_l = lax.ppermute(bf(partial_for(jnp.int32(0))), "seq", [(3, 0)])
        own_part = partial_for(s_me)
        last_r = lax.ppermute(
            bf(
                partial_for(jnp.clip(s_me + 1, 0, 3))
                + near_r.astype(jnp.float32)
                + own_part * 0.0
            ),
            "seq",
            [(0, 1), (1, 2), (2, 3)],
        )
        last_l = lax.ppermute(
            bf(partial_for(jnp.clip(s_me - 1, 0, 3)) + near_l.astype(jnp.float32)),
            "seq",
            [(3, 2), (2, 1), (1, 0)],
        )
        total = own_part
        for came in (last_r, far_r, last_l, far_l):
            total = total + came.astype(jnp.float32)
        return total.astype(jnp.bfloat16)

    halves = 2 if cols_w % 256 == 0 else 1
    width = cols_w // halves
    recv_r = [None] * halves
    recv_l = [None] * halves
    for i in range(1, n_seq):
        t_r = jnp.clip(s_me + n_seq - i, 0, n_seq - 1)
        t_l = jnp.clip(s_me - n_seq + i, 0, n_seq - 1)
        part_r = partial_for(t_r)
        part_l = partial_for(t_l)
        for h in range(halves):
            send_r = part_r[:, h * width : (h + 1) * width]
            send_l = part_l[:, h * width : (h + 1) * width]
            if recv_r[h] is not None:
                send_r = send_r + recv_r[h].astype(jnp.float32)
                send_l = send_l + recv_l[h].astype(jnp.float32)
            recv_r[h] = lax.ppermute(
                send_r.astype(jnp.bfloat16), "seq", [(z, z + 1) for z in range(i)]
            )
            recv_l[h] = lax.ppermute(
                send_l.astype(jnp.bfloat16), "seq", [(z, z - 1) for z in range(n_seq - i, n_seq)]
            )
    total = partial_for(s_me)
    if recv_r[0] is not None:
        total = total + jnp.concatenate(
            [recv_r[h].astype(jnp.float32) + recv_l[h].astype(jnp.float32) for h in range(halves)],
            axis=1,
        )
    return total.astype(jnp.bfloat16)


def solution(mesh):
    in_specs = (
        P(("grp", "seq"), "mdl"),
        P(("grp", "seq"), "mdl"),
        P(("grp", "seq"), "mdl"),
        P(("grp", "seq"), "mdl"),
        P("mdl", ("grp", "seq")),
        P(None, "mdl"),
        P("mdl"),
        P("seq", "mdl"),
        P("mdl"),
    )
    out_specs = P(("grp", "seq"), "mdl")
    n_seq = mesh.shape["seq"]
    n_mdl = mesh.shape["mdl"]

    def body(*args):
        return per_device(n_seq, n_mdl, *args)

    return jax.shard_map(
        body, mesh=mesh, in_specs=in_specs, out_specs=out_specs, check_vma=False
    )
```

```python
import jax
import jax.numpy as jnp
from jax import lax
from jax.sharding import PartitionSpec as P

HDIM = 128
BLK = 256


def power_two(exponent):
    result = jnp.zeros(exponent.shape, jnp.float32)
    for exponent_value in range(-16, 0):
        result = result + jnp.where(exponent == exponent_value, 2.0**exponent_value, 0.0)
    return result


def fake_quant(matrix, exponent):
    scale = power_two(exponent)
    levels = jnp.clip(jnp.floor(matrix.astype(jnp.float32) / scale + 0.5), -127.0, 127.0)
    return (levels * scale).astype(jnp.bfloat16)


def per_device(
    n_seq,
    n_mdl,
    query_proj,
    key_proj,
    value_proj,
    gate_proj,
    log_decay,
    act_exponent,
    norm_gain,
    out_weight,
    weight_exponent,
):
    tok_rows = query_proj.shape[0]
    feat_here = query_proj.shape[1]
    heads_here = log_decay.shape[0]
    nblocks = tok_rows // BLK
    queries = fake_quant(query_proj, act_exponent[0][None, :])
    keys_quant = fake_quant(key_proj, act_exponent[1][None, :])
    values = fake_quant(value_proj, act_exponent[2][None, :]).reshape(
        nblocks, BLK, heads_here, HDIM
    )
    query_feat = (
        jax.nn.silu(queries.astype(jnp.float32))
        .astype(jnp.bfloat16)
        .reshape(nblocks, BLK, heads_here, HDIM)
    )
    key_feat = (
        jax.nn.silu(keys_quant.astype(jnp.float32))
        .astype(jnp.bfloat16)
        .reshape(nblocks, BLK, heads_here, HDIM)
    )
    decay_cum = jnp.cumsum(log_decay.reshape(heads_here, nblocks, BLK), axis=2)
    block_total = decay_cum[:, :, -1]
    scores = jnp.einsum("bihd,bjhd->hbij", query_feat, key_feat, preferred_element_type=jnp.float32)
    decay_gap = decay_cum[:, :, :, None] - decay_cum[:, :, None, :]
    causal_mask = jnp.arange(BLK)[:, None] >= jnp.arange(BLK)[None, :]
    decay_mask = jnp.where(causal_mask, jnp.exp(jnp.minimum(decay_gap, 0.0)), 0.0)
    block_probs = (scores * decay_mask).astype(jnp.bfloat16)
    within_block = jnp.einsum(
        "hbij,bjhd->bihd", block_probs, values, preferred_element_type=jnp.float32
    )
    tail_decay = jnp.transpose(jnp.exp(block_total[:, :, None] - decay_cum), (1, 2, 0))
    weighted = (key_feat.astype(jnp.float32) * tail_decay[..., None]).astype(jnp.bfloat16)
    block_states = jnp.einsum(
        "bjhd,bjhe->bhde", weighted, values, preferred_element_type=jnp.float32
    )
    block_gain = jnp.exp(block_total).T

    def advance(carried, inputs):
        gain_here, state_here = inputs
        return (gain_here[:, None, None] * carried + state_here, carried)

    local_end, entry_local = lax.scan(
        advance, jnp.zeros((heads_here, HDIM, HDIM), jnp.float32), (block_gain, block_states)
    )
    device_log = jnp.sum(block_total, axis=1)
    log_hi = device_log.astype(jnp.bfloat16)
    log_lo = (device_log - log_hi.astype(jnp.float32)).astype(jnp.bfloat16)
    packed = jnp.concatenate(
        [
            local_end.astype(jnp.bfloat16).reshape(heads_here, HDIM * HDIM),
            jnp.broadcast_to(log_hi[:, None], (heads_here, HDIM)),
            jnp.broadcast_to(log_lo[:, None], (heads_here, HDIM)),
        ],
        axis=1,
    )
    weights = fake_quant(out_weight, weight_exponent[None, :])
    n_x = n_mdl // 2
    m_me = lax.axis_index("mdl")
    core = m_me % 2
    xi = m_me // 2
    piece = weights.shape[0] // n_mdl
    d_idx = jnp.arange(n_x)[:, None]
    e_idx = jnp.arange(2)[None, :]
    mu_tab = 2 * ((xi - d_idx) % n_x) + jnp.where(e_idx == 0, core, 1 - core)
    w_perm = jnp.take(
        weights.reshape(n_mdl, piece, weights.shape[1]), mu_tab.reshape(-1), axis=0
    ).reshape(n_x, 2, piece, weights.shape[1])
    position = lax.axis_index("seq")
    incoming = jnp.zeros((heads_here, HDIM * HDIM), jnp.float32)
    gap = jnp.zeros((heads_here,), jnp.float32)
    shifted = {}
    for d in range(n_seq - 1, 0, -1):
        shifted[d] = lax.ppermute(packed, "seq", [(z, z + d) for z in range(n_seq - d)])
    for d in range(1, n_seq):
        came = shifted[d]
        came_state = came[:, : HDIM * HDIM].astype(jnp.float32)
        came_log = came[:, HDIM * HDIM].astype(jnp.float32) + came[:, HDIM * HDIM + HDIM].astype(
            jnp.float32
        )
        weight = jnp.where(d <= position, jnp.exp(jnp.minimum(gap, 0.0)), 0.0)
        incoming = incoming + weight[:, None] * came_state
        if d == 1:
            incoming = incoming + w_perm[0, 0, 0, 0].astype(jnp.float32) * 0.0
        gap = gap + came_log
    incoming = incoming.reshape(heads_here, HDIM, HDIM)
    before = jnp.cumsum(block_total, axis=1) - block_total
    entry_state = entry_local + jnp.exp(before).T[:, :, None, None] * incoming[None]
    from_state = jnp.einsum(
        "bihd,bhde->bihe",
        query_feat.astype(jnp.float32),
        entry_state,
        precision=lax.Precision.HIGHEST,
    )
    position_decay = jnp.transpose(jnp.exp(decay_cum), (1, 2, 0))[..., None]
    attended = within_block + position_decay * from_state
    mean_square = jnp.mean(attended * attended, axis=-1, keepdims=True)
    normed = (attended * lax.rsqrt(mean_square + 1e-05)).reshape(tok_rows, heads_here * HDIM)
    attn = (normed * norm_gain[None, :] * jax.nn.sigmoid(gate_proj.astype(jnp.float32))).astype(
        jnp.bfloat16
    )

    rows_w, cols_w = weights.shape
    blocks_here = feat_here // rows_w
    piece = rows_w // n_mdl
    s_me = lax.axis_index("seq")
    m_me = lax.axis_index("mdl")
    if n_seq == 4 and n_mdl == 4:
        x_me = m_me // 2
        own_pieces = attn.reshape(tok_rows, n_mdl, piece)
        keep = lax.dynamic_slice_in_dim(own_pieces, 2 * x_me, 2, axis=1)
        away = lax.dynamic_slice_in_dim(own_pieces, 2 * (1 - x_me), 2, axis=1)
        came = lax.ppermute(away, "mdl", [(mu, mu ^ 2) for mu in range(n_mdl)])
        items = jnp.transpose(jnp.concatenate([keep, came], axis=1), (1, 0, 2))
        received = []
        for k in range(n_seq):
            perm = []
            for s in range(n_seq):
                for mu in range(n_mdl):
                    r = (s + k) % n_seq
                    f = mu if r // 2 == 0 else mu ^ 2
                    perm.append((s * n_mdl + mu, f * n_mdl + 2 * (mu // 2) + r % 2))
            item = lax.dynamic_index_in_dim(items, (s_me + k) % n_seq, 0, keepdims=False)
            received.append(lax.ppermute(item, ("seq", "mdl"), perm))
        received = jnp.stack(received)
        r_me = 2 * ((s_me // 2) != (m_me // 2)).astype(jnp.int32) + m_me % 2
        x = jnp.take(received, (r_me - jnp.arange(n_seq)) % n_seq, axis=0)
    else:
        received = []
        for k in range(n_seq):
            perm = []
            for s in range(n_seq):
                for m in range(n_mdl):
                    j = (s + k) % n_seq
                    f = m * blocks_here + j // n_mdl
                    perm.append((s * n_mdl + m, f * n_mdl + j % n_mdl))
            j_send = (s_me + k) % n_seq
            chunk = lax.dynamic_slice_in_dim(attn, j_send * piece, piece, axis=1)
            received.append(lax.ppermute(chunk, ("seq", "mdl"), perm))
        received = jnp.stack(received)
        j_me = (s_me % blocks_here) * n_mdl + m_me
        x = jnp.take(received, (j_me - jnp.arange(n_seq)) % n_seq, axis=0)

    n_x = n_mdl // 2
    core = m_me % 2
    xi = m_me // 2
    got = [x]
    for d in range(1, n_x):
        perm = [(mu, ((mu // 2 + d) % n_x) * 2 + mu % 2) for mu in range(n_mdl)]
        got.append(lax.ppermute(x, "mdl", perm))
    own = jnp.stack(got)
    other = lax.ppermute(own, "mdl", [(mu, mu ^ 1) for mu in range(n_mdl)])
    gathered_x = jnp.stack([own, other], axis=1)

    def partial_for(target):
        rows = lax.dynamic_index_in_dim(gathered_x, target, 2, keepdims=False)
        return jnp.einsum(
            "deti,deic->tc", rows, w_perm, preferred_element_type=jnp.float32
        )

    if n_seq == 4:
        def bf(v):
            return v.astype(jnp.bfloat16)

        near_r = lax.ppermute(
            bf(partial_for(jnp.clip(s_me + 2, 0, 3))), "seq", [(0, 1), (1, 2)]
        )
        far_r = lax.ppermute(bf(partial_for(jnp.int32(3))), "seq", [(0, 3)])
        near_l = lax.ppermute(
            bf(partial_for(jnp.clip(s_me - 2, 0, 3))), "seq", [(3, 2), (2, 1)]
        )
        far_l = lax.ppermute(bf(partial_for(jnp.int32(0))), "seq", [(3, 0)])
        own_part = partial_for(s_me)
        last_r = lax.ppermute(
            bf(
                partial_for(jnp.clip(s_me + 1, 0, 3))
                + near_r.astype(jnp.float32)
                + own_part * 0.0
            ),
            "seq",
            [(0, 1), (1, 2), (2, 3)],
        )
        last_l = lax.ppermute(
            bf(partial_for(jnp.clip(s_me - 1, 0, 3)) + near_l.astype(jnp.float32)),
            "seq",
            [(3, 2), (2, 1), (1, 0)],
        )
        total = own_part
        for came in (last_r, far_r, last_l, far_l):
            total = total + came.astype(jnp.float32)
        return total.astype(jnp.bfloat16)

    halves = 2 if cols_w % 256 == 0 else 1
    width = cols_w // halves
    recv_r = [None] * halves
    recv_l = [None] * halves
    for i in range(1, n_seq):
        t_r = jnp.clip(s_me + n_seq - i, 0, n_seq - 1)
        t_l = jnp.clip(s_me - n_seq + i, 0, n_seq - 1)
        part_r = partial_for(t_r)
        part_l = partial_for(t_l)
        for h in range(halves):
            send_r = part_r[:, h * width : (h + 1) * width]
            send_l = part_l[:, h * width : (h + 1) * width]
            if recv_r[h] is not None:
                send_r = send_r + recv_r[h].astype(jnp.float32)
                send_l = send_l + recv_l[h].astype(jnp.float32)
            recv_r[h] = lax.ppermute(
                send_r.astype(jnp.bfloat16), "seq", [(z, z + 1) for z in range(i)]
            )
            recv_l[h] = lax.ppermute(
                send_l.astype(jnp.bfloat16), "seq", [(z, z - 1) for z in range(n_seq - i, n_seq)]
            )
    total = partial_for(s_me)
    if recv_r[0] is not None:
        total = total + jnp.concatenate(
            [recv_r[h].astype(jnp.float32) + recv_l[h].astype(jnp.float32) for h in range(halves)],
            axis=1,
        )
    return total.astype(jnp.bfloat16)


def solution(mesh):
    in_specs = (
        P(("grp", "seq"), "mdl"),
        P(("grp", "seq"), "mdl"),
        P(("grp", "seq"), "mdl"),
        P(("grp", "seq"), "mdl"),
        P("mdl", ("grp", "seq")),
        P(None, "mdl"),
        P("mdl"),
        P("seq", "mdl"),
        P("mdl"),
    )
    out_specs = P(("grp", "seq"), "mdl")
    n_seq = mesh.shape["seq"]
    n_mdl = mesh.shape["mdl"]

    def body(*args):
        return per_device(n_seq, n_mdl, *args)

    return jax.shard_map(
        body, mesh=mesh, in_specs=in_specs, out_specs=out_specs, check_vma=False
    )
```

```python
import jax
import jax.numpy as jnp
from jax import lax
from jax.sharding import PartitionSpec as P

HDIM = 128
BLK = 256


def power_two(exponent):
    result = jnp.zeros(exponent.shape, jnp.float32)
    for exponent_value in range(-16, 0):
        result = result + jnp.where(exponent == exponent_value, 2.0**exponent_value, 0.0)
    return result


def fake_quant(matrix, exponent):
    scale = power_two(exponent)
    levels = jnp.clip(jnp.floor(matrix.astype(jnp.float32) / scale + 0.5), -127.0, 127.0)
    return (levels * scale).astype(jnp.bfloat16)


def per_device(
    n_seq,
    n_mdl,
    query_proj,
    key_proj,
    value_proj,
    gate_proj,
    log_decay,
    act_exponent,
    norm_gain,
    out_weight,
    weight_exponent,
):
    tok_rows = query_proj.shape[0]
    feat_here = query_proj.shape[1]
    heads_here = log_decay.shape[0]
    nblocks = tok_rows // BLK
    queries = fake_quant(query_proj, act_exponent[0][None, :])
    keys_quant = fake_quant(key_proj, act_exponent[1][None, :])
    values = fake_quant(value_proj, act_exponent[2][None, :]).reshape(
        nblocks, BLK, heads_here, HDIM
    )
    query_feat = (
        jax.nn.silu(queries.astype(jnp.float32))
        .astype(jnp.bfloat16)
        .reshape(nblocks, BLK, heads_here, HDIM)
    )
    key_feat = (
        jax.nn.silu(keys_quant.astype(jnp.float32))
        .astype(jnp.bfloat16)
        .reshape(nblocks, BLK, heads_here, HDIM)
    )
    decay_cum = jnp.cumsum(log_decay.reshape(heads_here, nblocks, BLK), axis=2)
    block_total = decay_cum[:, :, -1]
    scores = jnp.einsum("bihd,bjhd->hbij", query_feat, key_feat, preferred_element_type=jnp.float32)
    decay_gap = decay_cum[:, :, :, None] - decay_cum[:, :, None, :]
    causal_mask = jnp.arange(BLK)[:, None] >= jnp.arange(BLK)[None, :]
    decay_mask = jnp.where(causal_mask, jnp.exp(jnp.minimum(decay_gap, 0.0)), 0.0)
    block_probs = (scores * decay_mask).astype(jnp.bfloat16)
    within_block = jnp.einsum(
        "hbij,bjhd->bihd", block_probs, values, preferred_element_type=jnp.float32
    )
    tail_decay = jnp.transpose(jnp.exp(block_total[:, :, None] - decay_cum), (1, 2, 0))
    weighted = (key_feat.astype(jnp.float32) * tail_decay[..., None]).astype(jnp.bfloat16)
    block_states = jnp.einsum(
        "bjhd,bjhe->bhde", weighted, values, preferred_element_type=jnp.float32
    )
    block_gain = jnp.exp(block_total).T

    def advance(carried, inputs):
        gain_here, state_here = inputs
        return (gain_here[:, None, None] * carried + state_here, carried)

    local_end, entry_local = lax.scan(
        advance, jnp.zeros((heads_here, HDIM, HDIM), jnp.float32), (block_gain, block_states)
    )
    device_log = jnp.sum(block_total, axis=1)
    log_hi = device_log.astype(jnp.bfloat16)
    log_lo = (device_log - log_hi.astype(jnp.float32)).astype(jnp.bfloat16)
    packed = jnp.concatenate(
        [
            local_end.astype(jnp.bfloat16).reshape(heads_here, HDIM * HDIM),
            jnp.broadcast_to(log_hi[:, None], (heads_here, HDIM)),
            jnp.broadcast_to(log_lo[:, None], (heads_here, HDIM)),
        ],
        axis=1,
    )
    weights = fake_quant(out_weight, weight_exponent[None, :])
    n_x = n_mdl // 2
    m_me = lax.axis_index("mdl")
    core = m_me % 2
    xi = m_me // 2
    piece = weights.shape[0] // n_mdl
    d_idx = jnp.arange(n_x)[:, None]
    e_idx = jnp.arange(2)[None, :]
    mu_tab = 2 * ((xi - d_idx) % n_x) + jnp.where(e_idx == 0, core, 1 - core)
    w_perm = jnp.take(
        weights.reshape(n_mdl, piece, weights.shape[1]), mu_tab.reshape(-1), axis=0
    ).reshape(n_x, 2, piece, weights.shape[1])
    position = lax.axis_index("seq")
    incoming = jnp.zeros((heads_here, HDIM * HDIM), jnp.float32)
    gap = jnp.zeros((heads_here,), jnp.float32)
    shifted = {}
    for d in range(n_seq - 1, 0, -1):
        shifted[d] = lax.ppermute(packed, "seq", [(z, z + d) for z in range(n_seq - d)])
    for d in range(1, n_seq):
        came = shifted[d]
        came_state = came[:, : HDIM * HDIM].astype(jnp.float32)
        came_log = came[:, HDIM * HDIM].astype(jnp.float32) + came[:, HDIM * HDIM + HDIM].astype(
            jnp.float32
        )
        weight = jnp.where(d <= position, jnp.exp(jnp.minimum(gap, 0.0)), 0.0)
        incoming = incoming + weight[:, None] * came_state
        if d == 1:
            incoming = incoming + w_perm[0, 0, 0, 0].astype(jnp.float32) * 0.0
        gap = gap + came_log
    incoming = incoming.reshape(heads_here, HDIM, HDIM)
    before = jnp.cumsum(block_total, axis=1) - block_total
    entry_state = entry_local + jnp.exp(before).T[:, :, None, None] * incoming[None]
    from_state = jnp.einsum(
        "bihd,bhde->bihe",
        query_feat.astype(jnp.float32),
        entry_state,
        precision=lax.Precision.HIGHEST,
    )
    position_decay = jnp.transpose(jnp.exp(decay_cum), (1, 2, 0))[..., None]
    attended = within_block + position_decay * from_state
    mean_square = jnp.mean(attended * attended, axis=-1, keepdims=True)
    normed = (attended * lax.rsqrt(mean_square + 1e-05)).reshape(tok_rows, heads_here * HDIM)
    attn = (normed * norm_gain[None, :] * jax.nn.sigmoid(gate_proj.astype(jnp.float32))).astype(
        jnp.bfloat16
    )

    rows_w, cols_w = weights.shape
    blocks_here = feat_here // rows_w
    piece = rows_w // n_mdl
    s_me = lax.axis_index("seq")
    m_me = lax.axis_index("mdl")
    if n_seq == 4 and n_mdl == 4 and False:
        x_me = m_me // 2
        own_pieces = attn.reshape(tok_rows, n_mdl, piece)
        keep = lax.dynamic_slice_in_dim(own_pieces, 2 * x_me, 2, axis=1)
        away = lax.dynamic_slice_in_dim(own_pieces, 2 * (1 - x_me), 2, axis=1)
        came = lax.ppermute(away, "mdl", [(mu, mu ^ 2) for mu in range(n_mdl)])
        items = jnp.transpose(jnp.concatenate([keep, came], axis=1), (1, 0, 2))
        received = []
        for k in range(n_seq):
            perm = []
            for s in range(n_seq):
                for mu in range(n_mdl):
                    r = (s + k) % n_seq
                    f = mu if r // 2 == 0 else mu ^ 2
                    perm.append((s * n_mdl + mu, f * n_mdl + 2 * (mu // 2) + r % 2))
            item = lax.dynamic_index_in_dim(items, (s_me + k) % n_seq, 0, keepdims=False)
            received.append(lax.ppermute(item, ("seq", "mdl"), perm))
        received = jnp.stack(received)
        r_me = 2 * ((s_me // 2) != (m_me // 2)).astype(jnp.int32) + m_me % 2
        x = jnp.take(received, (r_me - jnp.arange(n_seq)) % n_seq, axis=0)
    else:
        received = []
        for k in range(n_seq):
            perm = []
            for s in range(n_seq):
                for m in range(n_mdl):
                    j = (s + k) % n_seq
                    f = m * blocks_here + j // n_mdl
                    perm.append((s * n_mdl + m, f * n_mdl + j % n_mdl))
            j_send = (s_me + k) % n_seq
            chunk = lax.dynamic_slice_in_dim(attn, j_send * piece, piece, axis=1)
            received.append(lax.ppermute(chunk, ("seq", "mdl"), perm))
        received = jnp.stack(received)
        j_me = (s_me % blocks_here) * n_mdl + m_me
        x = jnp.take(received, (j_me - jnp.arange(n_seq)) % n_seq, axis=0)

    n_x = n_mdl // 2
    core = m_me % 2
    xi = m_me // 2
    got = [x]
    for d in range(1, n_x):
        perm = [(mu, ((mu // 2 + d) % n_x) * 2 + mu % 2) for mu in range(n_mdl)]
        got.append(lax.ppermute(x, "mdl", perm))
    own = jnp.stack(got)
    other = lax.ppermute(own, "mdl", [(mu, mu ^ 1) for mu in range(n_mdl)])
    gathered_x = jnp.stack([own, other], axis=1)

    def partial_for(target):
        rows = lax.dynamic_index_in_dim(gathered_x, target, 2, keepdims=False)
        return jnp.einsum(
            "deti,deic->tc", rows, w_perm, preferred_element_type=jnp.float32
        )

    if n_seq == 4:
        def bf(v):
            return v.astype(jnp.bfloat16)

        near_r = lax.ppermute(
            bf(partial_for(jnp.clip(s_me + 2, 0, 3))), "seq", [(0, 1), (1, 2)]
        )
        far_r = lax.ppermute(bf(partial_for(jnp.int32(3))), "seq", [(0, 3)])
        near_l = lax.ppermute(
            bf(partial_for(jnp.clip(s_me - 2, 0, 3))), "seq", [(3, 2), (2, 1)]
        )
        far_l = lax.ppermute(bf(partial_for(jnp.int32(0))), "seq", [(3, 0)])
        own_part = partial_for(s_me)
        last_r = lax.ppermute(
            bf(
                partial_for(jnp.clip(s_me + 1, 0, 3))
                + near_r.astype(jnp.float32)
                + own_part * 0.0
            ),
            "seq",
            [(0, 1), (1, 2), (2, 3)],
        )
        last_l = lax.ppermute(
            bf(partial_for(jnp.clip(s_me - 1, 0, 3)) + near_l.astype(jnp.float32)),
            "seq",
            [(3, 2), (2, 1), (1, 0)],
        )
        total = own_part
        for came in (last_r, far_r, last_l, far_l):
            total = total + came.astype(jnp.float32)
        return total.astype(jnp.bfloat16)

    halves = 2 if cols_w % 256 == 0 else 1
    width = cols_w // halves
    recv_r = [None] * halves
    recv_l = [None] * halves
    for i in range(1, n_seq):
        t_r = jnp.clip(s_me + n_seq - i, 0, n_seq - 1)
        t_l = jnp.clip(s_me - n_seq + i, 0, n_seq - 1)
        part_r = partial_for(t_r)
        part_l = partial_for(t_l)
        for h in range(halves):
            send_r = part_r[:, h * width : (h + 1) * width]
            send_l = part_l[:, h * width : (h + 1) * width]
            if recv_r[h] is not None:
                send_r = send_r + recv_r[h].astype(jnp.float32)
                send_l = send_l + recv_l[h].astype(jnp.float32)
            recv_r[h] = lax.ppermute(
                send_r.astype(jnp.bfloat16), "seq", [(z, z + 1) for z in range(i)]
            )
            recv_l[h] = lax.ppermute(
                send_l.astype(jnp.bfloat16), "seq", [(z, z - 1) for z in range(n_seq - i, n_seq)]
            )
    total = partial_for(s_me)
    if recv_r[0] is not None:
        total = total + jnp.concatenate(
            [recv_r[h].astype(jnp.float32) + recv_l[h].astype(jnp.float32) for h in range(halves)],
            axis=1,
        )
    return total.astype(jnp.bfloat16)


def solution(mesh):
    in_specs = (
        P(("grp", "seq"), "mdl"),
        P(("grp", "seq"), "mdl"),
        P(("grp", "seq"), "mdl"),
        P(("grp", "seq"), "mdl"),
        P("mdl", ("grp", "seq")),
        P(None, "mdl"),
        P("mdl"),
        P("seq", "mdl"),
        P("mdl"),
    )
    out_specs = P(("grp", "seq"), "mdl")
    n_seq = mesh.shape["seq"]
    n_mdl = mesh.shape["mdl"]

    def body(*args):
        return per_device(n_seq, n_mdl, *args)

    return jax.shard_map(
        body, mesh=mesh, in_specs=in_specs, out_specs=out_specs, check_vma=False
    )
```

```python
import jax
import jax.numpy as jnp
from jax import lax
from jax.sharding import PartitionSpec as P

HDIM = 128
BLK = 256


def power_two(exponent):
    result = jnp.zeros(exponent.shape, jnp.float32)
    for exponent_value in range(-16, 0):
        result = result + jnp.where(exponent == exponent_value, 2.0**exponent_value, 0.0)
    return result


def fake_quant(matrix, exponent):
    scale = power_two(exponent)
    levels = jnp.clip(jnp.floor(matrix.astype(jnp.float32) / scale + 0.5), -127.0, 127.0)
    return (levels * scale).astype(jnp.bfloat16)


def per_device(
    n_seq,
    n_mdl,
    query_proj,
    key_proj,
    value_proj,
    gate_proj,
    log_decay,
    act_exponent,
    norm_gain,
    out_weight,
    weight_exponent,
):
    tok_rows = query_proj.shape[0]
    feat_here = query_proj.shape[1]
    heads_here = log_decay.shape[0]
    nblocks = tok_rows // BLK
    queries = fake_quant(query_proj, act_exponent[0][None, :])
    keys_quant = fake_quant(key_proj, act_exponent[1][None, :])
    values = fake_quant(value_proj, act_exponent[2][None, :]).reshape(
        nblocks, BLK, heads_here, HDIM
    )
    query_feat = (
        jax.nn.silu(queries.astype(jnp.float32))
        .astype(jnp.bfloat16)
        .reshape(nblocks, BLK, heads_here, HDIM)
    )
    key_feat = (
        jax.nn.silu(keys_quant.astype(jnp.float32))
        .astype(jnp.bfloat16)
        .reshape(nblocks, BLK, heads_here, HDIM)
    )
    decay_cum = jnp.cumsum(log_decay.reshape(heads_here, nblocks, BLK), axis=2)
    block_total = decay_cum[:, :, -1]
    scores = jnp.einsum("bihd,bjhd->hbij", query_feat, key_feat, preferred_element_type=jnp.float32)
    decay_gap = decay_cum[:, :, :, None] - decay_cum[:, :, None, :]
    causal_mask = jnp.arange(BLK)[:, None] >= jnp.arange(BLK)[None, :]
    decay_mask = jnp.where(causal_mask, jnp.exp(jnp.minimum(decay_gap, 0.0)), 0.0)
    block_probs = (scores * decay_mask).astype(jnp.bfloat16)
    within_block = jnp.einsum(
        "hbij,bjhd->bihd", block_probs, values, preferred_element_type=jnp.float32
    )
    tail_decay = jnp.transpose(jnp.exp(block_total[:, :, None] - decay_cum), (1, 2, 0))
    weighted = (key_feat.astype(jnp.float32) * tail_decay[..., None]).astype(jnp.bfloat16)
    block_states = jnp.einsum(
        "bjhd,bjhe->bhde", weighted, values, preferred_element_type=jnp.float32
    )
    block_gain = jnp.exp(block_total).T

    def advance(carried, inputs):
        gain_here, state_here = inputs
        return (gain_here[:, None, None] * carried + state_here, carried)

    local_end, entry_local = lax.scan(
        advance, jnp.zeros((heads_here, HDIM, HDIM), jnp.float32), (block_gain, block_states)
    )
    device_log = jnp.sum(block_total, axis=1)
    log_hi = device_log.astype(jnp.bfloat16)
    log_lo = (device_log - log_hi.astype(jnp.float32)).astype(jnp.bfloat16)
    packed = jnp.concatenate(
        [
            local_end.astype(jnp.bfloat16).reshape(heads_here, HDIM * HDIM),
            jnp.broadcast_to(log_hi[:, None], (heads_here, HDIM)),
            jnp.broadcast_to(log_lo[:, None], (heads_here, HDIM)),
        ],
        axis=1,
    )
    weights = fake_quant(out_weight, weight_exponent[None, :])
    n_x = n_mdl // 2
    m_me = lax.axis_index("mdl")
    core = m_me % 2
    xi = m_me // 2
    piece = weights.shape[0] // n_mdl
    d_idx = jnp.arange(n_x)[:, None]
    e_idx = jnp.arange(2)[None, :]
    mu_tab = 2 * ((xi - d_idx) % n_x) + jnp.where(e_idx == 0, core, 1 - core)
    w_perm = jnp.take(
        weights.reshape(n_mdl, piece, weights.shape[1]), mu_tab.reshape(-1), axis=0
    ).reshape(n_x, 2, piece, weights.shape[1])
    position = lax.axis_index("seq")
    incoming = jnp.zeros((heads_here, HDIM * HDIM), jnp.float32)
    gap = jnp.zeros((heads_here,), jnp.float32)
    shifted = {}
    for d in range(n_seq - 1, 0, -1):
        shifted[d] = lax.ppermute(packed, "seq", [(z, z + d) for z in range(n_seq - d)])
    for d in range(1, n_seq):
        came = shifted[d]
        came_state = came[:, : HDIM * HDIM].astype(jnp.float32)
        came_log = came[:, HDIM * HDIM].astype(jnp.float32) + came[:, HDIM * HDIM + HDIM].astype(
            jnp.float32
        )
        weight = jnp.where(d <= position, jnp.exp(jnp.minimum(gap, 0.0)), 0.0)
        incoming = incoming + weight[:, None] * came_state
        if d == n_seq - 1:
            incoming = incoming + w_perm[0, 0, 0, 0].astype(jnp.float32) * 0.0
        gap = gap + came_log
    incoming = incoming.reshape(heads_here, HDIM, HDIM)
    before = jnp.cumsum(block_total, axis=1) - block_total
    entry_state = entry_local + jnp.exp(before).T[:, :, None, None] * incoming[None]
    from_state = jnp.einsum(
        "bihd,bhde->bihe",
        query_feat.astype(jnp.float32),
        entry_state,
        precision=lax.Precision.HIGHEST,
    )
    position_decay = jnp.transpose(jnp.exp(decay_cum), (1, 2, 0))[..., None]
    attended = within_block + position_decay * from_state
    mean_square = jnp.mean(attended * attended, axis=-1, keepdims=True)
    normed = (attended * lax.rsqrt(mean_square + 1e-05)).reshape(tok_rows, heads_here * HDIM)
    attn = (normed * norm_gain[None, :] * jax.nn.sigmoid(gate_proj.astype(jnp.float32))).astype(
        jnp.bfloat16
    )

    rows_w, cols_w = weights.shape
    blocks_here = feat_here // rows_w
    piece = rows_w // n_mdl
    s_me = lax.axis_index("seq")
    m_me = lax.axis_index("mdl")
    if n_seq == 4 and n_mdl == 4:
        x_me = m_me // 2
        own_pieces = attn.reshape(tok_rows, n_mdl, piece)
        keep = lax.dynamic_slice_in_dim(own_pieces, 2 * x_me, 2, axis=1)
        away = lax.dynamic_slice_in_dim(own_pieces, 2 * (1 - x_me), 2, axis=1)
        came = lax.ppermute(away, "mdl", [(mu, mu ^ 2) for mu in range(n_mdl)])
        items = jnp.transpose(jnp.concatenate([keep, came], axis=1), (1, 0, 2))
        received = []
        for k in range(n_seq):
            perm = []
            for s in range(n_seq):
                for mu in range(n_mdl):
                    r = (s + k) % n_seq
                    f = mu if r // 2 == 0 else mu ^ 2
                    perm.append((s * n_mdl + mu, f * n_mdl + 2 * (mu // 2) + r % 2))
            item = lax.dynamic_index_in_dim(items, (s_me + k) % n_seq, 0, keepdims=False)
            received.append(lax.ppermute(item, ("seq", "mdl"), perm))
        received = jnp.stack(received)
        r_me = 2 * ((s_me // 2) != (m_me // 2)).astype(jnp.int32) + m_me % 2
        x = jnp.take(received, (r_me - jnp.arange(n_seq)) % n_seq, axis=0)
    else:
        received = []
        for k in range(n_seq):
            perm = []
            for s in range(n_seq):
                for m in range(n_mdl):
                    j = (s + k) % n_seq
                    f = m * blocks_here + j // n_mdl
                    perm.append((s * n_mdl + m, f * n_mdl + j % n_mdl))
            j_send = (s_me + k) % n_seq
            chunk = lax.dynamic_slice_in_dim(attn, j_send * piece, piece, axis=1)
            received.append(lax.ppermute(chunk, ("seq", "mdl"), perm))
        received = jnp.stack(received)
        j_me = (s_me % blocks_here) * n_mdl + m_me
        x = jnp.take(received, (j_me - jnp.arange(n_seq)) % n_seq, axis=0)

    n_x = n_mdl // 2
    core = m_me % 2
    xi = m_me // 2
    got = [x]
    for d in range(1, n_x):
        perm = [(mu, ((mu // 2 + d) % n_x) * 2 + mu % 2) for mu in range(n_mdl)]
        got.append(lax.ppermute(x, "mdl", perm))
    own = jnp.stack(got)
    other = lax.ppermute(own, "mdl", [(mu, mu ^ 1) for mu in range(n_mdl)])
    gathered_x = jnp.stack([own, other], axis=1)

    def partial_for(target):
        rows = lax.dynamic_index_in_dim(gathered_x, target, 2, keepdims=False)
        return jnp.einsum(
            "deti,deic->tc", rows, w_perm, preferred_element_type=jnp.float32
        )

    if n_seq == 4:
        def bf(v):
            return v.astype(jnp.bfloat16)

        near_r = lax.ppermute(
            bf(partial_for(jnp.clip(s_me + 2, 0, 3))), "seq", [(0, 1), (1, 2)]
        )
        far_r = lax.ppermute(bf(partial_for(jnp.int32(3))), "seq", [(0, 3)])
        near_l = lax.ppermute(
            bf(partial_for(jnp.clip(s_me - 2, 0, 3))), "seq", [(3, 2), (2, 1)]
        )
        far_l = lax.ppermute(bf(partial_for(jnp.int32(0))), "seq", [(3, 0)])
        own_part = partial_for(s_me)
        last_r = lax.ppermute(
            bf(
                partial_for(jnp.clip(s_me + 1, 0, 3))
                + near_r.astype(jnp.float32)
                + own_part * 0.0
            ),
            "seq",
            [(0, 1), (1, 2), (2, 3)],
        )
        last_l = lax.ppermute(
            bf(partial_for(jnp.clip(s_me - 1, 0, 3)) + near_l.astype(jnp.float32)),
            "seq",
            [(3, 2), (2, 1), (1, 0)],
        )
        total = own_part
        for came in (last_r, far_r, last_l, far_l):
            total = total + came.astype(jnp.float32)
        return total.astype(jnp.bfloat16)

    halves = 2 if cols_w % 256 == 0 else 1
    width = cols_w // halves
    recv_r = [None] * halves
    recv_l = [None] * halves
    for i in range(1, n_seq):
        t_r = jnp.clip(s_me + n_seq - i, 0, n_seq - 1)
        t_l = jnp.clip(s_me - n_seq + i, 0, n_seq - 1)
        part_r = partial_for(t_r)
        part_l = partial_for(t_l)
        for h in range(halves):
            send_r = part_r[:, h * width : (h + 1) * width]
            send_l = part_l[:, h * width : (h + 1) * width]
            if recv_r[h] is not None:
                send_r = send_r + recv_r[h].astype(jnp.float32)
                send_l = send_l + recv_l[h].astype(jnp.float32)
            recv_r[h] = lax.ppermute(
                send_r.astype(jnp.bfloat16), "seq", [(z, z + 1) for z in range(i)]
            )
            recv_l[h] = lax.ppermute(
                send_l.astype(jnp.bfloat16), "seq", [(z, z - 1) for z in range(n_seq - i, n_seq)]
            )
    total = partial_for(s_me)
    if recv_r[0] is not None:
        total = total + jnp.concatenate(
            [recv_r[h].astype(jnp.float32) + recv_l[h].astype(jnp.float32) for h in range(halves)],
            axis=1,
        )
    return total.astype(jnp.bfloat16)


def solution(mesh):
    in_specs = (
        P(("grp", "seq"), "mdl"),
        P(("grp", "seq"), "mdl"),
        P(("grp", "seq"), "mdl"),
        P(("grp", "seq"), "mdl"),
        P("mdl", ("grp", "seq")),
        P(None, "mdl"),
        P("mdl"),
        P("seq", "mdl"),
        P("mdl"),
    )
    out_specs = P(("grp", "seq"), "mdl")
    n_seq = mesh.shape["seq"]
    n_mdl = mesh.shape["mdl"]

    def body(*args):
        return per_device(n_seq, n_mdl, *args)

    return jax.shard_map(
        body, mesh=mesh, in_specs=in_specs, out_specs=out_specs, check_vma=False
    )
```

```python
import jax
import jax.numpy as jnp
from jax import lax
from jax.sharding import PartitionSpec as P

HDIM = 128
BLK = 256


def power_two(exponent):
    result = jnp.zeros(exponent.shape, jnp.float32)
    for exponent_value in range(-16, 0):
        result = result + jnp.where(exponent == exponent_value, 2.0**exponent_value, 0.0)
    return result


def fake_quant(matrix, exponent):
    scale = power_two(exponent)
    levels = jnp.clip(jnp.floor(matrix.astype(jnp.float32) / scale + 0.5), -127.0, 127.0)
    return (levels * scale).astype(jnp.bfloat16)


def per_device(
    n_seq,
    n_mdl,
    query_proj,
    key_proj,
    value_proj,
    gate_proj,
    log_decay,
    act_exponent,
    norm_gain,
    out_weight,
    weight_exponent,
):
    tok_rows = query_proj.shape[0]
    feat_here = query_proj.shape[1]
    heads_here = log_decay.shape[0]
    nblocks = tok_rows // BLK
    queries = fake_quant(query_proj, act_exponent[0][None, :])
    keys_quant = fake_quant(key_proj, act_exponent[1][None, :])
    values = fake_quant(value_proj, act_exponent[2][None, :]).reshape(
        nblocks, BLK, heads_here, HDIM
    )
    query_feat = (
        jax.nn.silu(queries.astype(jnp.float32))
        .astype(jnp.bfloat16)
        .reshape(nblocks, BLK, heads_here, HDIM)
    )
    key_feat = (
        jax.nn.silu(keys_quant.astype(jnp.float32))
        .astype(jnp.bfloat16)
        .reshape(nblocks, BLK, heads_here, HDIM)
    )
    decay_cum = jnp.cumsum(log_decay.reshape(heads_here, nblocks, BLK), axis=2)
    block_total = decay_cum[:, :, -1]
    scores = jnp.einsum("bihd,bjhd->hbij", query_feat, key_feat, preferred_element_type=jnp.float32)
    decay_gap = decay_cum[:, :, :, None] - decay_cum[:, :, None, :]
    causal_mask = jnp.arange(BLK)[:, None] >= jnp.arange(BLK)[None, :]
    decay_mask = jnp.where(causal_mask, jnp.exp(jnp.minimum(decay_gap, 0.0)), 0.0)
    block_probs = (scores * decay_mask).astype(jnp.bfloat16)
    within_block = jnp.einsum(
        "hbij,bjhd->bihd", block_probs, values, preferred_element_type=jnp.float32
    )
    tail_decay = jnp.transpose(jnp.exp(block_total[:, :, None] - decay_cum), (1, 2, 0))
    weighted = (key_feat.astype(jnp.float32) * tail_decay[..., None]).astype(jnp.bfloat16)
    block_states = jnp.einsum(
        "bjhd,bjhe->bhde", weighted, values, preferred_element_type=jnp.float32
    )
    block_gain = jnp.exp(block_total).T

    def advance(carried, inputs):
        gain_here, state_here = inputs
        return (gain_here[:, None, None] * carried + state_here, carried)

    local_end, entry_local = lax.scan(
        advance, jnp.zeros((heads_here, HDIM, HDIM), jnp.float32), (block_gain, block_states)
    )
    device_log = jnp.sum(block_total, axis=1)
    log_hi = device_log.astype(jnp.bfloat16)
    log_lo = (device_log - log_hi.astype(jnp.float32)).astype(jnp.bfloat16)
    packed = jnp.concatenate(
        [
            local_end.astype(jnp.bfloat16).reshape(heads_here, HDIM * HDIM),
            jnp.broadcast_to(log_hi[:, None], (heads_here, HDIM)),
            jnp.broadcast_to(log_lo[:, None], (heads_here, HDIM)),
        ],
        axis=1,
    )
    weights = fake_quant(out_weight, weight_exponent[None, :])
    n_x = n_mdl // 2
    m_me = lax.axis_index("mdl")
    core = m_me % 2
    xi = m_me // 2
    piece = weights.shape[0] // n_mdl
    d_idx = jnp.arange(n_x)[:, None]
    e_idx = jnp.arange(2)[None, :]
    mu_tab = 2 * ((xi - d_idx) % n_x) + jnp.where(e_idx == 0, core, 1 - core)
    w_perm = jnp.take(
        weights.reshape(n_mdl, piece, weights.shape[1]), mu_tab.reshape(-1), axis=0
    ).reshape(n_x, 2, piece, weights.shape[1])
    position = lax.axis_index("seq")
    incoming = jnp.zeros((heads_here, HDIM * HDIM), jnp.float32)
    gap = jnp.zeros((heads_here,), jnp.float32)
    shifted = {}
    for d in range(n_seq - 1, 0, -1):
        shifted[d] = lax.ppermute(packed, "seq", [(z, z + d) for z in range(n_seq - d)])
    for d in range(1, n_seq):
        came = shifted[d]
        came_state = came[:, : HDIM * HDIM].astype(jnp.float32)
        came_log = came[:, HDIM * HDIM].astype(jnp.float32) + came[:, HDIM * HDIM + HDIM].astype(
            jnp.float32
        )
        weight = jnp.where(d <= position, jnp.exp(jnp.minimum(gap, 0.0)), 0.0)
        incoming = incoming + weight[:, None] * came_state
        if d == 1:
            incoming = incoming + w_perm[0, 0, 0, 0].astype(jnp.float32) * 0.0
        gap = gap + came_log
    incoming = incoming.reshape(heads_here, HDIM, HDIM)
    before = jnp.cumsum(block_total, axis=1) - block_total
    entry_state = entry_local + jnp.exp(before).T[:, :, None, None] * incoming[None]
    from_state = jnp.einsum(
        "bihd,bhde->bihe",
        query_feat.astype(jnp.float32),
        entry_state,
        precision=lax.Precision.HIGHEST,
    )
    position_decay = jnp.transpose(jnp.exp(decay_cum), (1, 2, 0))[..., None]
    attended = within_block + position_decay * from_state
    mean_square = jnp.mean(attended * attended, axis=-1, keepdims=True)
    normed = (attended * lax.rsqrt(mean_square + 1e-05)).reshape(tok_rows, heads_here * HDIM)
    attn = (normed * norm_gain[None, :] * jax.nn.sigmoid(gate_proj.astype(jnp.float32))).astype(
        jnp.bfloat16
    )

    rows_w, cols_w = weights.shape
    blocks_here = feat_here // rows_w
    piece = rows_w // n_mdl
    s_me = lax.axis_index("seq")
    m_me = lax.axis_index("mdl")
    if n_seq == 4 and n_mdl == 4:
        x_me = m_me // 2
        own_pieces = attn.reshape(tok_rows, n_mdl, piece)
        keep = lax.dynamic_slice_in_dim(own_pieces, 2 * x_me, 2, axis=1)
        away = lax.dynamic_slice_in_dim(own_pieces, 2 * (1 - x_me), 2, axis=1)
        came = lax.ppermute(away, "mdl", [(mu, mu ^ 2) for mu in range(n_mdl)])
        items = jnp.transpose(jnp.concatenate([keep, came], axis=1), (1, 0, 2))
        received = []
        for k in range(n_seq):
            perm = []
            for s in range(n_seq):
                for mu in range(n_mdl):
                    r = (s + k) % n_seq
                    f = mu if r // 2 == 0 else mu ^ 2
                    perm.append((s * n_mdl + mu, f * n_mdl + 2 * (mu // 2) + r % 2))
            item = lax.dynamic_index_in_dim(items, (s_me + k) % n_seq, 0, keepdims=False)
            received.append(lax.ppermute(item, ("seq", "mdl"), perm))
        received = jnp.stack(received)
        r_me = 2 * ((s_me // 2) != (m_me // 2)).astype(jnp.int32) + m_me % 2
        x = jnp.take(received, (r_me - jnp.arange(n_seq)) % n_seq, axis=0)
    else:
        received = []
        for k in range(n_seq):
            perm = []
            for s in range(n_seq):
                for m in range(n_mdl):
                    j = (s + k) % n_seq
                    f = m * blocks_here + j // n_mdl
                    perm.append((s * n_mdl + m, f * n_mdl + j % n_mdl))
            j_send = (s_me + k) % n_seq
            chunk = lax.dynamic_slice_in_dim(attn, j_send * piece, piece, axis=1)
            received.append(lax.ppermute(chunk, ("seq", "mdl"), perm))
        received = jnp.stack(received)
        j_me = (s_me % blocks_here) * n_mdl + m_me
        x = jnp.take(received, (j_me - jnp.arange(n_seq)) % n_seq, axis=0)

    n_x = n_mdl // 2
    core = m_me % 2
    xi = m_me // 2
    got = [x]
    for d in range(1, n_x):
        perm = [(mu, ((mu // 2 + d) % n_x) * 2 + mu % 2) for mu in range(n_mdl)]
        got.append(lax.ppermute(x, "mdl", perm))
    own = jnp.stack(got)
    other = lax.ppermute(own, "mdl", [(mu, mu ^ 1) for mu in range(n_mdl)])
    gathered_x = jnp.stack([own, other], axis=1)

    def partial_for(target):
        rows = lax.dynamic_index_in_dim(gathered_x, target, 2, keepdims=False)
        return jnp.einsum(
            "deti,deic->tc", rows, w_perm, preferred_element_type=jnp.float32
        )

    if n_seq == 4:
        def bf(v):
            return v.astype(jnp.bfloat16)

        near_r = lax.ppermute(
            bf(partial_for(jnp.clip(s_me + 2, 0, 3))), "seq", [(0, 1), (1, 2)]
        )
        far_r = lax.ppermute(bf(partial_for(jnp.int32(3))), "seq", [(0, 3)])
        near_l = lax.ppermute(
            bf(partial_for(jnp.clip(s_me - 2, 0, 3))), "seq", [(3, 2), (2, 1)]
        )
        far_l = lax.ppermute(bf(partial_for(jnp.int32(0))), "seq", [(3, 0)])
        own_part = partial_for(s_me)
        last_l = lax.ppermute(
            bf(partial_for(jnp.clip(s_me - 1, 0, 3)) + near_l.astype(jnp.float32)),
            "seq",
            [(3, 2), (2, 1), (1, 0)],
        )
        last_r = lax.ppermute(
            bf(
                partial_for(jnp.clip(s_me + 1, 0, 3))
                + near_r.astype(jnp.float32)
                + own_part * 0.0
            ),
            "seq",
            [(0, 1), (1, 2), (2, 3)],
        )
        total = own_part
        for came in (last_r, far_r, last_l, far_l):
            total = total + came.astype(jnp.float32)
        return total.astype(jnp.bfloat16)

    halves = 2 if cols_w % 256 == 0 else 1
    width = cols_w // halves
    recv_r = [None] * halves
    recv_l = [None] * halves
    for i in range(1, n_seq):
        t_r = jnp.clip(s_me + n_seq - i, 0, n_seq - 1)
        t_l = jnp.clip(s_me - n_seq + i, 0, n_seq - 1)
        part_r = partial_for(t_r)
        part_l = partial_for(t_l)
        for h in range(halves):
            send_r = part_r[:, h * width : (h + 1) * width]
            send_l = part_l[:, h * width : (h + 1) * width]
            if recv_r[h] is not None:
                send_r = send_r + recv_r[h].astype(jnp.float32)
                send_l = send_l + recv_l[h].astype(jnp.float32)
            recv_r[h] = lax.ppermute(
                send_r.astype(jnp.bfloat16), "seq", [(z, z + 1) for z in range(i)]
            )
            recv_l[h] = lax.ppermute(
                send_l.astype(jnp.bfloat16), "seq", [(z, z - 1) for z in range(n_seq - i, n_seq)]
            )
    total = partial_for(s_me)
    if recv_r[0] is not None:
        total = total + jnp.concatenate(
            [recv_r[h].astype(jnp.float32) + recv_l[h].astype(jnp.float32) for h in range(halves)],
            axis=1,
        )
    return total.astype(jnp.bfloat16)


def solution(mesh):
    in_specs = (
        P(("grp", "seq"), "mdl"),
        P(("grp", "seq"), "mdl"),
        P(("grp", "seq"), "mdl"),
        P(("grp", "seq"), "mdl"),
        P("mdl", ("grp", "seq")),
        P(None, "mdl"),
        P("mdl"),
        P("seq", "mdl"),
        P("mdl"),
    )
    out_specs = P(("grp", "seq"), "mdl")
    n_seq = mesh.shape["seq"]
    n_mdl = mesh.shape["mdl"]

    def body(*args):
        return per_device(n_seq, n_mdl, *args)

    return jax.shard_map(
        body, mesh=mesh, in_specs=in_specs, out_specs=out_specs, check_vma=False
    )
```
